32 devices in a mesh: seq: 16 (over z, y, x), fsdp: 2 (over core).
Axes of the slice: x: 2, y: 2, z: 4, core: 2. Of those that a mesh axis runs over, the one named last changes fastest.
Arguments:
- tokens: bfloat16 [12288, 4096], P('seq'), may hold values from -6 to 6
- norm_gain: float32 [4096], replicated, may hold values from 0.5 to 1.5
- w_zx: bfloat16 [4096, 2, 4096], P('seq', None, 'fsdp'), may hold values from -0.09375 to 0.09375
- w_bc: bfloat16 [4096, 2, 512], P('seq', None, 'fsdp'), may hold values from -0.09375 to 0.09375
- w_dt: bfloat16 [4096, 64], P('seq', 'fsdp'), may hold values from -0.09375 to 0.09375
- conv_x: bfloat16 [4, 4096], P(None, 'fsdp'), may hold values from -3 to 3
- conv_bc: bfloat16 [4, 2, 512], P(None, None, 'fsdp'), may hold values from -3 to 3
- dt_bias: float32 [64], P('fsdp'), may hold values from -4 to -1
- decay_rate: float32 [64], P('fsdp'), may hold values from 8.138021e-05 to 8
- d_skip: float32 [64], P('fsdp'), may hold values from 0.2 to 1
- gated_gain: float32 [4096], P('fsdp'), may hold values from 0.5 to 1.5
- w_out: bfloat16 [4096, 4096], P('fsdp', 'seq'), may hold values from -0.09375 to 0.09375
- prompt_lengths: int32 [8], replicated, may hold values from 1 to 3072, 12288 in all
- pack_order: int32 [8], replicated, may hold values from 0 to 7, each once
- resume_prompt: int32 [1], replicated, may hold values from 0 to 7
- carry_state: float32 [64, 64, 128], P('fsdp'), may hold values from -12 to 12
- carry_conv_x: bfloat16 [3, 4096], P(None, 'fsdp'), may hold values from -6 to 6
- carry_conv_bc: bfloat16 [3, 2, 512], P(None, None, 'fsdp'), may hold values from -6 to 6
Outputs:
- mixed: bfloat16 [12288, 4096], P(('seq', 'fsdp'))
The draws below stay inside these ranges and needn't reach their ends.
Inputs may be any that keep to these rules, and one draw needn't show every extreme that they name: `prompt_lengths`: they sum to 12288; the longest prompt holds exactly 3072 tokens. `pack_order`: each prompt stands at one place.
All inputs are finite; a program needn't handle non-finite values.
Results may differ from the reference program's by a relative error of at most 0.008.
Values may be sent and summed in bfloat16 or wider, within the bound.
No kernel may reach another device: no remote copies, remote signals or barrier semaphores. Data moves between devices by JAX's collectives and lax.ppermute only.
A program may use at most 128 MiB of HBM per device.

```python
import math
import jax
import jax.numpy as jnp
import numpy as np
from jax import lax

D = 4096
HEADS = 64
HEADDIM = 64
GROUPS = 4
STATE = 128
CONV = 4
SPAN = 256
TOKENS = 12288
INNER = 4096
MOST = 3072
PROMPTS = 8


def head_rates(key):
    folded = jax.random.fold_in(key, 4242)
    key_kind, key_bias, key_rate = jax.random.split(folded, 3)
    fast_share = 0.5
    fast = jax.random.bernoulli(key_kind, fast_share, (HEADS,))
    bias = jax.random.uniform(key_bias, (HEADS,), jnp.float32, -4.0, -1.0)
    typical = jax.nn.softplus(bias)
    spread = jax.random.uniform(key_rate, (HEADS,), jnp.float32, 0.0, 1.0)
    quick = jnp.exp(math.log(0.5) + spread * math.log(4.0)) / (40.0 * typical)
    lasting = jnp.exp(math.log(0.1) + spread * math.log(10.0)) / (MOST * typical)
    return (bias, jnp.where(fast, quick, lasting))


def draw_dt_bias(key, part):
    return head_rates(key)[0]


def draw_decay_rate(key, part):
    return head_rates(key)[1]


def block_levels(key, shape, cuts, least, high):
    gain, own = 1.0, jax.random.fold_in(key, 6)
    for dim, blocks in cuts:
        heights = jnp.exp(jax.random.uniform(jax.random.fold_in(own, dim), (blocks,), jnp.float32, least / len(cuts), high / len(cuts)))
        gain = gain * jnp.repeat(heights, shape[dim] // blocks).reshape([-1 if axis == dim else 1 for axis in range(len(shape))])
    return gain


def length_profile(number_of, total, most, lean):
    weights = [(1 << 20) // math.isqrt(grade ** lean) + 1 for grade in range(2, number_of + 1)]
    rest, holding = total - most - (number_of - 1), [1] * (number_of - 1)
    while rest > 0:
        candidates = [i for i in range(number_of - 1) if holding[i] < most]
        whole, remaining = sum([weights[i] for i in candidates]), rest
        for i in candidates:
            extra = min(most - holding[i], max(1, remaining * weights[i] // whole), rest)
            holding[i] = holding[i] + extra
            rest = rest - extra
    return np.array([most] + holding)


def ragged(own_key, count, total, limit, lean):
    if count == 2:
        one = jax.random.randint(own_key, (), max(1, total - limit), min(limit, total - 1) + 1)
        return jnp.stack([one, total - one])
    tallies = jnp.asarray(length_profile(count, total, limit, lean), jnp.int32)
    pairs = (count - 1) // 2
    donor, taker = tallies[1:1 + 2 * pairs:2], tallies[2:2 + 2 * pairs:2]
    margin = jnp.minimum(donor - 1, limit - taker)
    passed = jax.random.randint(jax.random.fold_in(own_key, 1), (pairs,), 0, 1 << 20) % (margin + 1)
    tallies = tallies.at[1:1 + 2 * pairs:2].set(donor - passed).at[2:2 + 2 * pairs:2].set(taker + passed)
    return tallies[jax.random.permutation(jax.random.fold_in(own_key, 2), count)]


def normal_values(own_key, extent, width, bound, cuts=(), kind=jnp.bfloat16):
    entries = jax.random.normal(own_key, extent, jnp.float32) * width
    if len(cuts) > 0:
        entries = block_levels(own_key, extent, cuts, -0.22, 0.18) * entries
    return jnp.clip(entries, min=-bound, max=bound).astype(kind)


def setup_inputs(seed: int = 0) -> dict:
    keys = jax.random.split(jax.random.key(seed), 19)
    return {
        "tokens": normal_values(keys[0], (TOKENS, D), 1.0, 6.0, ((0, 16),)),
        "norm_gain": jnp.clip(1.0 + 0.1 * jax.random.normal(keys[1], (D,), jnp.float32), 0.5, 1.5),
        "w_zx": normal_values(keys[2], (D, 2, INNER), D ** -0.5, 0.09375, ((0, 16), (2, 2))),
        "w_bc": normal_values(keys[3], (D, 2, GROUPS * STATE), D ** -0.5, 0.09375, ((0, 16), (2, 2))),
        "w_dt": normal_values(keys[4], (D, HEADS), D ** -0.5, 0.09375, ((0, 16), (1, 2))),
        "conv_x": normal_values(keys[5], (CONV, INNER), CONV ** -0.5, 3.0, ((1, 2),)),
        "conv_bc": normal_values(keys[6], (CONV, 2, GROUPS * STATE), CONV ** -0.5, 3.0, ((2, 2),)),
        "dt_bias": draw_dt_bias(jax.random.fold_in(keys[18], 71), 0),
        "decay_rate": draw_decay_rate(jax.random.fold_in(keys[18], 71), 0),
        "d_skip": jnp.clip(0.2 + 0.8 * jax.random.uniform(keys[9], (HEADS,), jnp.float32) ** block_levels(keys[9], (HEADS,), ((0, 2),), -0.2, 0.2), 0.2, 1.0),
        "gated_gain": jnp.clip(1.0 + 0.1 * jax.random.normal(keys[10], (INNER,), jnp.float32), 0.5, 1.5),
        "w_out": normal_values(keys[11], (INNER, D), INNER ** -0.5, 0.09375, ((0, 2), (1, 16))),
        "prompt_lengths": ragged(keys[12], PROMPTS, TOKENS, MOST, 2).astype(jnp.int32),
        "pack_order": jax.random.permutation(keys[13], PROMPTS).astype(jnp.int32),
        "resume_prompt": jax.random.randint(keys[14], (1,), 0, PROMPTS).astype(jnp.int32),
        "carry_state": normal_values(keys[15], (HEADS, HEADDIM, STATE), 2.0, 12.0, ((0, 2),), jnp.float32),
        "carry_conv_x": normal_values(keys[16], (CONV - 1, INNER), 1.0, 6.0, ((1, 2),)),
        "carry_conv_bc": normal_values(keys[17], (CONV - 1, 2, GROUPS * STATE), 1.0, 6.0, ((2, 2),)),
    }


EPS = 1e-05

def product_of(form, left, right):
    return jnp.einsum(form, left.astype(jnp.float32), right.astype(jnp.float32), precision=lax.Precision.HIGHEST)

def norm_rows(values, row_gain):
    widened = values.astype(jnp.float32)
    factor = lax.rsqrt(lax.optimization_barrier(jnp.mean(widened * widened, axis=-1, keepdims=True)) + EPS)
    return (widened * factor * row_gain[None, :]).astype(jnp.bfloat16)

def layout(prompt_lengths, pack_order, resume_prompt, position):
    prompt_count = pack_order.shape[0]
    slot_ids = jnp.arange(prompt_count, dtype=jnp.int32)
    ordered = lax.optimization_barrier(jnp.sum(jnp.where(pack_order[:, None] == slot_ids[None, :], prompt_lengths[None, :], 0), axis=1)).astype(jnp.int32)
    seg_starts = (jnp.cumsum(ordered, dtype=jnp.int32) - ordered).astype(jnp.int32)
    reached = position[:, None] >= seg_starts[None, :]
    segment = (lax.optimization_barrier(jnp.sum(reached.astype(jnp.int32), axis=1)) - 1).astype(jnp.int32)
    seg_start = lax.optimization_barrier(jnp.max(jnp.where(reached, seg_starts[None, :], 0), axis=1)).astype(jnp.int32)
    resume_slot = jnp.sum(jnp.where(pack_order == resume_prompt[0], slot_ids, 0)).astype(jnp.int32)
    resume_start = jnp.sum(jnp.where(slot_ids == resume_slot, seg_starts, 0)).astype(jnp.int32)
    return (segment, seg_start, resume_slot, resume_start)

def conv_rows(source, prior_rows, weight, carry_rows, segment, seg_start, position, resume_slot, resume_start):
    row_count = source.shape[0]
    edge_rows = prior_rows.shape[0]
    extended = jnp.concatenate([prior_rows, source], axis=0)
    resumed = (segment == resume_slot)[:, None]
    summed = jnp.zeros(source.shape, jnp.float32)
    for back_by in range(edge_rows + 1):
        shifted = extended[edge_rows - back_by:edge_rows - back_by + row_count].astype(jnp.float32)
        inside = (position - back_by >= seg_start)[:, None]
        carry_index = position - back_by - resume_start + edge_rows
        from_carry = jnp.zeros(source.shape, jnp.float32)
        for slot_id in range(edge_rows):
            from_carry = from_carry + jnp.where((carry_index == slot_id)[:, None], carry_rows[slot_id].astype(jnp.float32)[None, :], 0.0)
        chosen = jnp.where(inside, shifted, jnp.where(resumed, from_carry, 0.0))
        summed = summed + chosen * weight[edge_rows - back_by].astype(jnp.float32)[None, :]
    return jax.nn.silu(summed).astype(jnp.bfloat16)

def span_pieces(x_blocks, b_blocks, c_blocks, dt_blocks, head_rate, segment, starting, resumed, resume_hit, carry_init, skip_gain):
    block_len = segment.shape[1]
    log_decay = -dt_blocks * head_rate[None, None]
    cumulative = jnp.cumsum(log_decay, axis=1)
    indices = jnp.arange(block_len, dtype=jnp.int32)
    causal = (indices[:, None] >= indices[None, :])[None] & (segment[:, :, None] == segment[:, None, :])
    cum_rows = jnp.moveaxis(cumulative, 1, -1)
    log_gap = cum_rows[..., :, None] - cum_rows[..., None, :]
    within = causal[:, None, None]
    decays = jnp.where(within, jnp.exp(jnp.where(within, log_gap, 0.0)), 0.0)
    scores = product_of('cqgn,csgn->cgqs', c_blocks, b_blocks)
    dt_source = jnp.moveaxis(dt_blocks, 1, -1)[..., None, :]
    weights = (scores[:, :, None] * decays * dt_source).astype(jnp.bfloat16)
    direct = product_of('cghqs,csghp->cqghp', weights, x_blocks)
    cum_end = cumulative[:, -1]
    tail_mask = (segment == segment[:, -1:])[:, :, None, None]
    to_end = jnp.where(tail_mask, jnp.exp(jnp.where(tail_mask, cum_end[:, None] - cumulative, 0.0)), 0.0) * dt_blocks
    scaled = (x_blocks.astype(jnp.float32) * to_end[..., None]).astype(jnp.bfloat16)
    update = product_of('cqghp,cqgn->cghpn', scaled, b_blocks)
    opened = jnp.any(starting, axis=1)
    span_decay = jnp.where(opened[:, None, None], 0.0, jnp.exp(cum_end))
    hit_mask = resume_hit[:, :, None, None]
    has_hit = jnp.any(resume_hit, axis=1)[:, None, None, None]
    cum_hit = lax.optimization_barrier(jnp.sum(jnp.where(hit_mask, cumulative - log_decay, 0.0), axis=1, keepdims=True))
    carry_mask = resumed[:, :, None, None] & has_hit
    carry_gain = jnp.where(carry_mask, jnp.exp(jnp.where(carry_mask, cumulative - cum_hit, 0.0)), 0.0)
    end_gain = carry_gain[:, -1]
    update = update + end_gain[..., None, None] * carry_init[None]
    direct = direct + carry_gain[..., None] * product_of('ghpn,cqgn->cqghp', carry_init, c_blocks)
    direct = direct + skip_gain[None, None, :, :, None] * x_blocks.astype(jnp.float32)
    unopened = jnp.cumsum(starting.astype(jnp.int32), axis=1, dtype=jnp.int32) == 0
    state_gain = jnp.where(unopened[:, :, None, None], jnp.exp(cumulative), 0.0)
    return (direct, state_gain, update, span_decay)

def reference(tokens, norm_gain, w_zx, w_bc, w_dt, conv_x, conv_bc, dt_bias, decay_rate, d_skip, gated_gain, w_out, prompt_lengths, pack_order, resume_prompt, carry_state, carry_conv_x, carry_conv_bc):
    token_count = tokens.shape[0]
    model_width = tokens.shape[1]
    inner_width = w_zx.shape[2]
    state_cols = w_bc.shape[2]
    head_count = w_dt.shape[1]
    head_width = carry_state.shape[1]
    state_width = carry_state.shape[2]
    group_count = state_cols // state_width
    per_group = head_count // group_count
    edge_rows = conv_x.shape[0] - 1
    span_count = token_count // SPAN
    position = jnp.arange(token_count, dtype=jnp.int32)
    segment, seg_start, resume_slot, resume_start = layout(prompt_lengths, pack_order, resume_prompt, position)
    normed = norm_rows(tokens, norm_gain)
    proj_zx = jnp.dot(normed, w_zx.reshape(model_width, 2 * inner_width), preferred_element_type=jnp.float32).astype(jnp.bfloat16).reshape(token_count, 2, inner_width)
    proj_bc = jnp.dot(normed, w_bc.reshape(model_width, 2 * state_cols), preferred_element_type=jnp.float32).astype(jnp.bfloat16).reshape(token_count, 2, state_cols)
    dt_raw = jnp.dot(normed, w_dt, preferred_element_type=jnp.float32).astype(jnp.bfloat16)
    source = jnp.concatenate([proj_zx[:, 1], proj_bc[:, 0], proj_bc[:, 1]], axis=1)
    weight = jnp.concatenate([conv_x, conv_bc[:, 0], conv_bc[:, 1]], axis=1)
    carry_rows = jnp.concatenate([carry_conv_x, carry_conv_bc[:, 0], carry_conv_bc[:, 1]], axis=1)
    prior_rows = jnp.zeros((edge_rows, source.shape[1]), jnp.bfloat16)
    conv_out = conv_rows(source, prior_rows, weight, carry_rows, segment, seg_start, position, resume_slot, resume_start)
    x_conv = conv_out[:, :inner_width].reshape(span_count, SPAN, group_count, per_group, head_width)
    b_conv = conv_out[:, inner_width:inner_width + state_cols].reshape(span_count, SPAN, group_count, state_width)
    c_conv = conv_out[:, inner_width + state_cols:].reshape(span_count, SPAN, group_count, state_width)
    dt_full = jax.nn.softplus(dt_raw.astype(jnp.float32) + dt_bias[None, :]).reshape(span_count, SPAN, group_count, per_group)
    seg_blocks = segment.reshape(span_count, SPAN)
    starting = (position == seg_start).reshape(span_count, SPAN)
    resumed = (segment == resume_slot).reshape(span_count, SPAN)
    resume_hit = (position == resume_start).reshape(span_count, SPAN)
    head_rate = decay_rate.reshape(group_count, per_group)
    skip_gain = d_skip.reshape(group_count, per_group)
    carry_init = carry_state.reshape(group_count, per_group, head_width, state_width)

    def advance(state_in, inputs):
        x_one, b_one, c_one, dt_one, seg_one, start_one, resumed_one, hit_one = inputs
        direct, state_gain, update, span_decay = span_pieces(x_one[None], b_one[None], c_one[None], dt_one[None], head_rate, seg_one[None], start_one[None], resumed_one[None], hit_one[None], carry_init, skip_gain)
        from_state = product_of('ghpn,qgn->qghp', state_in, c_one)
        output = direct[0] + state_gain[0][..., None] * from_state
        return (span_decay[0][..., None, None] * state_in + update[0], output)
    start_state = jnp.zeros((group_count, per_group, head_width, state_width), jnp.float32)
    _, outputs = lax.scan(advance, start_state, (x_conv, b_conv, c_conv, dt_full, seg_blocks, starting, resumed, resume_hit))
    ssd_out = outputs.reshape(token_count, inner_width)
    gate_act = jax.nn.silu(proj_zx[:, 0].astype(jnp.float32))
    gated = (ssd_out * gate_act).reshape(token_count, group_count, inner_width // group_count)
    factor = lax.rsqrt(lax.optimization_barrier(jnp.mean(gated * gated, axis=-1, keepdims=True)) + EPS)
    normed_y = ((gated * factor).reshape(token_count, inner_width) * gated_gain[None, :]).astype(jnp.bfloat16)
    return jnp.dot(normed_y, w_out, preferred_element_type=jnp.float32).astype(jnp.bfloat16)
```

```python
import jax
import jax.numpy as jnp
from jax import lax
from jax.sharding import PartitionSpec as P

SPAN = 256


EPS = 1e-05


def from_behind(value, axis, steps):
    count = lax.axis_size(axis)
    leading, last = (max(0, -steps), min(count, count - steps))
    return lax.ppermute(value, axis, [(source, source + steps) for source in range(leading, last)])


def product_of(form, left, right):
    if left.dtype == jnp.bfloat16 and right.dtype == jnp.bfloat16:
        return jnp.einsum(form, left, right, preferred_element_type=jnp.float32)
    return jnp.einsum(form, left, right.astype(jnp.float32), precision=lax.Precision.HIGHEST)


def norm_rows(values, row_gain):
    widened = values.astype(jnp.float32)
    factor = lax.rsqrt(jnp.mean(widened * widened, axis=-1, keepdims=True) + EPS)
    return (widened * factor * row_gain[None, :]).astype(jnp.bfloat16)


def layout(prompt_lengths, pack_order, resume_prompt, position):
    prompt_count = pack_order.shape[0]
    slot_ids = jnp.arange(prompt_count, dtype=jnp.int32)
    ordered = jnp.sum(
        jnp.where(pack_order[:, None] == slot_ids[None, :], prompt_lengths[None, :], 0), axis=1
    )
    seg_starts = jnp.cumsum(ordered, dtype=jnp.int32) - ordered
    reached = position[:, None] >= seg_starts[None, :]
    segment = jnp.sum(reached.astype(jnp.int32), axis=1) - 1
    seg_start = jnp.max(jnp.where(reached, seg_starts[None, :], 0), axis=1)
    resume_slot = jnp.sum(jnp.where(pack_order == resume_prompt[0], slot_ids, 0))
    resume_start = jnp.sum(jnp.where(slot_ids == resume_slot, seg_starts, 0))
    return (segment, seg_start, resume_slot, resume_start)


def conv_rows(
    source, prior_rows, weight, carry_rows, segment, seg_start, position, resume_slot, resume_start
):
    row_count = source.shape[0]
    edge_rows = prior_rows.shape[0]
    extended = jnp.concatenate([prior_rows, source], axis=0)
    resumed = (segment == resume_slot)[:, None]
    summed = jnp.zeros(source.shape, jnp.float32)
    for back_by in range(edge_rows + 1):
        shifted = extended[edge_rows - back_by : edge_rows - back_by + row_count].astype(
            jnp.float32
        )
        inside = (position - back_by >= seg_start)[:, None]
        carry_index = position - back_by - resume_start + edge_rows
        from_carry = jnp.zeros(source.shape, jnp.float32)
        for slot_id in range(edge_rows):
            from_carry = from_carry + jnp.where(
                (carry_index == slot_id)[:, None],
                carry_rows[slot_id].astype(jnp.float32)[None, :],
                0.0,
            )
        chosen = jnp.where(inside, shifted, jnp.where(resumed, from_carry, 0.0))
        summed = summed + chosen * weight[edge_rows - back_by].astype(jnp.float32)[None, :]
    return jax.nn.silu(summed).astype(jnp.bfloat16)


def span_pieces(
    x_blocks,
    b_blocks,
    c_blocks,
    dt_blocks,
    head_rate,
    segment,
    starting,
    resumed,
    resume_hit,
    carry_init,
    skip_gain,
):
    block_len = segment.shape[1]
    log_decay = -dt_blocks * head_rate[None, None]
    cumulative = jnp.cumsum(log_decay, axis=1)
    indices = jnp.arange(block_len, dtype=jnp.int32)
    causal = (indices[:, None] >= indices[None, :])[None] & (
        segment[:, :, None] == segment[:, None, :]
    )
    cum_rows = jnp.moveaxis(cumulative, 1, -1)
    log_gap = cum_rows[..., :, None] - cum_rows[..., None, :]
    within = causal[:, None, None]
    decays = jnp.where(within, jnp.exp(jnp.where(within, log_gap, 0.0)), 0.0)
    scores = product_of("cqgn,csgn->cgqs", c_blocks, b_blocks)
    dt_source = jnp.moveaxis(dt_blocks, 1, -1)[..., None, :]
    weights = (scores[:, :, None] * decays * dt_source).astype(jnp.bfloat16)
    direct = product_of("cghqs,csghp->cqghp", weights, x_blocks)
    cum_end = cumulative[:, -1]
    tail_mask = (segment == segment[:, -1:])[:, :, None, None]
    to_end = (
        jnp.where(tail_mask, jnp.exp(jnp.where(tail_mask, cum_end[:, None] - cumulative, 0.0)), 0.0)
        * dt_blocks
    )
    scaled = (x_blocks.astype(jnp.float32) * to_end[..., None]).astype(jnp.bfloat16)
    update = product_of("cqghp,cqgn->cghpn", scaled, b_blocks)
    opened = jnp.any(starting, axis=1)
    span_decay = jnp.where(opened[:, None, None], 0.0, jnp.exp(cum_end))
    hit_mask = resume_hit[:, :, None, None]
    has_hit = jnp.any(resume_hit, axis=1)[:, None, None, None]
    cum_hit = jnp.sum(jnp.where(hit_mask, cumulative - log_decay, 0.0), axis=1, keepdims=True)
    carry_mask = resumed[:, :, None, None] & has_hit
    carry_gain = jnp.where(
        carry_mask, jnp.exp(jnp.where(carry_mask, cumulative - cum_hit, 0.0)), 0.0
    )
    end_gain = carry_gain[:, -1]
    update = update + end_gain[..., None, None] * carry_init[None]
    direct = direct + carry_gain[..., None] * product_of("ghpn,cqgn->cqghp", carry_init, c_blocks)
    direct = direct + skip_gain[None, None, :, :, None] * x_blocks.astype(jnp.float32)
    unopened = jnp.cumsum(starting.astype(jnp.int32), axis=1, dtype=jnp.int32) == 0
    state_gain = jnp.where(unopened[:, :, None, None], jnp.exp(cumulative), 0.0)
    return (direct, state_gain, update, span_decay)


def body(
    tokens,
    norm_gain,
    w_zx,
    w_bc,
    w_dt,
    conv_x,
    conv_bc,
    dt_bias,
    decay_rate,
    d_skip,
    gated_gain,
    w_out,
    prompt_lengths,
    pack_order,
    resume_prompt,
    carry_state,
    carry_conv_x,
    carry_conv_bc,
):
    row_count = tokens.shape[0]
    edge_rows = conv_x.shape[0] - 1
    inner_local = w_zx.shape[2]
    state_cols = w_bc.shape[2]
    head_local = w_dt.shape[1]
    head_width = carry_state.shape[1]
    state_width = carry_state.shape[2]
    group_local = state_cols // state_width
    per_group = head_local // group_local
    span_count = row_count // SPAN
    position = lax.axis_index("seq") * row_count + jnp.arange(row_count, dtype=jnp.int32)
    segment, seg_start, resume_slot, resume_start = layout(
        prompt_lengths, pack_order, resume_prompt, position
    )
    normed = norm_rows(tokens, norm_gain)
    first_local = jnp.concatenate(
        [w_zx[:, 1], w_bc.reshape(w_bc.shape[0], 2 * state_cols), w_dt], axis=1
    )
    first_full = lax.all_gather(first_local, "seq", axis=0, tiled=True)
    proj_first = jnp.dot(normed, first_full, preferred_element_type=jnp.float32).astype(
        jnp.bfloat16
    )
    conv_width = inner_local + 2 * state_cols
    conv_in = proj_first[:, :conv_width]
    proj_dt = proj_first[:, conv_width:]
    z_local, out_local, _ = lax.optimization_barrier((w_zx[:, 0], w_out, proj_first))
    z_full = lax.all_gather(z_local, "seq", axis=0, tiled=True)
    out_full = lax.all_gather(out_local, "seq", axis=1, tiled=True)
    proj_z = jnp.dot(normed, z_full, preferred_element_type=jnp.float32).astype(jnp.bfloat16)
    prior_rows = from_behind(conv_in[row_count - edge_rows :], "seq", 1)
    weight = jnp.concatenate([conv_x, conv_bc[:, 0], conv_bc[:, 1]], axis=1)
    carry_rows = jnp.concatenate([carry_conv_x, carry_conv_bc[:, 0], carry_conv_bc[:, 1]], axis=1)
    conv_out = conv_rows(
        conv_in,
        prior_rows,
        weight,
        carry_rows,
        segment,
        seg_start,
        position,
        resume_slot,
        resume_start,
    )
    x_conv = conv_out[:, :inner_local].reshape(span_count, SPAN, group_local, per_group, head_width)
    b_conv = conv_out[:, inner_local : inner_local + state_cols].reshape(
        span_count, SPAN, group_local, state_width
    )
    c_conv = conv_out[:, inner_local + state_cols :].reshape(
        span_count, SPAN, group_local, state_width
    )
    dt_full = jax.nn.softplus(proj_dt.astype(jnp.float32) + dt_bias[None, :]).reshape(
        span_count, SPAN, group_local, per_group
    )
    seg_blocks = segment.reshape(span_count, SPAN)
    starting = (position == seg_start).reshape(span_count, SPAN)
    resumed = (segment == resume_slot).reshape(span_count, SPAN)
    resume_hit = (position == resume_start).reshape(span_count, SPAN)
    head_rate = decay_rate.reshape(group_local, per_group)
    skip_gain = d_skip.reshape(group_local, per_group)
    carry_init = carry_state.reshape(group_local, per_group, head_width, state_width)
    direct, state_gain, update, span_decay = span_pieces(
        x_conv,
        b_conv,
        c_conv,
        dt_full,
        head_rate,
        seg_blocks,
        starting,
        resumed,
        resume_hit,
        carry_init,
        skip_gain,
    )

    def fold_span(carried, pieces):
        return (
            (pieces[1][..., None, None] * carried[0] + pieces[0], pieces[1] * carried[1]),
            carried,
        )

    empty_state = jnp.zeros((group_local, per_group, head_width, state_width), jnp.float32)
    unit_decay = jnp.ones((group_local, per_group), jnp.float32)
    (local_state, local_decay), (prefix_state, prefix_decay) = lax.scan(
        fold_span, (empty_state, unit_decay), (update, span_decay)
    )
    hop_count = lax.axis_size("seq") // 4
    incoming = jnp.zeros_like(local_state)
    reach = jnp.ones_like(local_decay)
    for steps in range(1, hop_count + 1):
        state_back, decay_back = from_behind((local_state, local_decay), "seq", steps)
        incoming = incoming + reach[..., None, None] * state_back
        reach = reach * decay_back
    entering = prefix_decay[..., None, None] * incoming[None] + prefix_state
    from_state = product_of("cghpn,cqgn->cqghp", entering, c_conv)
    ssd_out = (direct + state_gain[..., None] * from_state).reshape(row_count, inner_local)
    gate_act = jax.nn.silu(proj_z.astype(jnp.float32))
    gated = (ssd_out * gate_act).reshape(row_count, group_local, inner_local // group_local)
    factor = lax.rsqrt(jnp.mean(gated * gated, axis=-1, keepdims=True) + EPS)
    normed_y = ((gated * factor).reshape(row_count, inner_local) * gated_gain[None, :]).astype(
        jnp.bfloat16
    )
    core_count = lax.axis_size("fsdp")
    piece = row_count // core_count
    core = lax.axis_index("fsdp")
    total = None
    for shift in list(range(1, core_count)) + [0]:
        rows = lax.dynamic_slice_in_dim(normed_y, (core + shift) % core_count * piece, piece, 0)
        part = jnp.dot(rows, out_full, preferred_element_type=jnp.float32)
        if shift:
            part = lax.ppermute(
                part, "fsdp", [(j, (j + shift) % core_count) for j in range(core_count)]
            )
        total = part if total is None else total + part
    return total.astype(jnp.bfloat16)


def solution(mesh):
    return jax.shard_map(
        body,
        mesh=mesh,
        in_specs=(
            P("seq", None),
            P(),
            P("seq", None, "fsdp"),
            P("seq", None, "fsdp"),
            P("seq", "fsdp"),
            P(None, "fsdp"),
            P(None, None, "fsdp"),
            P("fsdp"),
            P("fsdp"),
            P("fsdp"),
            P("fsdp"),
            P("fsdp", "seq"),
            P(),
            P(),
            P(),
            P("fsdp", None, None),
            P(None, "fsdp"),
            P(None, None, "fsdp"),
        ),
        out_specs=P(("seq", "fsdp"), None),
        check_vma=False,
    )
```

```python
import jax
import jax.numpy as jnp
from jax import lax
from jax.sharding import PartitionSpec as P

SPAN = 256


EPS = 1e-05


def from_behind(value, axis, steps):
    count = lax.axis_size(axis)
    leading, last = (max(0, -steps), min(count, count - steps))
    return lax.ppermute(value, axis, [(source, source + steps) for source in range(leading, last)])


def ring_order(count):
    return list(range(0, count, 2)) + list(range(count - 1, 0, -2))


def ring_gather(local, axis, order):
    count = len(order)
    forward = [(order[k], order[(k + 1) % count]) for k in range(count)]
    backward = [(order[k], order[(k - 1) % count]) for k in range(count)]
    chunks = [local] + [None] * (count - 1)
    ahead, behind = local, local
    for steps in range(1, count // 2 + 1):
        ahead = lax.ppermute(ahead, axis, forward)
        chunks[steps] = ahead
        if steps < count - steps:
            behind = lax.ppermute(behind, axis, backward)
            chunks[count - steps] = behind
    return chunks


def ring_columns(values, axis, order, width):
    count = len(order)
    table = jnp.asarray(order, jnp.int32)
    places = jnp.asarray([order.index(k) for k in range(count)], jnp.int32)
    place = places[lax.axis_index(axis)]
    blocks = [
        lax.dynamic_slice_in_dim(values, table[(place - offset) % count] * width, width, 1)
        for offset in range(count)
    ]
    return jnp.concatenate(blocks, axis=1)


def product_of(form, left, right):
    if left.dtype == jnp.bfloat16 and right.dtype == jnp.bfloat16:
        return jnp.einsum(form, left, right, preferred_element_type=jnp.float32)
    return jnp.einsum(form, left, right.astype(jnp.float32), precision=lax.Precision.HIGHEST)


def norm_rows(values, row_gain):
    widened = values.astype(jnp.float32)
    factor = lax.rsqrt(jnp.mean(widened * widened, axis=-1, keepdims=True) + EPS)
    return (widened * factor * row_gain[None, :]).astype(jnp.bfloat16)


def layout(prompt_lengths, pack_order, resume_prompt, position):
    prompt_count = pack_order.shape[0]
    slot_ids = jnp.arange(prompt_count, dtype=jnp.int32)
    ordered = jnp.sum(
        jnp.where(pack_order[:, None] == slot_ids[None, :], prompt_lengths[None, :], 0), axis=1
    )
    seg_starts = jnp.cumsum(ordered, dtype=jnp.int32) - ordered
    reached = position[:, None] >= seg_starts[None, :]
    segment = jnp.sum(reached.astype(jnp.int32), axis=1) - 1
    seg_start = jnp.max(jnp.where(reached, seg_starts[None, :], 0), axis=1)
    resume_slot = jnp.sum(jnp.where(pack_order == resume_prompt[0], slot_ids, 0))
    resume_start = jnp.sum(jnp.where(slot_ids == resume_slot, seg_starts, 0))
    return (segment, seg_start, resume_slot, resume_start)


def conv_rows(
    source, prior_rows, weight, carry_rows, segment, seg_start, position, resume_slot, resume_start
):
    row_count = source.shape[0]
    edge_rows = prior_rows.shape[0]
    extended = jnp.concatenate([prior_rows, source], axis=0)
    resumed = (segment == resume_slot)[:, None]
    summed = jnp.zeros(source.shape, jnp.float32)
    for back_by in range(edge_rows + 1):
        shifted = extended[edge_rows - back_by : edge_rows - back_by + row_count].astype(
            jnp.float32
        )
        inside = (position - back_by >= seg_start)[:, None]
        carry_index = position - back_by - resume_start + edge_rows
        from_carry = jnp.zeros(source.shape, jnp.float32)
        for slot_id in range(edge_rows):
            from_carry = from_carry + jnp.where(
                (carry_index == slot_id)[:, None],
                carry_rows[slot_id].astype(jnp.float32)[None, :],
                0.0,
            )
        chosen = jnp.where(inside, shifted, jnp.where(resumed, from_carry, 0.0))
        summed = summed + chosen * weight[edge_rows - back_by].astype(jnp.float32)[None, :]
    return jax.nn.silu(summed).astype(jnp.bfloat16)


def span_pieces(
    x_blocks,
    b_blocks,
    c_blocks,
    dt_blocks,
    head_rate,
    segment,
    starting,
    resumed,
    resume_hit,
    carry_init,
    skip_gain,
):
    block_len = segment.shape[1]
    log_decay = -dt_blocks * head_rate[None, None]
    cumulative = jnp.cumsum(log_decay, axis=1)
    indices = jnp.arange(block_len, dtype=jnp.int32)
    causal = (indices[:, None] >= indices[None, :])[None] & (
        segment[:, :, None] == segment[:, None, :]
    )
    cum_rows = jnp.moveaxis(cumulative, 1, -1)
    log_gap = cum_rows[..., :, None] - cum_rows[..., None, :]
    within = causal[:, None, None]
    decays = jnp.where(within, jnp.exp(jnp.where(within, log_gap, 0.0)), 0.0)
    scores = product_of("cqgn,csgn->cgqs", c_blocks, b_blocks)
    dt_source = jnp.moveaxis(dt_blocks, 1, -1)[..., None, :]
    weights = (scores[:, :, None] * decays * dt_source).astype(jnp.bfloat16)
    direct = product_of("cghqs,csghp->cqghp", weights, x_blocks)
    cum_end = cumulative[:, -1]
    tail_mask = (segment == segment[:, -1:])[:, :, None, None]
    to_end = (
        jnp.where(tail_mask, jnp.exp(jnp.where(tail_mask, cum_end[:, None] - cumulative, 0.0)), 0.0)
        * dt_blocks
    )
    scaled = (x_blocks.astype(jnp.float32) * to_end[..., None]).astype(jnp.bfloat16)
    update = product_of("cqghp,cqgn->cghpn", scaled, b_blocks)
    opened = jnp.any(starting, axis=1)
    span_decay = jnp.where(opened[:, None, None], 0.0, jnp.exp(cum_end))
    hit_mask = resume_hit[:, :, None, None]
    has_hit = jnp.any(resume_hit, axis=1)[:, None, None, None]
    cum_hit = jnp.sum(jnp.where(hit_mask, cumulative - log_decay, 0.0), axis=1, keepdims=True)
    carry_mask = resumed[:, :, None, None] & has_hit
    carry_gain = jnp.where(
        carry_mask, jnp.exp(jnp.where(carry_mask, cumulative - cum_hit, 0.0)), 0.0
    )
    end_gain = carry_gain[:, -1]
    update = update + end_gain[..., None, None] * carry_init[None]
    direct = direct + carry_gain[..., None] * product_of("ghpn,cqgn->cqghp", carry_init, c_blocks)
    direct = direct + skip_gain[None, None, :, :, None] * x_blocks.astype(jnp.float32)
    unopened = jnp.cumsum(starting.astype(jnp.int32), axis=1, dtype=jnp.int32) == 0
    state_gain = jnp.where(unopened[:, :, None, None], jnp.exp(cumulative), 0.0)
    return (direct, state_gain, update, span_decay)


def body(
    tokens,
    norm_gain,
    w_zx,
    w_bc,
    w_dt,
    conv_x,
    conv_bc,
    dt_bias,
    decay_rate,
    d_skip,
    gated_gain,
    w_out,
    prompt_lengths,
    pack_order,
    resume_prompt,
    carry_state,
    carry_conv_x,
    carry_conv_bc,
):
    row_count = tokens.shape[0]
    edge_rows = conv_x.shape[0] - 1
    inner_local = w_zx.shape[2]
    state_cols = w_bc.shape[2]
    head_local = w_dt.shape[1]
    head_width = carry_state.shape[1]
    state_width = carry_state.shape[2]
    group_local = state_cols // state_width
    per_group = head_local // group_local
    span_count = row_count // SPAN
    position = lax.axis_index("seq") * row_count + jnp.arange(row_count, dtype=jnp.int32)
    segment, seg_start, resume_slot, resume_start = layout(
        prompt_lengths, pack_order, resume_prompt, position
    )
    normed = norm_rows(tokens, norm_gain)
    first_local = jnp.concatenate(
        [w_zx[:, 1], w_bc.reshape(w_bc.shape[0], 2 * state_cols), w_dt], axis=1
    )
    order = ring_order(lax.axis_size("seq"))
    out_full = lax.all_gather(w_out, "seq", axis=1, tiled=True)
    first_chunks = ring_gather(first_local, "seq", order)
    normed_ring = ring_columns(normed, "seq", order, first_local.shape[0])
    proj_first = jnp.dot(
        normed_ring, jnp.concatenate(first_chunks, axis=0), preferred_element_type=jnp.float32
    ).astype(jnp.bfloat16)
    conv_width = inner_local + 2 * state_cols
    conv_in = proj_first[:, :conv_width]
    proj_dt = proj_first[:, conv_width:]
    z_local, _ = lax.optimization_barrier((w_zx[:, 0], first_chunks))
    z_chunks = ring_gather(z_local, "seq", order)
    proj_z = jnp.dot(
        normed_ring, jnp.concatenate(z_chunks, axis=0), preferred_element_type=jnp.float32
    ).astype(jnp.bfloat16)
    prior_rows = from_behind(conv_in[row_count - edge_rows :], "seq", 1)
    weight = jnp.concatenate([conv_x, conv_bc[:, 0], conv_bc[:, 1]], axis=1)
    carry_rows = jnp.concatenate([carry_conv_x, carry_conv_bc[:, 0], carry_conv_bc[:, 1]], axis=1)
    conv_out = conv_rows(
        conv_in,
        prior_rows,
        weight,
        carry_rows,
        segment,
        seg_start,
        position,
        resume_slot,
        resume_start,
    )
    x_conv = conv_out[:, :inner_local].reshape(span_count, SPAN, group_local, per_group, head_width)
    b_conv = conv_out[:, inner_local : inner_local + state_cols].reshape(
        span_count, SPAN, group_local, state_width
    )
    c_conv = conv_out[:, inner_local + state_cols :].reshape(
        span_count, SPAN, group_local, state_width
    )
    dt_full = jax.nn.softplus(proj_dt.astype(jnp.float32) + dt_bias[None, :]).reshape(
        span_count, SPAN, group_local, per_group
    )
    seg_blocks = segment.reshape(span_count, SPAN)
    starting = (position == seg_start).reshape(span_count, SPAN)
    resumed = (segment == resume_slot).reshape(span_count, SPAN)
    resume_hit = (position == resume_start).reshape(span_count, SPAN)
    head_rate = decay_rate.reshape(group_local, per_group)
    skip_gain = d_skip.reshape(group_local, per_group)
    carry_init = carry_state.reshape(group_local, per_group, head_width, state_width)
    direct, state_gain, update, span_decay = span_pieces(
        x_conv,
        b_conv,
        c_conv,
        dt_full,
        head_rate,
        seg_blocks,
        starting,
        resumed,
        resume_hit,
        carry_init,
        skip_gain,
    )

    def fold_span(carried, pieces):
        return (
            (pieces[1][..., None, None] * carried[0] + pieces[0], pieces[1] * carried[1]),
            carried,
        )

    empty_state = jnp.zeros((group_local, per_group, head_width, state_width), jnp.float32)
    unit_decay = jnp.ones((group_local, per_group), jnp.float32)
    (local_state, local_decay), (prefix_state, prefix_decay) = lax.scan(
        fold_span, (empty_state, unit_decay), (update, span_decay)
    )
    hop_count = lax.axis_size("seq") // 4
    incoming = jnp.zeros_like(local_state)
    reach = jnp.ones_like(local_decay)
    for steps in range(1, hop_count + 1):
        state_back, decay_back = from_behind((local_state, local_decay), "seq", steps)
        incoming = incoming + reach[..., None, None] * state_back
        reach = reach * decay_back
    entering = prefix_decay[..., None, None] * incoming[None] + prefix_state
    from_state = product_of("cghpn,cqgn->cqghp", entering, c_conv)
    ssd_out = (direct + state_gain[..., None] * from_state).reshape(row_count, inner_local)
    gate_act = jax.nn.silu(proj_z.astype(jnp.float32))
    gated = (ssd_out * gate_act).reshape(row_count, group_local, inner_local // group_local)
    factor = lax.rsqrt(jnp.mean(gated * gated, axis=-1, keepdims=True) + EPS)
    normed_y = ((gated * factor).reshape(row_count, inner_local) * gated_gain[None, :]).astype(
        jnp.bfloat16
    )
    core_count = lax.axis_size("fsdp")
    piece = row_count // core_count
    core = lax.axis_index("fsdp")
    total = None
    for shift in list(range(1, core_count)) + [0]:
        rows = lax.dynamic_slice_in_dim(normed_y, (core + shift) % core_count * piece, piece, 0)
        part = jnp.dot(rows, out_full, preferred_element_type=jnp.float32)
        if shift:
            part = lax.ppermute(
                part, "fsdp", [(j, (j + shift) % core_count) for j in range(core_count)]
            )
        total = part if total is None else total + part
    return total.astype(jnp.bfloat16)


def solution(mesh):
    return jax.shard_map(
        body,
        mesh=mesh,
        in_specs=(
            P("seq", None),
            P(),
            P("seq", None, "fsdp"),
            P("seq", None, "fsdp"),
            P("seq", "fsdp"),
            P(None, "fsdp"),
            P(None, None, "fsdp"),
            P("fsdp"),
            P("fsdp"),
            P("fsdp"),
            P("fsdp"),
            P("fsdp", "seq"),
            P(),
            P(),
            P(),
            P("fsdp", None, None),
            P(None, "fsdp"),
            P(None, None, "fsdp"),
        ),
        out_specs=P(("seq", "fsdp"), None),
        check_vma=False,
    )
```

```python
import jax
import jax.numpy as jnp
from jax import lax
from jax.sharding import PartitionSpec as P

SPAN = 256


EPS = 1e-05


def from_behind(value, axis, steps):
    count = lax.axis_size(axis)
    leading, last = (max(0, -steps), min(count, count - steps))
    return lax.ppermute(value, axis, [(source, source + steps) for source in range(leading, last)])


def product_of(form, left, right):
    if left.dtype == jnp.bfloat16 and right.dtype == jnp.bfloat16:
        return jnp.einsum(form, left, right, preferred_element_type=jnp.float32)
    return jnp.einsum(form, left, right.astype(jnp.float32), precision=lax.Precision.HIGHEST)


def norm_rows(values, row_gain):
    widened = values.astype(jnp.float32)
    factor = lax.rsqrt(jnp.mean(widened * widened, axis=-1, keepdims=True) + EPS)
    return (widened * factor * row_gain[None, :]).astype(jnp.bfloat16)


def layout(prompt_lengths, pack_order, resume_prompt, position):
    prompt_count = pack_order.shape[0]
    slot_ids = jnp.arange(prompt_count, dtype=jnp.int32)
    ordered = jnp.sum(
        jnp.where(pack_order[:, None] == slot_ids[None, :], prompt_lengths[None, :], 0), axis=1
    )
    seg_starts = jnp.cumsum(ordered, dtype=jnp.int32) - ordered
    reached = position[:, None] >= seg_starts[None, :]
    segment = jnp.sum(reached.astype(jnp.int32), axis=1) - 1
    seg_start = jnp.max(jnp.where(reached, seg_starts[None, :], 0), axis=1)
    resume_slot = jnp.sum(jnp.where(pack_order == resume_prompt[0], slot_ids, 0))
    resume_start = jnp.sum(jnp.where(slot_ids == resume_slot, seg_starts, 0))
    return (segment, seg_start, resume_slot, resume_start)


def conv_rows(
    source, prior_rows, weight, carry_rows, segment, seg_start, position, resume_slot, resume_start
):
    row_count = source.shape[0]
    edge_rows = prior_rows.shape[0]
    extended = jnp.concatenate([prior_rows, source], axis=0)
    resumed = (segment == resume_slot)[:, None]
    summed = jnp.zeros(source.shape, jnp.float32)
    for back_by in range(edge_rows + 1):
        shifted = extended[edge_rows - back_by : edge_rows - back_by + row_count].astype(
            jnp.float32
        )
        inside = (position - back_by >= seg_start)[:, None]
        carry_index = position - back_by - resume_start + edge_rows
        from_carry = jnp.zeros(source.shape, jnp.float32)
        for slot_id in range(edge_rows):
            from_carry = from_carry + jnp.where(
                (carry_index == slot_id)[:, None],
                carry_rows[slot_id].astype(jnp.float32)[None, :],
                0.0,
            )
        chosen = jnp.where(inside, shifted, jnp.where(resumed, from_carry, 0.0))
        summed = summed + chosen * weight[edge_rows - back_by].astype(jnp.float32)[None, :]
    return jax.nn.silu(summed).astype(jnp.bfloat16)


def span_pieces(
    x_blocks,
    b_blocks,
    c_blocks,
    dt_blocks,
    head_rate,
    segment,
    starting,
    resumed,
    resume_hit,
    carry_init,
    skip_gain,
):
    block_len = segment.shape[1]
    log_decay = -dt_blocks * head_rate[None, None]
    cumulative = jnp.cumsum(log_decay, axis=1)
    indices = jnp.arange(block_len, dtype=jnp.int32)
    causal = (indices[:, None] >= indices[None, :])[None] & (
        segment[:, :, None] == segment[:, None, :]
    )
    cum_rows = jnp.moveaxis(cumulative, 1, -1)
    log_gap = cum_rows[..., :, None] - cum_rows[..., None, :]
    within = causal[:, None, None]
    decays = jnp.where(within, jnp.exp(jnp.where(within, log_gap, 0.0)), 0.0)
    scores = product_of("cqgn,csgn->cgqs", c_blocks, b_blocks)
    dt_source = jnp.moveaxis(dt_blocks, 1, -1)[..., None, :]
    weights = (scores[:, :, None] * decays * dt_source).astype(jnp.bfloat16)
    direct = product_of("cghqs,csghp->cqghp", weights, x_blocks)
    cum_end = cumulative[:, -1]
    tail_mask = (segment == segment[:, -1:])[:, :, None, None]
    to_end = (
        jnp.where(tail_mask, jnp.exp(jnp.where(tail_mask, cum_end[:, None] - cumulative, 0.0)), 0.0)
        * dt_blocks
    )
    scaled = (x_blocks.astype(jnp.float32) * to_end[..., None]).astype(jnp.bfloat16)
    update = product_of("cqghp,cqgn->cghpn", scaled, b_blocks)
    opened = jnp.any(starting, axis=1)
    span_decay = jnp.where(opened[:, None, None], 0.0, jnp.exp(cum_end))
    hit_mask = resume_hit[:, :, None, None]
    has_hit = jnp.any(resume_hit, axis=1)[:, None, None, None]
    cum_hit = jnp.sum(jnp.where(hit_mask, cumulative - log_decay, 0.0), axis=1, keepdims=True)
    carry_mask = resumed[:, :, None, None] & has_hit
    carry_gain = jnp.where(
        carry_mask, jnp.exp(jnp.where(carry_mask, cumulative - cum_hit, 0.0)), 0.0
    )
    end_gain = carry_gain[:, -1]
    update = update + end_gain[..., None, None] * carry_init[None]
    direct = direct + carry_gain[..., None] * product_of("ghpn,cqgn->cqghp", carry_init, c_blocks)
    direct = direct + skip_gain[None, None, :, :, None] * x_blocks.astype(jnp.float32)
    unopened = jnp.cumsum(starting.astype(jnp.int32), axis=1, dtype=jnp.int32) == 0
    state_gain = jnp.where(unopened[:, :, None, None], jnp.exp(cumulative), 0.0)
    return (direct, state_gain, update, span_decay)


def swap_half(value):
    count = lax.axis_size("half")
    return lax.ppermute(value, "half", [(k, count - 1 - k) for k in range(count)])


def ordered_pair(own, other, half, axis):
    return jnp.where(
        half == 0,
        jnp.concatenate([own, other], axis=axis),
        jnp.concatenate([other, own], axis=axis),
    )


def body(
    tokens,
    norm_gain,
    w_zx,
    w_bc,
    w_dt,
    conv_x,
    conv_bc,
    dt_bias,
    decay_rate,
    d_skip,
    gated_gain,
    w_out,
    prompt_lengths,
    pack_order,
    resume_prompt,
    carry_state,
    carry_conv_x,
    carry_conv_bc,
):
    own_rows = tokens.shape[0]
    row_count = 2 * own_rows
    edge_rows = conv_x.shape[0] - 1
    head_width = carry_state.shape[1]
    state_width = carry_state.shape[2]
    head_fsdp = w_dt.shape[1]
    group_fsdp = w_bc.shape[2] // state_width
    per_group = head_fsdp // group_fsdp
    head_local = head_fsdp // 2
    group_local = max(1, head_local // per_group)
    per_local = min(per_group, head_local)
    inner_local = head_local * head_width
    state_cols = group_local * state_width
    span_count = row_count // SPAN
    half = lax.axis_index("half")
    core = lax.axis_index("fsdp")
    core_count = lax.axis_size("fsdp")
    x_off = half * inner_local
    bc_off = (half * head_local) // per_group * state_width
    h_off = half * head_local

    def cut(value, axis, offset, width):
        return lax.dynamic_slice_in_dim(value, offset, width, axis)

    normed_own = norm_rows(tokens, norm_gain)
    share = own_rows // core_count
    fetched = swap_half(cut(normed_own, 0, core * share, share))
    normed_other = lax.all_gather(fetched, "fsdp", axis=0, tiled=True)
    normed = ordered_pair(normed_own, normed_other, half, 0)

    def first_cols(offset_x, offset_bc, offset_h):
        return jnp.concatenate(
            [
                cut(w_zx[:, 1], 1, offset_x, inner_local),
                cut(w_bc[:, 0], 1, offset_bc, state_cols),
                cut(w_bc[:, 1], 1, offset_bc, state_cols),
                cut(w_dt, 1, offset_h, head_local),
            ],
            axis=1,
        )

    other = 1 - half
    first_mine = first_cols(x_off, bc_off, h_off)
    first_theirs = swap_half(
        first_cols(other * inner_local, (other * head_local) // per_group * state_width, other * head_local)
    )
    first_local = ordered_pair(first_mine, first_theirs, half, 0)
    first_full = lax.all_gather(first_local, "pair", axis=0, tiled=True)
    proj_first = jnp.dot(normed, first_full, preferred_element_type=jnp.float32).astype(
        jnp.bfloat16
    )
    conv_width = inner_local + 2 * state_cols
    conv_in = proj_first[:, :conv_width]
    proj_dt = proj_first[:, conv_width:]
    w_z_all, w_out_all, _ = lax.optimization_barrier((w_zx[:, 0], w_out, proj_first))
    z_local = ordered_pair(
        cut(w_z_all, 1, x_off, inner_local),
        swap_half(cut(w_z_all, 1, other * inner_local, inner_local)),
        half,
        0,
    )
    out_local = ordered_pair(
        cut(w_out_all, 0, x_off, inner_local),
        swap_half(cut(w_out_all, 0, other * inner_local, inner_local)),
        half,
        1,
    )
    z_full = lax.all_gather(z_local, "pair", axis=0, tiled=True)
    out_full = lax.all_gather(out_local, "pair", axis=1, tiled=True)
    proj_z = jnp.dot(normed, z_full, preferred_element_type=jnp.float32).astype(jnp.bfloat16)

    position = lax.axis_index("pair") * row_count + jnp.arange(row_count, dtype=jnp.int32)
    segment, seg_start, resume_slot, resume_start = layout(
        prompt_lengths, pack_order, resume_prompt, position
    )
    prior_rows = from_behind(conv_in[row_count - edge_rows :], "pair", 1)
    weight = jnp.concatenate(
        [
            cut(conv_x, 1, x_off, inner_local),
            cut(conv_bc[:, 0], 1, bc_off, state_cols),
            cut(conv_bc[:, 1], 1, bc_off, state_cols),
        ],
        axis=1,
    )
    carry_rows = jnp.concatenate(
        [
            cut(carry_conv_x, 1, x_off, inner_local),
            cut(carry_conv_bc[:, 0], 1, bc_off, state_cols),
            cut(carry_conv_bc[:, 1], 1, bc_off, state_cols),
        ],
        axis=1,
    )
    conv_out = conv_rows(
        conv_in,
        prior_rows,
        weight,
        carry_rows,
        segment,
        seg_start,
        position,
        resume_slot,
        resume_start,
    )
    x_conv = conv_out[:, :inner_local].reshape(span_count, SPAN, group_local, per_local, head_width)
    b_conv = conv_out[:, inner_local : inner_local + state_cols].reshape(
        span_count, SPAN, group_local, state_width
    )
    c_conv = conv_out[:, inner_local + state_cols :].reshape(
        span_count, SPAN, group_local, state_width
    )
    dt_full = jax.nn.softplus(
        proj_dt.astype(jnp.float32) + cut(dt_bias, 0, h_off, head_local)[None, :]
    ).reshape(span_count, SPAN, group_local, per_local)
    seg_blocks = segment.reshape(span_count, SPAN)
    starting = (position == seg_start).reshape(span_count, SPAN)
    resumed = (segment == resume_slot).reshape(span_count, SPAN)
    resume_hit = (position == resume_start).reshape(span_count, SPAN)
    head_rate = cut(decay_rate, 0, h_off, head_local).reshape(group_local, per_local)
    skip_gain = cut(d_skip, 0, h_off, head_local).reshape(group_local, per_local)
    carry_init = cut(carry_state, 0, h_off, head_local).reshape(
        group_local, per_local, head_width, state_width
    )
    direct, state_gain, update, span_decay = span_pieces(
        x_conv,
        b_conv,
        c_conv,
        dt_full,
        head_rate,
        seg_blocks,
        starting,
        resumed,
        resume_hit,
        carry_init,
        skip_gain,
    )

    def fold_span(carried, pieces):
        return (
            (pieces[1][..., None, None] * carried[0] + pieces[0], pieces[1] * carried[1]),
            carried,
        )

    empty_state = jnp.zeros((group_local, per_local, head_width, state_width), jnp.float32)
    unit_decay = jnp.ones((group_local, per_local), jnp.float32)
    (local_state, local_decay), (prefix_state, prefix_decay) = lax.scan(
        fold_span, (empty_state, unit_decay), (update, span_decay)
    )
    hop_count = max(1, lax.axis_size("pair") // 4)
    incoming = jnp.zeros_like(local_state)
    reach = jnp.ones_like(local_decay)
    for steps in range(1, hop_count + 1):
        state_back, decay_back = from_behind((local_state, local_decay), "pair", steps)
        incoming = incoming + reach[..., None, None] * state_back
        reach = reach * decay_back
    entering = prefix_decay[..., None, None] * incoming[None] + prefix_state
    from_state = product_of("cghpn,cqgn->cqghp", entering, c_conv)
    ssd_out = (direct + state_gain[..., None] * from_state).reshape(row_count, inner_local)
    gate_act = jax.nn.silu(proj_z.astype(jnp.float32))
    gated = (ssd_out * gate_act).reshape(row_count, group_local, inner_local // group_local)
    squares = jnp.sum(gated * gated, axis=-1, keepdims=True)
    if head_local < per_group:
        squares = lax.psum(squares, "half")
    factor = lax.rsqrt(squares / (per_group * head_width) + EPS)
    normed_y = (
        (gated * factor).reshape(row_count, inner_local) * cut(gated_gain, 0, x_off, inner_local)[None, :]
    ).astype(jnp.bfloat16)
    piece = own_rows // core_count
    by_owner = normed_y.reshape(2, core_count, piece, inner_local)
    total = None
    for shift in list(range(1, core_count)) + [0]:
        rows = lax.dynamic_index_in_dim(by_owner, (core + shift) % core_count, 1, keepdims=False)
        part = jnp.einsum("hrc,cd->hrd", rows, out_full, preferred_element_type=jnp.float32)
        if shift:
            part = lax.ppermute(
                part, "fsdp", [(j, (j + shift) % core_count) for j in range(core_count)]
            )
        total = part if total is None else total + part
    mine = lax.dynamic_index_in_dim(total, half, 0, keepdims=False)
    theirs = swap_half(lax.dynamic_index_in_dim(total, 1 - half, 0, keepdims=False))
    return (mine + theirs).astype(jnp.bfloat16)


def solution(mesh):
    seq_count = mesh.shape["seq"]
    devices = mesh.devices.reshape(seq_count // 2, 2, mesh.shape["fsdp"])
    paired = jax.sharding.Mesh(devices, ("pair", "half", "fsdp"))
    seq = ("pair", "half")
    return jax.shard_map(
        body,
        mesh=paired,
        in_specs=(
            P(seq, None),
            P(),
            P(seq, None, "fsdp"),
            P(seq, None, "fsdp"),
            P(seq, "fsdp"),
            P(None, "fsdp"),
            P(None, None, "fsdp"),
            P("fsdp"),
            P("fsdp"),
            P("fsdp"),
            P("fsdp"),
            P("fsdp", seq),
            P(),
            P(),
            P(),
            P("fsdp", None, None),
            P(None, "fsdp"),
            P(None, None, "fsdp"),
        ),
        out_specs=P(("pair", "half", "fsdp"), None),
        check_vma=False,
    )
```

```python
import jax
import jax.numpy as jnp
from jax import lax
from jax.sharding import PartitionSpec as P

SPAN = 256


EPS = 1e-05


def from_behind(value, axis, steps):
    count = lax.axis_size(axis)
    leading, last = (max(0, -steps), min(count, count - steps))
    return lax.ppermute(value, axis, [(source, source + steps) for source in range(leading, last)])


def product_of(form, left, right):
    if left.dtype == jnp.bfloat16 and right.dtype == jnp.bfloat16:
        return jnp.einsum(form, left, right, preferred_element_type=jnp.float32)
    return jnp.einsum(form, left, right.astype(jnp.float32), precision=lax.Precision.HIGHEST)


def norm_rows(values, row_gain):
    widened = values.astype(jnp.float32)
    factor = lax.rsqrt(jnp.mean(widened * widened, axis=-1, keepdims=True) + EPS)
    return (widened * factor * row_gain[None, :]).astype(jnp.bfloat16)


def layout(prompt_lengths, pack_order, resume_prompt, position):
    prompt_count = pack_order.shape[0]
    slot_ids = jnp.arange(prompt_count, dtype=jnp.int32)
    ordered = jnp.sum(
        jnp.where(pack_order[:, None] == slot_ids[None, :], prompt_lengths[None, :], 0), axis=1
    )
    seg_starts = jnp.cumsum(ordered, dtype=jnp.int32) - ordered
    reached = position[:, None] >= seg_starts[None, :]
    segment = jnp.sum(reached.astype(jnp.int32), axis=1) - 1
    seg_start = jnp.max(jnp.where(reached, seg_starts[None, :], 0), axis=1)
    resume_slot = jnp.sum(jnp.where(pack_order == resume_prompt[0], slot_ids, 0))
    resume_start = jnp.sum(jnp.where(slot_ids == resume_slot, seg_starts, 0))
    return (segment, seg_start, resume_slot, resume_start)


def conv_rows(
    source, prior_rows, weight, carry_rows, segment, seg_start, position, resume_slot, resume_start
):
    row_count = source.shape[0]
    edge_rows = prior_rows.shape[0]
    extended = jnp.concatenate([prior_rows, source], axis=0)
    resumed = (segment == resume_slot)[:, None]
    summed = jnp.zeros(source.shape, jnp.float32)
    for back_by in range(edge_rows + 1):
        shifted = extended[edge_rows - back_by : edge_rows - back_by + row_count].astype(
            jnp.float32
        )
        inside = (position - back_by >= seg_start)[:, None]
        carry_index = position - back_by - resume_start + edge_rows
        from_carry = jnp.zeros(source.shape, jnp.float32)
        for slot_id in range(edge_rows):
            from_carry = from_carry + jnp.where(
                (carry_index == slot_id)[:, None],
                carry_rows[slot_id].astype(jnp.float32)[None, :],
                0.0,
            )
        chosen = jnp.where(inside, shifted, jnp.where(resumed, from_carry, 0.0))
        summed = summed + chosen * weight[edge_rows - back_by].astype(jnp.float32)[None, :]
    return jax.nn.silu(summed).astype(jnp.bfloat16)


def span_pieces(
    x_blocks,
    b_blocks,
    c_blocks,
    dt_blocks,
    head_rate,
    segment,
    starting,
    resumed,
    resume_hit,
    carry_init,
    skip_gain,
):
    block_len = segment.shape[1]
    log_decay = -dt_blocks * head_rate[None, None]
    cumulative = jnp.cumsum(log_decay, axis=1)
    indices = jnp.arange(block_len, dtype=jnp.int32)
    causal = (indices[:, None] >= indices[None, :])[None] & (
        segment[:, :, None] == segment[:, None, :]
    )
    cum_rows = jnp.moveaxis(cumulative, 1, -1)
    log_gap = cum_rows[..., :, None] - cum_rows[..., None, :]
    within = causal[:, None, None]
    decays = jnp.where(within, jnp.exp(jnp.where(within, log_gap, 0.0)), 0.0)
    scores = product_of("cqgn,csgn->cgqs", c_blocks, b_blocks)
    dt_source = jnp.moveaxis(dt_blocks, 1, -1)[..., None, :]
    weights = (scores[:, :, None] * decays * dt_source).astype(jnp.bfloat16)
    direct = product_of("cghqs,csghp->cqghp", weights, x_blocks)
    cum_end = cumulative[:, -1]
    tail_mask = (segment == segment[:, -1:])[:, :, None, None]
    to_end = (
        jnp.where(tail_mask, jnp.exp(jnp.where(tail_mask, cum_end[:, None] - cumulative, 0.0)), 0.0)
        * dt_blocks
    )
    scaled = (x_blocks.astype(jnp.float32) * to_end[..., None]).astype(jnp.bfloat16)
    update = product_of("cqghp,cqgn->cghpn", scaled, b_blocks)
    opened = jnp.any(starting, axis=1)
    span_decay = jnp.where(opened[:, None, None], 0.0, jnp.exp(cum_end))
    hit_mask = resume_hit[:, :, None, None]
    has_hit = jnp.any(resume_hit, axis=1)[:, None, None, None]
    cum_hit = jnp.sum(jnp.where(hit_mask, cumulative - log_decay, 0.0), axis=1, keepdims=True)
    carry_mask = resumed[:, :, None, None] & has_hit
    carry_gain = jnp.where(
        carry_mask, jnp.exp(jnp.where(carry_mask, cumulative - cum_hit, 0.0)), 0.0
    )
    end_gain = carry_gain[:, -1]
    update = update + end_gain[..., None, None] * carry_init[None]
    direct = direct + carry_gain[..., None] * product_of("ghpn,cqgn->cqghp", carry_init, c_blocks)
    direct = direct + skip_gain[None, None, :, :, None] * x_blocks.astype(jnp.float32)
    unopened = jnp.cumsum(starting.astype(jnp.int32), axis=1, dtype=jnp.int32) == 0
    state_gain = jnp.where(unopened[:, :, None, None], jnp.exp(cumulative), 0.0)
    return (direct, state_gain, update, span_decay)


def swap_half(value):
    count = lax.axis_size("half")
    return lax.ppermute(value, "half", [(k, count - 1 - k) for k in range(count)])


def ordered_pair(own, other, half, axis):
    return jnp.where(
        half == 0,
        jnp.concatenate([own, other], axis=axis),
        jnp.concatenate([other, own], axis=axis),
    )


def body(
    tokens,
    norm_gain,
    w_zx,
    w_bc,
    w_dt,
    conv_x,
    conv_bc,
    dt_bias,
    decay_rate,
    d_skip,
    gated_gain,
    w_out,
    prompt_lengths,
    pack_order,
    resume_prompt,
    carry_state,
    carry_conv_x,
    carry_conv_bc,
):
    own_rows = tokens.shape[0]
    row_count = 2 * own_rows
    edge_rows = conv_x.shape[0] - 1
    head_width = carry_state.shape[1]
    state_width = carry_state.shape[2]
    head_fsdp = w_dt.shape[1]
    group_fsdp = w_bc.shape[2] // state_width
    per_group = head_fsdp // group_fsdp
    head_local = head_fsdp // 2
    group_local = max(1, head_local // per_group)
    per_local = min(per_group, head_local)
    inner_local = head_local * head_width
    state_cols = group_local * state_width
    span_count = row_count // SPAN
    half = lax.axis_index("half")
    core = lax.axis_index("fsdp")
    core_count = lax.axis_size("fsdp")
    x_off = half * inner_local
    bc_off = (half * head_local) // per_group * state_width
    h_off = half * head_local

    def cut(value, axis, offset, width):
        return lax.dynamic_slice_in_dim(value, offset, width, axis)

    normed_own = norm_rows(tokens, norm_gain)
    share = own_rows // core_count
    fetched = swap_half(cut(normed_own, 0, core * share, share))
    arrived = [fetched] + [
        lax.ppermute(fetched, "fsdp", [(j, (j + shift) % core_count) for j in range(core_count)])
        for shift in range(1, core_count)
    ]
    arrived = jnp.stack(arrived)
    owners = (core - jnp.arange(core_count, dtype=jnp.int32)) % core_count
    normed_other = jnp.take(arrived, owners, axis=0).reshape(own_rows, tokens.shape[1])
    normed = ordered_pair(normed_own, normed_other, half, 0)

    def first_cols(offset_x, offset_bc, offset_h):
        return jnp.concatenate(
            [
                cut(w_zx[:, 1], 1, offset_x, inner_local),
                cut(w_bc[:, 0], 1, offset_bc, state_cols),
                cut(w_bc[:, 1], 1, offset_bc, state_cols),
                cut(w_dt, 1, offset_h, head_local),
            ],
            axis=1,
        )

    other = 1 - half
    first_mine = first_cols(x_off, bc_off, h_off)
    first_theirs = swap_half(
        first_cols(other * inner_local, (other * head_local) // per_group * state_width, other * head_local)
    )
    first_local = ordered_pair(first_mine, first_theirs, half, 0)
    first_full = lax.all_gather(first_local, "pair", axis=0, tiled=True)
    proj_first = jnp.dot(normed, first_full, preferred_element_type=jnp.float32).astype(
        jnp.bfloat16
    )
    conv_width = inner_local + 2 * state_cols
    conv_in = proj_first[:, :conv_width]
    proj_dt = proj_first[:, conv_width:]
    w_z_all, w_out_all, _ = lax.optimization_barrier((w_zx[:, 0], w_out, proj_first))
    z_local = ordered_pair(
        cut(w_z_all, 1, x_off, inner_local),
        swap_half(cut(w_z_all, 1, other * inner_local, inner_local)),
        half,
        0,
    )
    out_local = ordered_pair(
        cut(w_out_all, 0, x_off, inner_local),
        swap_half(cut(w_out_all, 0, other * inner_local, inner_local)),
        half,
        1,
    )
    z_full = lax.all_gather(z_local, "pair", axis=0, tiled=True)
    out_full = lax.all_gather(out_local, "pair", axis=1, tiled=True)
    proj_z = jnp.dot(normed, z_full, preferred_element_type=jnp.float32).astype(jnp.bfloat16)

    position = lax.axis_index("pair") * row_count + jnp.arange(row_count, dtype=jnp.int32)
    segment, seg_start, resume_slot, resume_start = layout(
        prompt_lengths, pack_order, resume_prompt, position
    )
    prior_rows = from_behind(conv_in[row_count - edge_rows :], "pair", 1)
    weight = jnp.concatenate(
        [
            cut(conv_x, 1, x_off, inner_local),
            cut(conv_bc[:, 0], 1, bc_off, state_cols),
            cut(conv_bc[:, 1], 1, bc_off, state_cols),
        ],
        axis=1,
    )
    carry_rows = jnp.concatenate(
        [
            cut(carry_conv_x, 1, x_off, inner_local),
            cut(carry_conv_bc[:, 0], 1, bc_off, state_cols),
            cut(carry_conv_bc[:, 1], 1, bc_off, state_cols),
        ],
        axis=1,
    )
    conv_out = conv_rows(
        conv_in,
        prior_rows,
        weight,
        carry_rows,
        segment,
        seg_start,
        position,
        resume_slot,
        resume_start,
    )
    x_conv = conv_out[:, :inner_local].reshape(span_count, SPAN, group_local, per_local, head_width)
    b_conv = conv_out[:, inner_local : inner_local + state_cols].reshape(
        span_count, SPAN, group_local, state_width
    )
    c_conv = conv_out[:, inner_local + state_cols :].reshape(
        span_count, SPAN, group_local, state_width
    )
    dt_full = jax.nn.softplus(
        proj_dt.astype(jnp.float32) + cut(dt_bias, 0, h_off, head_local)[None, :]
    ).reshape(span_count, SPAN, group_local, per_local)
    seg_blocks = segment.reshape(span_count, SPAN)
    starting = (position == seg_start).reshape(span_count, SPAN)
    resumed = (segment == resume_slot).reshape(span_count, SPAN)
    resume_hit = (position == resume_start).reshape(span_count, SPAN)
    head_rate = cut(decay_rate, 0, h_off, head_local).reshape(group_local, per_local)
    skip_gain = cut(d_skip, 0, h_off, head_local).reshape(group_local, per_local)
    carry_init = cut(carry_state, 0, h_off, head_local).reshape(
        group_local, per_local, head_width, state_width
    )
    direct, state_gain, update, span_decay = span_pieces(
        x_conv,
        b_conv,
        c_conv,
        dt_full,
        head_rate,
        seg_blocks,
        starting,
        resumed,
        resume_hit,
        carry_init,
        skip_gain,
    )

    def fold_span(carried, pieces):
        return (
            (pieces[1][..., None, None] * carried[0] + pieces[0], pieces[1] * carried[1]),
            carried,
        )

    empty_state = jnp.zeros((group_local, per_local, head_width, state_width), jnp.float32)
    unit_decay = jnp.ones((group_local, per_local), jnp.float32)
    (local_state, local_decay), (prefix_state, prefix_decay) = lax.scan(
        fold_span, (empty_state, unit_decay), (update, span_decay)
    )
    hop_count = max(1, lax.axis_size("pair") // 4)
    incoming = jnp.zeros_like(local_state)
    reach = jnp.ones_like(local_decay)
    for steps in range(1, hop_count + 1):
        state_back, decay_back = from_behind((local_state, local_decay), "pair", steps)
        incoming = incoming + reach[..., None, None] * state_back
        reach = reach * decay_back
    entering = prefix_decay[..., None, None] * incoming[None] + prefix_state
    from_state = product_of("cghpn,cqgn->cqghp", entering, c_conv)
    ssd_out = (direct + state_gain[..., None] * from_state).reshape(row_count, inner_local)
    gate_act = jax.nn.silu(proj_z.astype(jnp.float32))
    gated = (ssd_out * gate_act).reshape(row_count, group_local, inner_local // group_local)
    squares = jnp.sum(gated * gated, axis=-1, keepdims=True)
    if head_local < per_group:
        squares = lax.psum(squares, "half")
    factor = lax.rsqrt(squares / (per_group * head_width) + EPS)
    normed_y = (
        (gated * factor).reshape(row_count, inner_local) * cut(gated_gain, 0, x_off, inner_local)[None, :]
    ).astype(jnp.bfloat16)
    piece = own_rows // core_count
    by_owner = normed_y.reshape(2, core_count, piece, inner_local)
    chunk_count = 2
    chunk = out_full.shape[1] // chunk_count
    results = []
    for index in range(chunk_count):
        columns = out_full[:, index * chunk : (index + 1) * chunk]
        total = None
        for shift in list(range(1, core_count)) + [0]:
            rows = lax.dynamic_index_in_dim(by_owner, (core + shift) % core_count, 1, keepdims=False)
            part = jnp.einsum("hrc,cd->hrd", rows, columns, preferred_element_type=jnp.float32)
            if shift:
                part = lax.ppermute(
                    part, "fsdp", [(j, (j + shift) % core_count) for j in range(core_count)]
                )
            total = part if total is None else total + part
        mine = lax.dynamic_index_in_dim(total, half, 0, keepdims=False)
        theirs = lax.dynamic_index_in_dim(total, 1 - half, 0, keepdims=False)
        theirs = swap_half(theirs.astype(jnp.bfloat16))
        results.append((mine + theirs.astype(jnp.float32)).astype(jnp.bfloat16))
    return jnp.concatenate(results, axis=1)


def solution(mesh):
    seq_count = mesh.shape["seq"]
    devices = mesh.devices.reshape(seq_count // 2, 2, mesh.shape["fsdp"])
    paired = jax.sharding.Mesh(devices, ("pair", "half", "fsdp"))
    seq = ("pair", "half")
    return jax.shard_map(
        body,
        mesh=paired,
        in_specs=(
            P(seq, None),
            P(),
            P(seq, None, "fsdp"),
            P(seq, None, "fsdp"),
            P(seq, "fsdp"),
            P(None, "fsdp"),
            P(None, None, "fsdp"),
            P("fsdp"),
            P("fsdp"),
            P("fsdp"),
            P("fsdp"),
            P("fsdp", seq),
            P(),
            P(),
            P(),
            P("fsdp", None, None),
            P(None, "fsdp"),
            P(None, None, "fsdp"),
        ),
        out_specs=P(("pair", "half", "fsdp"), None),
        check_vma=False,
    )
```

```python
import jax
import jax.numpy as jnp
from jax import lax
from jax.sharding import PartitionSpec as P

SPAN = 256


EPS = 1e-05


def from_behind(value, axis, steps):
    count = lax.axis_size(axis)
    leading, last = (max(0, -steps), min(count, count - steps))
    return lax.ppermute(value, axis, [(source, source + steps) for source in range(leading, last)])


def product_of(form, left, right):
    if left.dtype == jnp.bfloat16 and right.dtype == jnp.bfloat16:
        return jnp.einsum(form, left, right, preferred_element_type=jnp.float32)
    return jnp.einsum(form, left, right.astype(jnp.float32), precision=lax.Precision.HIGHEST)


def norm_rows(values, row_gain):
    widened = values.astype(jnp.float32)
    factor = lax.rsqrt(jnp.mean(widened * widened, axis=-1, keepdims=True) + EPS)
    return (widened * factor * row_gain[None, :]).astype(jnp.bfloat16)


def layout(prompt_lengths, pack_order, resume_prompt, position):
    prompt_count = pack_order.shape[0]
    slot_ids = jnp.arange(prompt_count, dtype=jnp.int32)
    ordered = jnp.sum(
        jnp.where(pack_order[:, None] == slot_ids[None, :], prompt_lengths[None, :], 0), axis=1
    )
    seg_starts = jnp.cumsum(ordered, dtype=jnp.int32) - ordered
    reached = position[:, None] >= seg_starts[None, :]
    segment = jnp.sum(reached.astype(jnp.int32), axis=1) - 1
    seg_start = jnp.max(jnp.where(reached, seg_starts[None, :], 0), axis=1)
    resume_slot = jnp.sum(jnp.where(pack_order == resume_prompt[0], slot_ids, 0))
    resume_start = jnp.sum(jnp.where(slot_ids == resume_slot, seg_starts, 0))
    return (segment, seg_start, resume_slot, resume_start)


def conv_rows(
    source, prior_rows, weight, carry_rows, segment, seg_start, position, resume_slot, resume_start
):
    row_count = source.shape[0]
    edge_rows = prior_rows.shape[0]
    extended = jnp.concatenate([prior_rows, source], axis=0)
    resumed = (segment == resume_slot)[:, None]
    summed = jnp.zeros(source.shape, jnp.float32)
    for back_by in range(edge_rows + 1):
        shifted = extended[edge_rows - back_by : edge_rows - back_by + row_count].astype(
            jnp.float32
        )
        inside = (position - back_by >= seg_start)[:, None]
        carry_index = position - back_by - resume_start + edge_rows
        from_carry = jnp.zeros(source.shape, jnp.float32)
        for slot_id in range(edge_rows):
            from_carry = from_carry + jnp.where(
                (carry_index == slot_id)[:, None],
                carry_rows[slot_id].astype(jnp.float32)[None, :],
                0.0,
            )
        chosen = jnp.where(inside, shifted, jnp.where(resumed, from_carry, 0.0))
        summed = summed + chosen * weight[edge_rows - back_by].astype(jnp.float32)[None, :]
    return jax.nn.silu(summed).astype(jnp.bfloat16)


def span_pieces(
    x_blocks,
    b_blocks,
    c_blocks,
    dt_blocks,
    head_rate,
    segment,
    starting,
    resumed,
    resume_hit,
    carry_init,
    skip_gain,
):
    block_len = segment.shape[1]
    log_decay = -dt_blocks * head_rate[None, None]
    cumulative = jnp.cumsum(log_decay, axis=1)
    indices = jnp.arange(block_len, dtype=jnp.int32)
    causal = (indices[:, None] >= indices[None, :])[None] & (
        segment[:, :, None] == segment[:, None, :]
    )
    cum_rows = jnp.moveaxis(cumulative, 1, -1)
    log_gap = cum_rows[..., :, None] - cum_rows[..., None, :]
    within = causal[:, None, None]
    decays = jnp.where(within, jnp.exp(jnp.where(within, log_gap, 0.0)), 0.0)
    scores = product_of("cqgn,csgn->cgqs", c_blocks, b_blocks)
    dt_source = jnp.moveaxis(dt_blocks, 1, -1)[..., None, :]
    weights = (scores[:, :, None] * decays * dt_source).astype(jnp.bfloat16)
    direct = product_of("cghqs,csghp->cqghp", weights, x_blocks)
    cum_end = cumulative[:, -1]
    tail_mask = (segment == segment[:, -1:])[:, :, None, None]
    to_end = (
        jnp.where(tail_mask, jnp.exp(jnp.where(tail_mask, cum_end[:, None] - cumulative, 0.0)), 0.0)
        * dt_blocks
    )
    scaled = (x_blocks.astype(jnp.float32) * to_end[..., None]).astype(jnp.bfloat16)
    update = product_of("cqghp,cqgn->cghpn", scaled, b_blocks)
    opened = jnp.any(starting, axis=1)
    span_decay = jnp.where(opened[:, None, None], 0.0, jnp.exp(cum_end))
    hit_mask = resume_hit[:, :, None, None]
    has_hit = jnp.any(resume_hit, axis=1)[:, None, None, None]
    cum_hit = jnp.sum(jnp.where(hit_mask, cumulative - log_decay, 0.0), axis=1, keepdims=True)
    carry_mask = resumed[:, :, None, None] & has_hit
    carry_gain = jnp.where(
        carry_mask, jnp.exp(jnp.where(carry_mask, cumulative - cum_hit, 0.0)), 0.0
    )
    end_gain = carry_gain[:, -1]
    update = update + end_gain[..., None, None] * carry_init[None]
    direct = direct + carry_gain[..., None] * product_of("ghpn,cqgn->cqghp", carry_init, c_blocks)
    direct = direct + skip_gain[None, None, :, :, None] * x_blocks.astype(jnp.float32)
    unopened = jnp.cumsum(starting.astype(jnp.int32), axis=1, dtype=jnp.int32) == 0
    state_gain = jnp.where(unopened[:, :, None, None], jnp.exp(cumulative), 0.0)
    return (direct, state_gain, update, span_decay)


def swap_half(value):
    count = lax.axis_size("half")
    return lax.ppermute(value, "half", [(k, count - 1 - k) for k in range(count)])


def ordered_pair(own, other, half, axis):
    return jnp.where(
        half == 0,
        jnp.concatenate([own, other], axis=axis),
        jnp.concatenate([other, own], axis=axis),
    )


def body(
    tokens,
    norm_gain,
    w_zx,
    w_bc,
    w_dt,
    conv_x,
    conv_bc,
    dt_bias,
    decay_rate,
    d_skip,
    gated_gain,
    w_out,
    prompt_lengths,
    pack_order,
    resume_prompt,
    carry_state,
    carry_conv_x,
    carry_conv_bc,
):
    own_rows = tokens.shape[0]
    row_count = 2 * own_rows
    edge_rows = conv_x.shape[0] - 1
    head_width = carry_state.shape[1]
    state_width = carry_state.shape[2]
    head_fsdp = w_dt.shape[1]
    group_fsdp = w_bc.shape[2] // state_width
    per_group = head_fsdp // group_fsdp
    head_local = head_fsdp // 2
    group_local = max(1, head_local // per_group)
    per_local = min(per_group, head_local)
    inner_local = head_local * head_width
    state_cols = group_local * state_width
    span_count = row_count // SPAN
    half = lax.axis_index("half")
    core = lax.axis_index("fsdp")
    core_count = lax.axis_size("fsdp")
    x_off = half * inner_local
    bc_off = (half * head_local) // per_group * state_width
    h_off = half * head_local

    def cut(value, axis, offset, width):
        return lax.dynamic_slice_in_dim(value, offset, width, axis)

    normed_own = norm_rows(tokens, norm_gain)
    share = own_rows // core_count
    fetched = swap_half(cut(normed_own, 0, core * share, share))
    arrived = [fetched] + [
        lax.ppermute(fetched, "fsdp", [(j, (j + shift) % core_count) for j in range(core_count)])
        for shift in range(1, core_count)
    ]
    arrived = jnp.stack(arrived)
    owners = (core - jnp.arange(core_count, dtype=jnp.int32)) % core_count
    normed_other = jnp.take(arrived, owners, axis=0).reshape(own_rows, tokens.shape[1])
    normed = ordered_pair(normed_own, normed_other, half, 0)

    def first_cols(offset_x, offset_bc, offset_h):
        return jnp.concatenate(
            [
                cut(w_zx[:, 1], 1, offset_x, inner_local),
                cut(w_bc[:, 0], 1, offset_bc, state_cols),
                cut(w_bc[:, 1], 1, offset_bc, state_cols),
                cut(w_dt, 1, offset_h, head_local),
            ],
            axis=1,
        )

    other = 1 - half
    first_mine = first_cols(x_off, bc_off, h_off)
    first_theirs = swap_half(
        first_cols(other * inner_local, (other * head_local) // per_group * state_width, other * head_local)
    )
    first_local = ordered_pair(first_mine, first_theirs, half, 0)
    first_full = lax.all_gather(first_local, "pair", axis=0, tiled=True)
    proj_first = jnp.dot(normed, first_full, preferred_element_type=jnp.float32).astype(
        jnp.bfloat16
    )
    conv_width = inner_local + 2 * state_cols
    conv_in = proj_first[:, :conv_width]
    proj_dt = proj_first[:, conv_width:]
    w_z_all, w_out_all, _ = lax.optimization_barrier((w_zx[:, 0], w_out, proj_first))
    z_local = ordered_pair(
        cut(w_z_all, 1, x_off, inner_local),
        swap_half(cut(w_z_all, 1, other * inner_local, inner_local)),
        half,
        0,
    )
    out_local = ordered_pair(
        cut(w_out_all, 0, x_off, inner_local),
        swap_half(cut(w_out_all, 0, other * inner_local, inner_local)),
        half,
        1,
    )
    z_full = lax.all_gather(z_local, "pair", axis=0, tiled=True)
    block = out_local.shape[1] // 2
    out_first, _ = lax.optimization_barrier((out_local[:, :block], z_full))
    out_first = lax.all_gather(out_first, "pair", axis=1, tiled=True)
    out_second, _ = lax.optimization_barrier((out_local[:, block:], out_first))
    out_second = lax.all_gather(out_second, "pair", axis=1, tiled=True)
    proj_z = jnp.dot(normed, z_full, preferred_element_type=jnp.float32).astype(jnp.bfloat16)

    position = lax.axis_index("pair") * row_count + jnp.arange(row_count, dtype=jnp.int32)
    segment, seg_start, resume_slot, resume_start = layout(
        prompt_lengths, pack_order, resume_prompt, position
    )
    prior_rows = from_behind(conv_in[row_count - edge_rows :], "pair", 1)
    weight = jnp.concatenate(
        [
            cut(conv_x, 1, x_off, inner_local),
            cut(conv_bc[:, 0], 1, bc_off, state_cols),
            cut(conv_bc[:, 1], 1, bc_off, state_cols),
        ],
        axis=1,
    )
    carry_rows = jnp.concatenate(
        [
            cut(carry_conv_x, 1, x_off, inner_local),
            cut(carry_conv_bc[:, 0], 1, bc_off, state_cols),
            cut(carry_conv_bc[:, 1], 1, bc_off, state_cols),
        ],
        axis=1,
    )
    conv_out = conv_rows(
        conv_in,
        prior_rows,
        weight,
        carry_rows,
        segment,
        seg_start,
        position,
        resume_slot,
        resume_start,
    )
    x_conv = conv_out[:, :inner_local].reshape(span_count, SPAN, group_local, per_local, head_width)
    b_conv = conv_out[:, inner_local : inner_local + state_cols].reshape(
        span_count, SPAN, group_local, state_width
    )
    c_conv = conv_out[:, inner_local + state_cols :].reshape(
        span_count, SPAN, group_local, state_width
    )
    dt_full = jax.nn.softplus(
        proj_dt.astype(jnp.float32) + cut(dt_bias, 0, h_off, head_local)[None, :]
    ).reshape(span_count, SPAN, group_local, per_local)
    seg_blocks = segment.reshape(span_count, SPAN)
    starting = (position == seg_start).reshape(span_count, SPAN)
    resumed = (segment == resume_slot).reshape(span_count, SPAN)
    resume_hit = (position == resume_start).reshape(span_count, SPAN)
    head_rate = cut(decay_rate, 0, h_off, head_local).reshape(group_local, per_local)
    skip_gain = cut(d_skip, 0, h_off, head_local).reshape(group_local, per_local)
    carry_init = cut(carry_state, 0, h_off, head_local).reshape(
        group_local, per_local, head_width, state_width
    )
    direct, state_gain, update, span_decay = span_pieces(
        x_conv,
        b_conv,
        c_conv,
        dt_full,
        head_rate,
        seg_blocks,
        starting,
        resumed,
        resume_hit,
        carry_init,
        skip_gain,
    )

    def fold_span(carried, pieces):
        return (
            (pieces[1][..., None, None] * carried[0] + pieces[0], pieces[1] * carried[1]),
            carried,
        )

    empty_state = jnp.zeros((group_local, per_local, head_width, state_width), jnp.float32)
    unit_decay = jnp.ones((group_local, per_local), jnp.float32)
    (local_state, local_decay), (prefix_state, prefix_decay) = lax.scan(
        fold_span, (empty_state, unit_decay), (update, span_decay)
    )
    hop_count = max(1, lax.axis_size("pair") // 4)
    incoming = jnp.zeros_like(local_state)
    reach = jnp.ones_like(local_decay)
    for steps in range(1, hop_count + 1):
        state_back, decay_back = from_behind((local_state, local_decay), "pair", steps)
        incoming = incoming + reach[..., None, None] * state_back
        reach = reach * decay_back
    entering = prefix_decay[..., None, None] * incoming[None] + prefix_state
    from_state = product_of("cghpn,cqgn->cqghp", entering, c_conv)
    ssd_out = (direct + state_gain[..., None] * from_state).reshape(row_count, inner_local)
    gate_act = jax.nn.silu(proj_z.astype(jnp.float32))
    gated = (ssd_out * gate_act).reshape(row_count, group_local, inner_local // group_local)
    squares = jnp.sum(gated * gated, axis=-1, keepdims=True)
    if head_local < per_group:
        squares = lax.psum(squares, "half")
    factor = lax.rsqrt(squares / (per_group * head_width) + EPS)
    normed_y = (
        (gated * factor).reshape(row_count, inner_local) * cut(gated_gain, 0, x_off, inner_local)[None, :]
    ).astype(jnp.bfloat16)
    piece = own_rows // core_count
    by_owner = normed_y.reshape(2, core_count, piece, inner_local)
    results = []
    for columns in (out_first, out_second):
        total = None
        for shift in list(range(1, core_count)) + [0]:
            rows = lax.dynamic_index_in_dim(by_owner, (core + shift) % core_count, 1, keepdims=False)
            part = jnp.einsum("hrc,cd->hrd", rows, columns, preferred_element_type=jnp.float32)
            if shift:
                part = lax.ppermute(
                    part, "fsdp", [(j, (j + shift) % core_count) for j in range(core_count)]
                )
            total = part if total is None else total + part
        mine = lax.dynamic_index_in_dim(total, half, 0, keepdims=False)
        theirs = lax.dynamic_index_in_dim(total, 1 - half, 0, keepdims=False)
        theirs = swap_half(theirs.astype(jnp.bfloat16))
        results.append((mine + theirs.astype(jnp.float32)).astype(jnp.bfloat16))
    pair_count = lax.axis_size("pair")
    joined = jnp.stack([r.reshape(piece, pair_count, block) for r in results], axis=2)
    return joined.reshape(piece, 2 * pair_count * block)


def solution(mesh):
    seq_count = mesh.shape["seq"]
    devices = mesh.devices.reshape(seq_count // 2, 2, mesh.shape["fsdp"])
    paired = jax.sharding.Mesh(devices, ("pair", "half", "fsdp"))
    seq = ("pair", "half")
    return jax.shard_map(
        body,
        mesh=paired,
        in_specs=(
            P(seq, None),
            P(),
            P(seq, None, "fsdp"),
            P(seq, None, "fsdp"),
            P(seq, "fsdp"),
            P(None, "fsdp"),
            P(None, None, "fsdp"),
            P("fsdp"),
            P("fsdp"),
            P("fsdp"),
            P("fsdp"),
            P("fsdp", seq),
            P(),
            P(),
            P(),
            P("fsdp", None, None),
            P(None, "fsdp"),
            P(None, None, "fsdp"),
        ),
        out_specs=P(("pair", "half", "fsdp"), None),
        check_vma=False,
    )
```

```python
import jax
import jax.numpy as jnp
from jax import lax
from jax.sharding import PartitionSpec as P

SPAN = 256


EPS = 1e-05


def from_behind(value, axis, steps):
    count = lax.axis_size(axis)
    leading, last = (max(0, -steps), min(count, count - steps))
    return lax.ppermute(value, axis, [(source, source + steps) for source in range(leading, last)])


def product_of(form, left, right):
    if left.dtype == jnp.bfloat16 and right.dtype == jnp.bfloat16:
        return jnp.einsum(form, left, right, preferred_element_type=jnp.float32)
    return jnp.einsum(form, left, right.astype(jnp.float32), precision=lax.Precision.HIGHEST)


def norm_rows(values, row_gain):
    widened = values.astype(jnp.float32)
    factor = lax.rsqrt(jnp.mean(widened * widened, axis=-1, keepdims=True) + EPS)
    return (widened * factor * row_gain[None, :]).astype(jnp.bfloat16)


def layout(prompt_lengths, pack_order, resume_prompt, position):
    prompt_count = pack_order.shape[0]
    slot_ids = jnp.arange(prompt_count, dtype=jnp.int32)
    ordered = jnp.sum(
        jnp.where(pack_order[:, None] == slot_ids[None, :], prompt_lengths[None, :], 0), axis=1
    )
    seg_starts = jnp.cumsum(ordered, dtype=jnp.int32) - ordered
    reached = position[:, None] >= seg_starts[None, :]
    segment = jnp.sum(reached.astype(jnp.int32), axis=1) - 1
    seg_start = jnp.max(jnp.where(reached, seg_starts[None, :], 0), axis=1)
    resume_slot = jnp.sum(jnp.where(pack_order == resume_prompt[0], slot_ids, 0))
    resume_start = jnp.sum(jnp.where(slot_ids == resume_slot, seg_starts, 0))
    return (segment, seg_start, resume_slot, resume_start)


def conv_rows(
    source, prior_rows, weight, carry_rows, segment, seg_start, position, resume_slot, resume_start
):
    row_count = source.shape[0]
    edge_rows = prior_rows.shape[0]
    extended = jnp.concatenate([prior_rows, source], axis=0)
    resumed = (segment == resume_slot)[:, None]
    summed = jnp.zeros(source.shape, jnp.float32)
    for back_by in range(edge_rows + 1):
        shifted = extended[edge_rows - back_by : edge_rows - back_by + row_count].astype(
            jnp.float32
        )
        inside = (position - back_by >= seg_start)[:, None]
        carry_index = position - back_by - resume_start + edge_rows
        from_carry = jnp.zeros(source.shape, jnp.float32)
        for slot_id in range(edge_rows):
            from_carry = from_carry + jnp.where(
                (carry_index == slot_id)[:, None],
                carry_rows[slot_id].astype(jnp.float32)[None, :],
                0.0,
            )
        chosen = jnp.where(inside, shifted, jnp.where(resumed, from_carry, 0.0))
        summed = summed + chosen * weight[edge_rows - back_by].astype(jnp.float32)[None, :]
    return jax.nn.silu(summed).astype(jnp.bfloat16)


def span_pieces(
    x_blocks,
    b_blocks,
    c_blocks,
    dt_blocks,
    head_rate,
    segment,
    starting,
    resumed,
    resume_hit,
    carry_init,
    skip_gain,
):
    block_len = segment.shape[1]
    log_decay = -dt_blocks * head_rate[None, None]
    cumulative = jnp.cumsum(log_decay, axis=1)
    indices = jnp.arange(block_len, dtype=jnp.int32)
    causal = (indices[:, None] >= indices[None, :])[None] & (
        segment[:, :, None] == segment[:, None, :]
    )
    cum_rows = jnp.moveaxis(cumulative, 1, -1)
    log_gap = cum_rows[..., :, None] - cum_rows[..., None, :]
    within = causal[:, None, None]
    decays = jnp.where(within, jnp.exp(jnp.where(within, log_gap, 0.0)), 0.0)
    scores = product_of("cqgn,csgn->cgqs", c_blocks, b_blocks)
    dt_source = jnp.moveaxis(dt_blocks, 1, -1)[..., None, :]
    weights = (scores[:, :, None] * decays * dt_source).astype(jnp.bfloat16)
    direct = product_of("cghqs,csghp->cqghp", weights, x_blocks)
    cum_end = cumulative[:, -1]
    tail_mask = (segment == segment[:, -1:])[:, :, None, None]
    to_end = (
        jnp.where(tail_mask, jnp.exp(jnp.where(tail_mask, cum_end[:, None] - cumulative, 0.0)), 0.0)
        * dt_blocks
    )
    scaled = (x_blocks.astype(jnp.float32) * to_end[..., None]).astype(jnp.bfloat16)
    update = product_of("cqghp,cqgn->cghpn", scaled, b_blocks)
    opened = jnp.any(starting, axis=1)
    span_decay = jnp.where(opened[:, None, None], 0.0, jnp.exp(cum_end))
    hit_mask = resume_hit[:, :, None, None]
    has_hit = jnp.any(resume_hit, axis=1)[:, None, None, None]
    cum_hit = jnp.sum(jnp.where(hit_mask, cumulative - log_decay, 0.0), axis=1, keepdims=True)
    carry_mask = resumed[:, :, None, None] & has_hit
    carry_gain = jnp.where(
        carry_mask, jnp.exp(jnp.where(carry_mask, cumulative - cum_hit, 0.0)), 0.0
    )
    end_gain = carry_gain[:, -1]
    update = update + end_gain[..., None, None] * carry_init[None]
    direct = direct + carry_gain[..., None] * product_of("ghpn,cqgn->cqghp", carry_init, c_blocks)
    direct = direct + skip_gain[None, None, :, :, None] * x_blocks.astype(jnp.float32)
    unopened = jnp.cumsum(starting.astype(jnp.int32), axis=1, dtype=jnp.int32) == 0
    state_gain = jnp.where(unopened[:, :, None, None], jnp.exp(cumulative), 0.0)
    return (direct, state_gain, update, span_decay)


def swap_half(value):
    count = lax.axis_size("half")
    return lax.ppermute(value, "half", [(k, count - 1 - k) for k in range(count)])


def ordered_pair(own, other, half, axis):
    return jnp.where(
        half == 0,
        jnp.concatenate([own, other], axis=axis),
        jnp.concatenate([other, own], axis=axis),
    )


def body(
    tokens,
    norm_gain,
    w_zx,
    w_bc,
    w_dt,
    conv_x,
    conv_bc,
    dt_bias,
    decay_rate,
    d_skip,
    gated_gain,
    w_out,
    prompt_lengths,
    pack_order,
    resume_prompt,
    carry_state,
    carry_conv_x,
    carry_conv_bc,
):
    own_rows = tokens.shape[0]
    row_count = 2 * own_rows
    edge_rows = conv_x.shape[0] - 1
    head_width = carry_state.shape[1]
    state_width = carry_state.shape[2]
    head_fsdp = w_dt.shape[1]
    group_fsdp = w_bc.shape[2] // state_width
    per_group = head_fsdp // group_fsdp
    head_local = head_fsdp // 2
    group_local = max(1, head_local // per_group)
    per_local = min(per_group, head_local)
    inner_local = head_local * head_width
    state_cols = group_local * state_width
    span_count = row_count // SPAN
    half = lax.axis_index("half")
    core = lax.axis_index("fsdp")
    core_count = lax.axis_size("fsdp")
    x_off = half * inner_local
    bc_off = (half * head_local) // per_group * state_width
    h_off = half * head_local

    def cut(value, axis, offset, width):
        return lax.dynamic_slice_in_dim(value, offset, width, axis)

    normed_own = norm_rows(tokens, norm_gain)
    share = own_rows // core_count
    fetched = swap_half(cut(normed_own, 0, core * share, share))
    arrived = [fetched] + [
        lax.ppermute(fetched, "fsdp", [(j, (j + shift) % core_count) for j in range(core_count)])
        for shift in range(1, core_count)
    ]
    arrived = jnp.stack(arrived)
    owners = (core - jnp.arange(core_count, dtype=jnp.int32)) % core_count
    normed_other = jnp.take(arrived, owners, axis=0).reshape(own_rows, tokens.shape[1])
    normed = ordered_pair(normed_own, normed_other, half, 0)

    def first_cols(offset_x, offset_bc, offset_h):
        return jnp.concatenate(
            [
                cut(w_zx[:, 1], 1, offset_x, inner_local),
                cut(w_bc[:, 0], 1, offset_bc, state_cols),
                cut(w_bc[:, 1], 1, offset_bc, state_cols),
                cut(w_dt, 1, offset_h, head_local),
            ],
            axis=1,
        )

    other = 1 - half
    first_mine = first_cols(x_off, bc_off, h_off)
    first_theirs = swap_half(
        first_cols(other * inner_local, (other * head_local) // per_group * state_width, other * head_local)
    )
    first_local = ordered_pair(first_mine, first_theirs, half, 0)
    first_full = lax.all_gather(first_local, "pair", axis=0, tiled=True)
    proj_first = jnp.dot(normed, first_full, preferred_element_type=jnp.float32).astype(
        jnp.bfloat16
    )
    conv_width = inner_local + 2 * state_cols
    conv_in = proj_first[:, :conv_width]
    proj_dt = proj_first[:, conv_width:]
    w_z_all, w_out_all, _ = lax.optimization_barrier((w_zx[:, 0], w_out, proj_first))
    z_local = ordered_pair(
        cut(w_z_all, 1, x_off, inner_local),
        swap_half(cut(w_z_all, 1, other * inner_local, inner_local)),
        half,
        0,
    )
    out_local = ordered_pair(
        cut(w_out_all, 0, x_off, inner_local),
        swap_half(cut(w_out_all, 0, other * inner_local, inner_local)),
        half,
        1,
    )
    z_full = lax.all_gather(z_local, "pair", axis=0, tiled=True)
    block = out_local.shape[1] // 2
    out_first = lax.all_gather(out_local[:, :block], "pair", axis=1, tiled=True)
    out_second = lax.all_gather(out_local[:, block:], "pair", axis=1, tiled=True)
    proj_z = jnp.dot(normed, z_full, preferred_element_type=jnp.float32).astype(jnp.bfloat16)

    position = lax.axis_index("pair") * row_count + jnp.arange(row_count, dtype=jnp.int32)
    segment, seg_start, resume_slot, resume_start = layout(
        prompt_lengths, pack_order, resume_prompt, position
    )
    prior_rows = from_behind(conv_in[row_count - edge_rows :], "pair", 1)
    weight = jnp.concatenate(
        [
            cut(conv_x, 1, x_off, inner_local),
            cut(conv_bc[:, 0], 1, bc_off, state_cols),
            cut(conv_bc[:, 1], 1, bc_off, state_cols),
        ],
        axis=1,
    )
    carry_rows = jnp.concatenate(
        [
            cut(carry_conv_x, 1, x_off, inner_local),
            cut(carry_conv_bc[:, 0], 1, bc_off, state_cols),
            cut(carry_conv_bc[:, 1], 1, bc_off, state_cols),
        ],
        axis=1,
    )
    conv_out = conv_rows(
        conv_in,
        prior_rows,
        weight,
        carry_rows,
        segment,
        seg_start,
        position,
        resume_slot,
        resume_start,
    )
    x_conv = conv_out[:, :inner_local].reshape(span_count, SPAN, group_local, per_local, head_width)
    b_conv = conv_out[:, inner_local : inner_local + state_cols].reshape(
        span_count, SPAN, group_local, state_width
    )
    c_conv = conv_out[:, inner_local + state_cols :].reshape(
        span_count, SPAN, group_local, state_width
    )
    dt_full = jax.nn.softplus(
        proj_dt.astype(jnp.float32) + cut(dt_bias, 0, h_off, head_local)[None, :]
    ).reshape(span_count, SPAN, group_local, per_local)
    seg_blocks = segment.reshape(span_count, SPAN)
    starting = (position == seg_start).reshape(span_count, SPAN)
    resumed = (segment == resume_slot).reshape(span_count, SPAN)
    resume_hit = (position == resume_start).reshape(span_count, SPAN)
    head_rate = cut(decay_rate, 0, h_off, head_local).reshape(group_local, per_local)
    skip_gain = cut(d_skip, 0, h_off, head_local).reshape(group_local, per_local)
    carry_init = cut(carry_state, 0, h_off, head_local).reshape(
        group_local, per_local, head_width, state_width
    )
    direct, state_gain, update, span_decay = span_pieces(
        x_conv,
        b_conv,
        c_conv,
        dt_full,
        head_rate,
        seg_blocks,
        starting,
        resumed,
        resume_hit,
        carry_init,
        skip_gain,
    )

    def fold_span(carried, pieces):
        return (
            (pieces[1][..., None, None] * carried[0] + pieces[0], pieces[1] * carried[1]),
            carried,
        )

    empty_state = jnp.zeros((group_local, per_local, head_width, state_width), jnp.float32)
    unit_decay = jnp.ones((group_local, per_local), jnp.float32)
    (local_state, local_decay), (prefix_state, prefix_decay) = lax.scan(
        fold_span, (empty_state, unit_decay), (update, span_decay)
    )
    hop_count = max(1, lax.axis_size("pair") // 4)
    incoming = jnp.zeros_like(local_state)
    reach = jnp.ones_like(local_decay)
    for steps in range(1, hop_count + 1):
        state_back, decay_back = from_behind((local_state, local_decay), "pair", steps)
        incoming = incoming + reach[..., None, None] * state_back
        reach = reach * decay_back
    entering = prefix_decay[..., None, None] * incoming[None] + prefix_state
    from_state = product_of("cghpn,cqgn->cqghp", entering, c_conv)
    ssd_out = (direct + state_gain[..., None] * from_state).reshape(row_count, inner_local)
    gate_act = jax.nn.silu(proj_z.astype(jnp.float32))
    gated = (ssd_out * gate_act).reshape(row_count, group_local, inner_local // group_local)
    squares = jnp.sum(gated * gated, axis=-1, keepdims=True)
    if head_local < per_group:
        squares = lax.psum(squares, "half")
    factor = lax.rsqrt(squares / (per_group * head_width) + EPS)
    normed_y = (
        (gated * factor).reshape(row_count, inner_local) * cut(gated_gain, 0, x_off, inner_local)[None, :]
    ).astype(jnp.bfloat16)
    piece = own_rows // core_count
    by_owner = normed_y.reshape(2, core_count, piece, inner_local)
    results = []
    for columns in (out_first, out_second):
        total = None
        for shift in list(range(1, core_count)) + [0]:
            rows = lax.dynamic_index_in_dim(by_owner, (core + shift) % core_count, 1, keepdims=False)
            part = jnp.einsum("hrc,cd->hrd", rows, columns, preferred_element_type=jnp.float32)
            if shift:
                part = lax.ppermute(
                    part, "fsdp", [(j, (j + shift) % core_count) for j in range(core_count)]
                )
            total = part if total is None else total + part
        mine = lax.dynamic_index_in_dim(total, half, 0, keepdims=False)
        theirs = lax.dynamic_index_in_dim(total, 1 - half, 0, keepdims=False)
        theirs = swap_half(theirs.astype(jnp.bfloat16))
        results.append((mine + theirs.astype(jnp.float32)).astype(jnp.bfloat16))
    pair_count = lax.axis_size("pair")
    joined = jnp.stack([r.reshape(piece, pair_count, block) for r in results], axis=2)
    return joined.reshape(piece, 2 * pair_count * block)


def solution(mesh):
    seq_count = mesh.shape["seq"]
    devices = mesh.devices.reshape(seq_count // 2, 2, mesh.shape["fsdp"])
    paired = jax.sharding.Mesh(devices, ("pair", "half", "fsdp"))
    seq = ("pair", "half")
    return jax.shard_map(
        body,
        mesh=paired,
        in_specs=(
            P(seq, None),
            P(),
            P(seq, None, "fsdp"),
            P(seq, None, "fsdp"),
            P(seq, "fsdp"),
            P(None, "fsdp"),
            P(None, None, "fsdp"),
            P("fsdp"),
            P("fsdp"),
            P("fsdp"),
            P("fsdp"),
            P("fsdp", seq),
            P(),
            P(),
            P(),
            P("fsdp", None, None),
            P(None, "fsdp"),
            P(None, None, "fsdp"),
        ),
        out_specs=P(("pair", "half", "fsdp"), None),
        check_vma=False,
    )
```

```python
import jax
import jax.numpy as jnp
from jax import lax
from jax.sharding import PartitionSpec as P

SPAN = 256


EPS = 1e-05


def from_behind(value, axis, steps):
    count = lax.axis_size(axis)
    leading, last = (max(0, -steps), min(count, count - steps))
    return lax.ppermute(value, axis, [(source, source + steps) for source in range(leading, last)])


def product_of(form, left, right):
    if left.dtype == jnp.bfloat16 and right.dtype == jnp.bfloat16:
        return jnp.einsum(form, left, right, preferred_element_type=jnp.float32)
    return jnp.einsum(form, left, right.astype(jnp.float32), precision=lax.Precision.HIGHEST)


def norm_rows(values, row_gain):
    widened = values.astype(jnp.float32)
    factor = lax.rsqrt(jnp.mean(widened * widened, axis=-1, keepdims=True) + EPS)
    return (widened * factor * row_gain[None, :]).astype(jnp.bfloat16)


def layout(prompt_lengths, pack_order, resume_prompt, position):
    prompt_count = pack_order.shape[0]
    slot_ids = jnp.arange(prompt_count, dtype=jnp.int32)
    ordered = jnp.sum(
        jnp.where(pack_order[:, None] == slot_ids[None, :], prompt_lengths[None, :], 0), axis=1
    )
    seg_starts = jnp.cumsum(ordered, dtype=jnp.int32) - ordered
    reached = position[:, None] >= seg_starts[None, :]
    segment = jnp.sum(reached.astype(jnp.int32), axis=1) - 1
    seg_start = jnp.max(jnp.where(reached, seg_starts[None, :], 0), axis=1)
    resume_slot = jnp.sum(jnp.where(pack_order == resume_prompt[0], slot_ids, 0))
    resume_start = jnp.sum(jnp.where(slot_ids == resume_slot, seg_starts, 0))
    return (segment, seg_start, resume_slot, resume_start)


def conv_rows(
    source, prior_rows, weight, carry_rows, segment, seg_start, position, resume_slot, resume_start
):
    row_count = source.shape[0]
    edge_rows = prior_rows.shape[0]
    extended = jnp.concatenate([prior_rows, source], axis=0)
    resumed = (segment == resume_slot)[:, None]
    summed = jnp.zeros(source.shape, jnp.float32)
    for back_by in range(edge_rows + 1):
        shifted = extended[edge_rows - back_by : edge_rows - back_by + row_count].astype(
            jnp.float32
        )
        inside = (position - back_by >= seg_start)[:, None]
        carry_index = position - back_by - resume_start + edge_rows
        from_carry = jnp.zeros(source.shape, jnp.float32)
        for slot_id in range(edge_rows):
            from_carry = from_carry + jnp.where(
                (carry_index == slot_id)[:, None],
                carry_rows[slot_id].astype(jnp.float32)[None, :],
                0.0,
            )
        chosen = jnp.where(inside, shifted, jnp.where(resumed, from_carry, 0.0))
        summed = summed + chosen * weight[edge_rows - back_by].astype(jnp.float32)[None, :]
    return jax.nn.silu(summed).astype(jnp.bfloat16)


def span_pieces(
    x_blocks,
    b_blocks,
    c_blocks,
    dt_blocks,
    head_rate,
    segment,
    starting,
    resumed,
    resume_hit,
    carry_init,
    skip_gain,
):
    block_len = segment.shape[1]
    log_decay = -dt_blocks * head_rate[None, None]
    cumulative = jnp.cumsum(log_decay, axis=1)
    indices = jnp.arange(block_len, dtype=jnp.int32)
    causal = (indices[:, None] >= indices[None, :])[None] & (
        segment[:, :, None] == segment[:, None, :]
    )
    cum_rows = jnp.moveaxis(cumulative, 1, -1)
    log_gap = cum_rows[..., :, None] - cum_rows[..., None, :]
    within = causal[:, None, None]
    decays = jnp.where(within, jnp.exp(jnp.where(within, log_gap, 0.0)), 0.0)
    scores = product_of("cqgn,csgn->cgqs", c_blocks, b_blocks)
    dt_source = jnp.moveaxis(dt_blocks, 1, -1)[..., None, :]
    weights = (scores[:, :, None] * decays * dt_source).astype(jnp.bfloat16)
    direct = product_of("cghqs,csghp->cqghp", weights, x_blocks)
    cum_end = cumulative[:, -1]
    tail_mask = (segment == segment[:, -1:])[:, :, None, None]
    to_end = (
        jnp.where(tail_mask, jnp.exp(jnp.where(tail_mask, cum_end[:, None] - cumulative, 0.0)), 0.0)
        * dt_blocks
    )
    scaled = (x_blocks.astype(jnp.float32) * to_end[..., None]).astype(jnp.bfloat16)
    update = product_of("cqghp,cqgn->cghpn", scaled, b_blocks)
    opened = jnp.any(starting, axis=1)
    span_decay = jnp.where(opened[:, None, None], 0.0, jnp.exp(cum_end))
    hit_mask = resume_hit[:, :, None, None]
    has_hit = jnp.any(resume_hit, axis=1)[:, None, None, None]
    cum_hit = jnp.sum(jnp.where(hit_mask, cumulative - log_decay, 0.0), axis=1, keepdims=True)
    carry_mask = resumed[:, :, None, None] & has_hit
    carry_gain = jnp.where(
        carry_mask, jnp.exp(jnp.where(carry_mask, cumulative - cum_hit, 0.0)), 0.0
    )
    end_gain = carry_gain[:, -1]
    update = update + end_gain[..., None, None] * carry_init[None]
    direct = direct + carry_gain[..., None] * product_of("ghpn,cqgn->cqghp", carry_init, c_blocks)
    direct = direct + skip_gain[None, None, :, :, None] * x_blocks.astype(jnp.float32)
    unopened = jnp.cumsum(starting.astype(jnp.int32), axis=1, dtype=jnp.int32) == 0
    state_gain = jnp.where(unopened[:, :, None, None], jnp.exp(cumulative), 0.0)
    return (direct, state_gain, update, span_decay)


def swap_half(value):
    count = lax.axis_size("half")
    return lax.ppermute(value, "half", [(k, count - 1 - k) for k in range(count)])


def ordered_pair(own, other, half, axis):
    return jnp.where(
        half == 0,
        jnp.concatenate([own, other], axis=axis),
        jnp.concatenate([other, own], axis=axis),
    )


def body(
    tokens,
    norm_gain,
    w_zx,
    w_bc,
    w_dt,
    conv_x,
    conv_bc,
    dt_bias,
    decay_rate,
    d_skip,
    gated_gain,
    w_out,
    prompt_lengths,
    pack_order,
    resume_prompt,
    carry_state,
    carry_conv_x,
    carry_conv_bc,
):
    own_rows = tokens.shape[0]
    row_count = 2 * own_rows
    edge_rows = conv_x.shape[0] - 1
    head_width = carry_state.shape[1]
    state_width = carry_state.shape[2]
    head_fsdp = w_dt.shape[1]
    group_fsdp = w_bc.shape[2] // state_width
    per_group = head_fsdp // group_fsdp
    head_local = head_fsdp // 2
    group_local = max(1, head_local // per_group)
    per_local = min(per_group, head_local)
    inner_local = head_local * head_width
    state_cols = group_local * state_width
    span_count = row_count // SPAN
    half = lax.axis_index("half")
    core = lax.axis_index("fsdp")
    core_count = lax.axis_size("fsdp")
    x_off = half * inner_local
    bc_off = (half * head_local) // per_group * state_width
    h_off = half * head_local

    def cut(value, axis, offset, width):
        return lax.dynamic_slice_in_dim(value, offset, width, axis)

    normed_own = norm_rows(tokens, norm_gain)
    share = own_rows // core_count
    fetched = swap_half(cut(normed_own, 0, core * share, share))
    arrived = [fetched] + [
        lax.ppermute(fetched, "fsdp", [(j, (j + shift) % core_count) for j in range(core_count)])
        for shift in range(1, core_count)
    ]
    arrived = jnp.stack(arrived)
    owners = (core - jnp.arange(core_count, dtype=jnp.int32)) % core_count
    normed_other = jnp.take(arrived, owners, axis=0).reshape(own_rows, tokens.shape[1])
    normed = ordered_pair(normed_own, normed_other, half, 0)

    def first_cols(offset_x, offset_bc, offset_h):
        return jnp.concatenate(
            [
                cut(w_zx[:, 1], 1, offset_x, inner_local),
                cut(w_bc[:, 0], 1, offset_bc, state_cols),
                cut(w_bc[:, 1], 1, offset_bc, state_cols),
                cut(w_dt, 1, offset_h, head_local),
            ],
            axis=1,
        )

    other = 1 - half
    first_mine = first_cols(x_off, bc_off, h_off)
    first_theirs = swap_half(
        first_cols(other * inner_local, (other * head_local) // per_group * state_width, other * head_local)
    )
    first_local = ordered_pair(first_mine, first_theirs, half, 0)
    first_full = lax.all_gather(first_local, "pair", axis=0, tiled=True)
    proj_first = jnp.dot(normed, first_full, preferred_element_type=jnp.float32).astype(
        jnp.bfloat16
    )
    conv_width = inner_local + 2 * state_cols
    conv_in = proj_first[:, :conv_width]
    proj_dt = proj_first[:, conv_width:]
    w_z_all, w_out_all, _ = lax.optimization_barrier((w_zx[:, 0], w_out, proj_first))
    z_local = ordered_pair(
        cut(w_z_all, 1, x_off, inner_local),
        swap_half(cut(w_z_all, 1, other * inner_local, inner_local)),
        half,
        0,
    )
    out_local = ordered_pair(
        cut(w_out_all, 0, x_off, inner_local),
        swap_half(cut(w_out_all, 0, other * inner_local, inner_local)),
        half,
        1,
    )
    z_full = lax.all_gather(z_local, "pair", axis=0, tiled=True)
    block = out_local.shape[1] // 2
    out_first = lax.all_gather(out_local[:, :block], "pair", axis=1, tiled=True)
    proj_z = jnp.dot(normed, z_full, preferred_element_type=jnp.float32).astype(jnp.bfloat16)

    position = lax.axis_index("pair") * row_count + jnp.arange(row_count, dtype=jnp.int32)
    segment, seg_start, resume_slot, resume_start = layout(
        prompt_lengths, pack_order, resume_prompt, position
    )
    prior_rows = from_behind(conv_in[row_count - edge_rows :], "pair", 1)
    weight = jnp.concatenate(
        [
            cut(conv_x, 1, x_off, inner_local),
            cut(conv_bc[:, 0], 1, bc_off, state_cols),
            cut(conv_bc[:, 1], 1, bc_off, state_cols),
        ],
        axis=1,
    )
    carry_rows = jnp.concatenate(
        [
            cut(carry_conv_x, 1, x_off, inner_local),
            cut(carry_conv_bc[:, 0], 1, bc_off, state_cols),
            cut(carry_conv_bc[:, 1], 1, bc_off, state_cols),
        ],
        axis=1,
    )
    conv_out = conv_rows(
        conv_in,
        prior_rows,
        weight,
        carry_rows,
        segment,
        seg_start,
        position,
        resume_slot,
        resume_start,
    )
    x_conv = conv_out[:, :inner_local].reshape(span_count, SPAN, group_local, per_local, head_width)
    b_conv = conv_out[:, inner_local : inner_local + state_cols].reshape(
        span_count, SPAN, group_local, state_width
    )
    c_conv = conv_out[:, inner_local + state_cols :].reshape(
        span_count, SPAN, group_local, state_width
    )
    dt_full = jax.nn.softplus(
        proj_dt.astype(jnp.float32) + cut(dt_bias, 0, h_off, head_local)[None, :]
    ).reshape(span_count, SPAN, group_local, per_local)
    seg_blocks = segment.reshape(span_count, SPAN)
    starting = (position == seg_start).reshape(span_count, SPAN)
    resumed = (segment == resume_slot).reshape(span_count, SPAN)
    resume_hit = (position == resume_start).reshape(span_count, SPAN)
    head_rate = cut(decay_rate, 0, h_off, head_local).reshape(group_local, per_local)
    skip_gain = cut(d_skip, 0, h_off, head_local).reshape(group_local, per_local)
    carry_init = cut(carry_state, 0, h_off, head_local).reshape(
        group_local, per_local, head_width, state_width
    )
    direct, state_gain, update, span_decay = span_pieces(
        x_conv,
        b_conv,
        c_conv,
        dt_full,
        head_rate,
        seg_blocks,
        starting,
        resumed,
        resume_hit,
        carry_init,
        skip_gain,
    )

    def fold_span(carried, pieces):
        return (
            (pieces[1][..., None, None] * carried[0] + pieces[0], pieces[1] * carried[1]),
            carried,
        )

    empty_state = jnp.zeros((group_local, per_local, head_width, state_width), jnp.float32)
    unit_decay = jnp.ones((group_local, per_local), jnp.float32)
    (local_state, local_decay), (prefix_state, prefix_decay) = lax.scan(
        fold_span, (empty_state, unit_decay), (update, span_decay)
    )
    hop_count = max(1, lax.axis_size("pair") // 4)
    incoming = jnp.zeros_like(local_state)
    reach = jnp.ones_like(local_decay)
    for steps in range(1, hop_count + 1):
        state_back, decay_back = from_behind((local_state, local_decay), "pair", steps)
        incoming = incoming + reach[..., None, None] * state_back
        reach = reach * decay_back
    entering = prefix_decay[..., None, None] * incoming[None] + prefix_state
    from_state = product_of("cghpn,cqgn->cqghp", entering, c_conv)
    ssd_out = (direct + state_gain[..., None] * from_state).reshape(row_count, inner_local)
    gate_act = jax.nn.silu(proj_z.astype(jnp.float32))
    gated = (ssd_out * gate_act).reshape(row_count, group_local, inner_local // group_local)
    squares = jnp.sum(gated * gated, axis=-1, keepdims=True)
    if head_local < per_group:
        squares = lax.psum(squares, "half")
    factor = lax.rsqrt(squares / (per_group * head_width) + EPS)
    normed_y = (
        (gated * factor).reshape(row_count, inner_local) * cut(gated_gain, 0, x_off, inner_local)[None, :]
    ).astype(jnp.bfloat16)
    piece = own_rows // core_count
    by_owner = normed_y.reshape(2, core_count, piece, inner_local)
    results = []
    second_local = out_local[:, block:]
    for index in range(2):
        columns = out_first
        if index:
            columns, results[0] = lax.optimization_barrier((out_second, results[0]))
        total = None
        for shift in list(range(1, core_count)) + [0]:
            rows = lax.dynamic_index_in_dim(by_owner, (core + shift) % core_count, 1, keepdims=False)
            part = jnp.einsum("hrc,cd->hrd", rows, columns, preferred_element_type=jnp.float32)
            if index == 0 and total is None:
                second_local, part = lax.optimization_barrier((second_local, part))
                out_second = lax.all_gather(second_local, "pair", axis=1, tiled=True)
            if shift:
                part = lax.ppermute(
                    part, "fsdp", [(j, (j + shift) % core_count) for j in range(core_count)]
                )
            total = part if total is None else total + part
        mine = lax.dynamic_index_in_dim(total, half, 0, keepdims=False)
        theirs = lax.dynamic_index_in_dim(total, 1 - half, 0, keepdims=False)
        theirs = swap_half(theirs.astype(jnp.bfloat16))
        results.append((mine + theirs.astype(jnp.float32)).astype(jnp.bfloat16))
    pair_count = lax.axis_size("pair")
    joined = jnp.stack([r.reshape(piece, pair_count, block) for r in results], axis=2)
    return joined.reshape(piece, 2 * pair_count * block)


def solution(mesh):
    seq_count = mesh.shape["seq"]
    devices = mesh.devices.reshape(seq_count // 2, 2, mesh.shape["fsdp"])
    paired = jax.sharding.Mesh(devices, ("pair", "half", "fsdp"))
    seq = ("pair", "half")
    return jax.shard_map(
        body,
        mesh=paired,
        in_specs=(
            P(seq, None),
            P(),
            P(seq, None, "fsdp"),
            P(seq, None, "fsdp"),
            P(seq, "fsdp"),
            P(None, "fsdp"),
            P(None, None, "fsdp"),
            P("fsdp"),
            P("fsdp"),
            P("fsdp"),
            P("fsdp"),
            P("fsdp", seq),
            P(),
            P(),
            P(),
            P("fsdp", None, None),
            P(None, "fsdp"),
            P(None, None, "fsdp"),
        ),
        out_specs=P(("pair", "half", "fsdp"), None),
        check_vma=False,
    )
```

```python
import jax
import jax.numpy as jnp
from jax import lax
from jax.sharding import PartitionSpec as P

SPAN = 256


EPS = 1e-05


def from_behind(value, axis, steps):
    count = lax.axis_size(axis)
    leading, last = (max(0, -steps), min(count, count - steps))
    return lax.ppermute(value, axis, [(source, source + steps) for source in range(leading, last)])


def product_of(form, left, right):
    if left.dtype == jnp.bfloat16 and right.dtype == jnp.bfloat16:
        return jnp.einsum(form, left, right, preferred_element_type=jnp.float32)
    return jnp.einsum(form, left, right.astype(jnp.float32), precision=lax.Precision.HIGHEST)


def norm_rows(values, row_gain):
    widened = values.astype(jnp.float32)
    factor = lax.rsqrt(jnp.mean(widened * widened, axis=-1, keepdims=True) + EPS)
    return (widened * factor * row_gain[None, :]).astype(jnp.bfloat16)


def layout(prompt_lengths, pack_order, resume_prompt, position):
    prompt_count = pack_order.shape[0]
    slot_ids = jnp.arange(prompt_count, dtype=jnp.int32)
    ordered = jnp.sum(
        jnp.where(pack_order[:, None] == slot_ids[None, :], prompt_lengths[None, :], 0), axis=1
    )
    seg_starts = jnp.cumsum(ordered, dtype=jnp.int32) - ordered
    reached = position[:, None] >= seg_starts[None, :]
    segment = jnp.sum(reached.astype(jnp.int32), axis=1) - 1
    seg_start = jnp.max(jnp.where(reached, seg_starts[None, :], 0), axis=1)
    resume_slot = jnp.sum(jnp.where(pack_order == resume_prompt[0], slot_ids, 0))
    resume_start = jnp.sum(jnp.where(slot_ids == resume_slot, seg_starts, 0))
    return (segment, seg_start, resume_slot, resume_start)


def conv_rows(
    source, prior_rows, weight, carry_rows, segment, seg_start, position, resume_slot, resume_start
):
    row_count = source.shape[0]
    edge_rows = prior_rows.shape[0]
    extended = jnp.concatenate([prior_rows, source], axis=0)
    resumed = (segment == resume_slot)[:, None]
    summed = jnp.zeros(source.shape, jnp.float32)
    for back_by in range(edge_rows + 1):
        shifted = extended[edge_rows - back_by : edge_rows - back_by + row_count].astype(
            jnp.float32
        )
        inside = (position - back_by >= seg_start)[:, None]
        carry_index = position - back_by - resume_start + edge_rows
        from_carry = jnp.zeros(source.shape, jnp.float32)
        for slot_id in range(edge_rows):
            from_carry = from_carry + jnp.where(
                (carry_index == slot_id)[:, None],
                carry_rows[slot_id].astype(jnp.float32)[None, :],
                0.0,
            )
        chosen = jnp.where(inside, shifted, jnp.where(resumed, from_carry, 0.0))
        summed = summed + chosen * weight[edge_rows - back_by].astype(jnp.float32)[None, :]
    return jax.nn.silu(summed).astype(jnp.bfloat16)


def span_pieces(
    x_blocks,
    b_blocks,
    c_blocks,
    dt_blocks,
    head_rate,
    segment,
    starting,
    resumed,
    resume_hit,
    carry_init,
    skip_gain,
):
    block_len = segment.shape[1]
    log_decay = -dt_blocks * head_rate[None, None]
    cumulative = jnp.cumsum(log_decay, axis=1)
    indices = jnp.arange(block_len, dtype=jnp.int32)
    causal = (indices[:, None] >= indices[None, :])[None] & (
        segment[:, :, None] == segment[:, None, :]
    )
    cum_rows = jnp.moveaxis(cumulative, 1, -1)
    log_gap = cum_rows[..., :, None] - cum_rows[..., None, :]
    within = causal[:, None, None]
    decays = jnp.where(within, jnp.exp(jnp.where(within, log_gap, 0.0)), 0.0)
    scores = product_of("cqgn,csgn->cgqs", c_blocks, b_blocks)
    dt_source = jnp.moveaxis(dt_blocks, 1, -1)[..., None, :]
    weights = (scores[:, :, None] * decays * dt_source).astype(jnp.bfloat16)
    direct = product_of("cghqs,csghp->cqghp", weights, x_blocks)
    cum_end = cumulative[:, -1]
    tail_mask = (segment == segment[:, -1:])[:, :, None, None]
    to_end = (
        jnp.where(tail_mask, jnp.exp(jnp.where(tail_mask, cum_end[:, None] - cumulative, 0.0)), 0.0)
        * dt_blocks
    )
    scaled = (x_blocks.astype(jnp.float32) * to_end[..., None]).astype(jnp.bfloat16)
    update = product_of("cqghp,cqgn->cghpn", scaled, b_blocks)
    opened = jnp.any(starting, axis=1)
    span_decay = jnp.where(opened[:, None, None], 0.0, jnp.exp(cum_end))
    hit_mask = resume_hit[:, :, None, None]
    has_hit = jnp.any(resume_hit, axis=1)[:, None, None, None]
    cum_hit = jnp.sum(jnp.where(hit_mask, cumulative - log_decay, 0.0), axis=1, keepdims=True)
    carry_mask = resumed[:, :, None, None] & has_hit
    carry_gain = jnp.where(
        carry_mask, jnp.exp(jnp.where(carry_mask, cumulative - cum_hit, 0.0)), 0.0
    )
    end_gain = carry_gain[:, -1]
    update = update + end_gain[..., None, None] * carry_init[None]
    direct = direct + carry_gain[..., None] * product_of("ghpn,cqgn->cqghp", carry_init, c_blocks)
    direct = direct + skip_gain[None, None, :, :, None] * x_blocks.astype(jnp.float32)
    unopened = jnp.cumsum(starting.astype(jnp.int32), axis=1, dtype=jnp.int32) == 0
    state_gain = jnp.where(unopened[:, :, None, None], jnp.exp(cumulative), 0.0)
    return (direct, state_gain, update, span_decay)


def swap_half(value):
    count = lax.axis_size("half")
    return lax.ppermute(value, "half", [(k, count - 1 - k) for k in range(count)])


def ordered_pair(own, other, half, axis):
    return jnp.where(
        half == 0,
        jnp.concatenate([own, other], axis=axis),
        jnp.concatenate([other, own], axis=axis),
    )


def body(
    tokens,
    norm_gain,
    w_zx,
    w_bc,
    w_dt,
    conv_x,
    conv_bc,
    dt_bias,
    decay_rate,
    d_skip,
    gated_gain,
    w_out,
    prompt_lengths,
    pack_order,
    resume_prompt,
    carry_state,
    carry_conv_x,
    carry_conv_bc,
):
    own_rows = tokens.shape[0]
    row_count = 2 * own_rows
    edge_rows = conv_x.shape[0] - 1
    head_width = carry_state.shape[1]
    state_width = carry_state.shape[2]
    head_fsdp = w_dt.shape[1]
    group_fsdp = w_bc.shape[2] // state_width
    per_group = head_fsdp // group_fsdp
    head_local = head_fsdp // 2
    group_local = max(1, head_local // per_group)
    per_local = min(per_group, head_local)
    inner_local = head_local * head_width
    state_cols = group_local * state_width
    span_count = row_count // SPAN
    half = lax.axis_index("half")
    core = lax.axis_index("fsdp")
    core_count = lax.axis_size("fsdp")
    x_off = half * inner_local
    bc_off = (half * head_local) // per_group * state_width
    h_off = half * head_local

    def cut(value, axis, offset, width):
        return lax.dynamic_slice_in_dim(value, offset, width, axis)

    normed_own = norm_rows(tokens, norm_gain)
    share = own_rows // core_count
    fetched = swap_half(cut(normed_own, 0, core * share, share))
    arrived = [fetched] + [
        lax.ppermute(fetched, "fsdp", [(j, (j + shift) % core_count) for j in range(core_count)])
        for shift in range(1, core_count)
    ]
    arrived = jnp.stack(arrived)
    owners = (core - jnp.arange(core_count, dtype=jnp.int32)) % core_count
    normed_other = jnp.take(arrived, owners, axis=0).reshape(own_rows, tokens.shape[1])
    normed = ordered_pair(normed_own, normed_other, half, 0)

    def first_cols(offset_x, offset_bc, offset_h):
        return jnp.concatenate(
            [
                cut(w_zx[:, 1], 1, offset_x, inner_local),
                cut(w_bc[:, 0], 1, offset_bc, state_cols),
                cut(w_bc[:, 1], 1, offset_bc, state_cols),
                cut(w_dt, 1, offset_h, head_local),
            ],
            axis=1,
        )

    other = 1 - half
    first_mine = first_cols(x_off, bc_off, h_off)
    first_theirs = swap_half(
        first_cols(other * inner_local, (other * head_local) // per_group * state_width, other * head_local)
    )
    first_local = ordered_pair(first_mine, first_theirs, half, 0)
    first_full = lax.all_gather(first_local, "pair", axis=0, tiled=True)
    proj_first = jnp.dot(normed, first_full, preferred_element_type=jnp.float32).astype(
        jnp.bfloat16
    )
    conv_width = inner_local + 2 * state_cols
    conv_in = proj_first[:, :conv_width]
    proj_dt = proj_first[:, conv_width:]
    w_z_all, w_out_all, _ = lax.optimization_barrier((w_zx[:, 0], w_out, proj_first))
    z_local = ordered_pair(
        cut(w_z_all, 1, x_off, inner_local),
        swap_half(cut(w_z_all, 1, other * inner_local, inner_local)),
        half,
        0,
    )
    out_local = ordered_pair(
        cut(w_out_all, 0, x_off, inner_local),
        swap_half(cut(w_out_all, 0, other * inner_local, inner_local)),
        half,
        1,
    )
    z_full = lax.all_gather(z_local, "pair", axis=0, tiled=True)
    out_full = lax.all_gather(out_local, "pair", axis=1, tiled=True)
    proj_z = jnp.dot(normed, z_full, preferred_element_type=jnp.float32).astype(jnp.bfloat16)

    position = lax.axis_index("pair") * row_count + jnp.arange(row_count, dtype=jnp.int32)
    segment, seg_start, resume_slot, resume_start = layout(
        prompt_lengths, pack_order, resume_prompt, position
    )
    prior_rows = from_behind(conv_in[row_count - edge_rows :], "pair", 1)
    weight = jnp.concatenate(
        [
            cut(conv_x, 1, x_off, inner_local),
            cut(conv_bc[:, 0], 1, bc_off, state_cols),
            cut(conv_bc[:, 1], 1, bc_off, state_cols),
        ],
        axis=1,
    )
    carry_rows = jnp.concatenate(
        [
            cut(carry_conv_x, 1, x_off, inner_local),
            cut(carry_conv_bc[:, 0], 1, bc_off, state_cols),
            cut(carry_conv_bc[:, 1], 1, bc_off, state_cols),
        ],
        axis=1,
    )
    conv_out = conv_rows(
        conv_in,
        prior_rows,
        weight,
        carry_rows,
        segment,
        seg_start,
        position,
        resume_slot,
        resume_start,
    )
    x_conv = conv_out[:, :inner_local].reshape(span_count, SPAN, group_local, per_local, head_width)
    b_conv = conv_out[:, inner_local : inner_local + state_cols].reshape(
        span_count, SPAN, group_local, state_width
    )
    c_conv = conv_out[:, inner_local + state_cols :].reshape(
        span_count, SPAN, group_local, state_width
    )
    dt_full = jax.nn.softplus(
        proj_dt.astype(jnp.float32) + cut(dt_bias, 0, h_off, head_local)[None, :]
    ).reshape(span_count, SPAN, group_local, per_local)
    seg_blocks = segment.reshape(span_count, SPAN)
    starting = (position == seg_start).reshape(span_count, SPAN)
    resumed = (segment == resume_slot).reshape(span_count, SPAN)
    resume_hit = (position == resume_start).reshape(span_count, SPAN)
    head_rate = cut(decay_rate, 0, h_off, head_local).reshape(group_local, per_local)
    skip_gain = cut(d_skip, 0, h_off, head_local).reshape(group_local, per_local)
    carry_init = cut(carry_state, 0, h_off, head_local).reshape(
        group_local, per_local, head_width, state_width
    )
    direct, state_gain, update, span_decay = span_pieces(
        x_conv,
        b_conv,
        c_conv,
        dt_full,
        head_rate,
        seg_blocks,
        starting,
        resumed,
        resume_hit,
        carry_init,
        skip_gain,
    )

    def fold_span(carried, pieces):
        return (
            (pieces[1][..., None, None] * carried[0] + pieces[0], pieces[1] * carried[1]),
            carried,
        )

    empty_state = jnp.zeros((group_local, per_local, head_width, state_width), jnp.float32)
    unit_decay = jnp.ones((group_local, per_local), jnp.float32)
    (local_state, local_decay), (prefix_state, prefix_decay) = lax.scan(
        fold_span, (empty_state, unit_decay), (update, span_decay)
    )
    hop_count = max(1, lax.axis_size("pair") // 4)
    incoming = jnp.zeros_like(local_state)
    reach = jnp.ones_like(local_decay)
    for steps in range(1, hop_count + 1):
        state_back, decay_back = from_behind((local_state, local_decay), "pair", steps)
        incoming = incoming + reach[..., None, None] * state_back
        reach = reach * decay_back
    entering = prefix_decay[..., None, None] * incoming[None] + prefix_state
    from_state = product_of("cghpn,cqgn->cqghp", entering, c_conv)
    ssd_out = (direct + state_gain[..., None] * from_state).reshape(row_count, inner_local)
    gate_act = jax.nn.silu(proj_z.astype(jnp.float32))
    gated = (ssd_out * gate_act).reshape(row_count, group_local, inner_local // group_local)
    squares = jnp.sum(gated * gated, axis=-1, keepdims=True)
    if head_local < per_group:
        squares = lax.psum(squares, "half")
    factor = lax.rsqrt(squares / (per_group * head_width) + EPS)
    normed_y = (
        (gated * factor).reshape(row_count, inner_local) * cut(gated_gain, 0, x_off, inner_local)[None, :]
    ).astype(jnp.bfloat16)
    piece = own_rows // core_count
    by_owner = normed_y.reshape(2, core_count, piece, inner_local)
    chunk_count = 2
    chunk = out_full.shape[1] // chunk_count
    results = []
    for index in range(chunk_count):
        columns = out_full[:, index * chunk : (index + 1) * chunk]
        total = None
        for shift in list(range(1, core_count)) + [0]:
            rows = lax.dynamic_index_in_dim(by_owner, (core + shift) % core_count, 1, keepdims=False)
            part = jnp.einsum("hrc,cd->hrd", rows, columns, preferred_element_type=jnp.float32)
            if shift:
                part = lax.ppermute(
                    part.astype(jnp.bfloat16),
                    "fsdp",
                    [(j, (j + shift) % core_count) for j in range(core_count)],
                ).astype(jnp.float32)
            total = part if total is None else total + part
        mine = lax.dynamic_index_in_dim(total, half, 0, keepdims=False)
        theirs = lax.dynamic_index_in_dim(total, 1 - half, 0, keepdims=False)
        theirs = swap_half(theirs.astype(jnp.bfloat16))
        results.append((mine + theirs.astype(jnp.float32)).astype(jnp.bfloat16))
    return jnp.concatenate(results, axis=1)


def solution(mesh):
    seq_count = mesh.shape["seq"]
    devices = mesh.devices.reshape(seq_count // 2, 2, mesh.shape["fsdp"])
    paired = jax.sharding.Mesh(devices, ("pair", "half", "fsdp"))
    seq = ("pair", "half")
    return jax.shard_map(
        body,
        mesh=paired,
        in_specs=(
            P(seq, None),
            P(),
            P(seq, None, "fsdp"),
            P(seq, None, "fsdp"),
            P(seq, "fsdp"),
            P(None, "fsdp"),
            P(None, None, "fsdp"),
            P("fsdp"),
            P("fsdp"),
            P("fsdp"),
            P("fsdp"),
            P("fsdp", seq),
            P(),
            P(),
            P(),
            P("fsdp", None, None),
            P(None, "fsdp"),
            P(None, None, "fsdp"),
        ),
        out_specs=P(("pair", "half", "fsdp"), None),
        check_vma=False,
    )
```

```python
import jax
import jax.numpy as jnp
from jax import lax
from jax.sharding import PartitionSpec as P

SPAN = 256


EPS = 1e-05


def from_behind(value, axis, steps):
    count = lax.axis_size(axis)
    leading, last = (max(0, -steps), min(count, count - steps))
    return lax.ppermute(value, axis, [(source, source + steps) for source in range(leading, last)])


def product_of(form, left, right):
    if left.dtype == jnp.bfloat16 and right.dtype == jnp.bfloat16:
        return jnp.einsum(form, left, right, preferred_element_type=jnp.float32)
    return jnp.einsum(form, left, right.astype(jnp.float32), precision=lax.Precision.HIGHEST)


def norm_rows(values, row_gain):
    widened = values.astype(jnp.float32)
    factor = lax.rsqrt(jnp.mean(widened * widened, axis=-1, keepdims=True) + EPS)
    return (widened * factor * row_gain[None, :]).astype(jnp.bfloat16)


def layout(prompt_lengths, pack_order, resume_prompt, position):
    prompt_count = pack_order.shape[0]
    slot_ids = jnp.arange(prompt_count, dtype=jnp.int32)
    ordered = jnp.sum(
        jnp.where(pack_order[:, None] == slot_ids[None, :], prompt_lengths[None, :], 0), axis=1
    )
    seg_starts = jnp.cumsum(ordered, dtype=jnp.int32) - ordered
    reached = position[:, None] >= seg_starts[None, :]
    segment = jnp.sum(reached.astype(jnp.int32), axis=1) - 1
    seg_start = jnp.max(jnp.where(reached, seg_starts[None, :], 0), axis=1)
    resume_slot = jnp.sum(jnp.where(pack_order == resume_prompt[0], slot_ids, 0))
    resume_start = jnp.sum(jnp.where(slot_ids == resume_slot, seg_starts, 0))
    return (segment, seg_start, resume_slot, resume_start)


def conv_rows(
    source, prior_rows, weight, carry_rows, segment, seg_start, position, resume_slot, resume_start
):
    row_count = source.shape[0]
    edge_rows = prior_rows.shape[0]
    extended = jnp.concatenate([prior_rows, source], axis=0)
    resumed = (segment == resume_slot)[:, None]
    summed = jnp.zeros(source.shape, jnp.float32)
    for back_by in range(edge_rows + 1):
        shifted = extended[edge_rows - back_by : edge_rows - back_by + row_count].astype(
            jnp.float32
        )
        inside = (position - back_by >= seg_start)[:, None]
        carry_index = position - back_by - resume_start + edge_rows
        from_carry = jnp.zeros(source.shape, jnp.float32)
        for slot_id in range(edge_rows):
            from_carry = from_carry + jnp.where(
                (carry_index == slot_id)[:, None],
                carry_rows[slot_id].astype(jnp.float32)[None, :],
                0.0,
            )
        chosen = jnp.where(inside, shifted, jnp.where(resumed, from_carry, 0.0))
        summed = summed + chosen * weight[edge_rows - back_by].astype(jnp.float32)[None, :]
    return jax.nn.silu(summed).astype(jnp.bfloat16)


def span_pieces(
    x_blocks,
    b_blocks,
    c_blocks,
    dt_blocks,
    head_rate,
    segment,
    starting,
    resumed,
    resume_hit,
    carry_init,
    skip_gain,
):
    block_len = segment.shape[1]
    log_decay = -dt_blocks * head_rate[None, None]
    cumulative = jnp.cumsum(log_decay, axis=1)
    indices = jnp.arange(block_len, dtype=jnp.int32)
    causal = (indices[:, None] >= indices[None, :])[None] & (
        segment[:, :, None] == segment[:, None, :]
    )
    cum_rows = jnp.moveaxis(cumulative, 1, -1)
    log_gap = cum_rows[..., :, None] - cum_rows[..., None, :]
    within = causal[:, None, None]
    decays = jnp.where(within, jnp.exp(jnp.where(within, log_gap, 0.0)), 0.0)
    scores = product_of("cqgn,csgn->cgqs", c_blocks, b_blocks)
    dt_source = jnp.moveaxis(dt_blocks, 1, -1)[..., None, :]
    weights = (scores[:, :, None] * decays * dt_source).astype(jnp.bfloat16)
    direct = product_of("cghqs,csghp->cqghp", weights, x_blocks)
    cum_end = cumulative[:, -1]
    tail_mask = (segment == segment[:, -1:])[:, :, None, None]
    to_end = (
        jnp.where(tail_mask, jnp.exp(jnp.where(tail_mask, cum_end[:, None] - cumulative, 0.0)), 0.0)
        * dt_blocks
    )
    scaled = (x_blocks.astype(jnp.float32) * to_end[..., None]).astype(jnp.bfloat16)
    update = product_of("cqghp,cqgn->cghpn", scaled, b_blocks)
    opened = jnp.any(starting, axis=1)
    span_decay = jnp.where(opened[:, None, None], 0.0, jnp.exp(cum_end))
    hit_mask = resume_hit[:, :, None, None]
    has_hit = jnp.any(resume_hit, axis=1)[:, None, None, None]
    cum_hit = jnp.sum(jnp.where(hit_mask, cumulative - log_decay, 0.0), axis=1, keepdims=True)
    carry_mask = resumed[:, :, None, None] & has_hit
    carry_gain = jnp.where(
        carry_mask, jnp.exp(jnp.where(carry_mask, cumulative - cum_hit, 0.0)), 0.0
    )
    end_gain = carry_gain[:, -1]
    update = update + end_gain[..., None, None] * carry_init[None]
    direct = direct + carry_gain[..., None] * product_of("ghpn,cqgn->cqghp", carry_init, c_blocks)
    direct = direct + skip_gain[None, None, :, :, None] * x_blocks.astype(jnp.float32)
    unopened = jnp.cumsum(starting.astype(jnp.int32), axis=1, dtype=jnp.int32) == 0
    state_gain = jnp.where(unopened[:, :, None, None], jnp.exp(cumulative), 0.0)
    return (direct, state_gain, update, span_decay)


def swap_half(value):
    count = lax.axis_size("half")
    return lax.ppermute(value, "half", [(k, count - 1 - k) for k in range(count)])


def ordered_pair(own, other, half, axis):
    return jnp.where(
        half == 0,
        jnp.concatenate([own, other], axis=axis),
        jnp.concatenate([other, own], axis=axis),
    )


def body(
    tokens,
    norm_gain,
    w_zx,
    w_bc,
    w_dt,
    conv_x,
    conv_bc,
    dt_bias,
    decay_rate,
    d_skip,
    gated_gain,
    w_out,
    prompt_lengths,
    pack_order,
    resume_prompt,
    carry_state,
    carry_conv_x,
    carry_conv_bc,
):
    own_rows = tokens.shape[0]
    row_count = 2 * own_rows
    edge_rows = conv_x.shape[0] - 1
    head_width = carry_state.shape[1]
    state_width = carry_state.shape[2]
    head_fsdp = w_dt.shape[1]
    group_fsdp = w_bc.shape[2] // state_width
    per_group = head_fsdp // group_fsdp
    head_local = head_fsdp // 2
    group_local = max(1, head_local // per_group)
    per_local = min(per_group, head_local)
    inner_local = head_local * head_width
    state_cols = group_local * state_width
    span_count = row_count // SPAN
    half = lax.axis_index("half")
    core = lax.axis_index("fsdp")
    core_count = lax.axis_size("fsdp")
    x_off = half * inner_local
    bc_off = (half * head_local) // per_group * state_width
    h_off = half * head_local

    def cut(value, axis, offset, width):
        return lax.dynamic_slice_in_dim(value, offset, width, axis)

    normed_own = norm_rows(tokens, norm_gain)
    share = own_rows // core_count
    fetched = swap_half(cut(normed_own, 0, core * share, share))
    arrived = [fetched] + [
        lax.ppermute(fetched, "fsdp", [(j, (j + shift) % core_count) for j in range(core_count)])
        for shift in range(1, core_count)
    ]
    arrived = jnp.stack(arrived)
    owners = (core - jnp.arange(core_count, dtype=jnp.int32)) % core_count
    normed_other = jnp.take(arrived, owners, axis=0).reshape(own_rows, tokens.shape[1])
    normed = ordered_pair(normed_own, normed_other, half, 0)

    def first_cols(offset_x, offset_bc, offset_h):
        return jnp.concatenate(
            [
                cut(w_zx[:, 1], 1, offset_x, inner_local),
                cut(w_bc[:, 0], 1, offset_bc, state_cols),
                cut(w_bc[:, 1], 1, offset_bc, state_cols),
                cut(w_dt, 1, offset_h, head_local),
            ],
            axis=1,
        )

    other = 1 - half
    first_mine = first_cols(x_off, bc_off, h_off)
    first_theirs = swap_half(
        first_cols(other * inner_local, (other * head_local) // per_group * state_width, other * head_local)
    )
    first_local = ordered_pair(first_mine, first_theirs, half, 0)
    first_full = lax.all_gather(first_local, "pair", axis=0, tiled=True)
    proj_first = jnp.dot(normed, first_full, preferred_element_type=jnp.float32).astype(
        jnp.bfloat16
    )
    conv_width = inner_local + 2 * state_cols
    conv_in = proj_first[:, :conv_width]
    proj_dt = proj_first[:, conv_width:]
    w_z_all, w_out_all, _ = lax.optimization_barrier((w_zx[:, 0], w_out, proj_first))
    z_local = ordered_pair(
        cut(w_z_all, 1, x_off, inner_local),
        swap_half(cut(w_z_all, 1, other * inner_local, inner_local)),
        half,
        0,
    )
    out_local = ordered_pair(
        cut(w_out_all, 0, x_off, inner_local),
        swap_half(cut(w_out_all, 0, other * inner_local, inner_local)),
        half,
        1,
    )
    z_full = lax.all_gather(z_local, "pair", axis=0, tiled=True)
    out_full = lax.all_gather(out_local, "pair", axis=1, tiled=True)
    proj_z = jnp.dot(normed, z_full, preferred_element_type=jnp.float32).astype(jnp.bfloat16)

    position = lax.axis_index("pair") * row_count + jnp.arange(row_count, dtype=jnp.int32)
    segment, seg_start, resume_slot, resume_start = layout(
        prompt_lengths, pack_order, resume_prompt, position
    )
    prior_rows = from_behind(conv_in[row_count - edge_rows :], "pair", 1)
    weight = jnp.concatenate(
        [
            cut(conv_x, 1, x_off, inner_local),
            cut(conv_bc[:, 0], 1, bc_off, state_cols),
            cut(conv_bc[:, 1], 1, bc_off, state_cols),
        ],
        axis=1,
    )
    carry_rows = jnp.concatenate(
        [
            cut(carry_conv_x, 1, x_off, inner_local),
            cut(carry_conv_bc[:, 0], 1, bc_off, state_cols),
            cut(carry_conv_bc[:, 1], 1, bc_off, state_cols),
        ],
        axis=1,
    )
    conv_out = conv_rows(
        conv_in,
        prior_rows,
        weight,
        carry_rows,
        segment,
        seg_start,
        position,
        resume_slot,
        resume_start,
    )
    x_conv = conv_out[:, :inner_local].reshape(span_count, SPAN, group_local, per_local, head_width)
    b_conv = conv_out[:, inner_local : inner_local + state_cols].reshape(
        span_count, SPAN, group_local, state_width
    )
    c_conv = conv_out[:, inner_local + state_cols :].reshape(
        span_count, SPAN, group_local, state_width
    )
    dt_full = jax.nn.softplus(
        proj_dt.astype(jnp.float32) + cut(dt_bias, 0, h_off, head_local)[None, :]
    ).reshape(span_count, SPAN, group_local, per_local)
    seg_blocks = segment.reshape(span_count, SPAN)
    starting = (position == seg_start).reshape(span_count, SPAN)
    resumed = (segment == resume_slot).reshape(span_count, SPAN)
    resume_hit = (position == resume_start).reshape(span_count, SPAN)
    head_rate = cut(decay_rate, 0, h_off, head_local).reshape(group_local, per_local)
    skip_gain = cut(d_skip, 0, h_off, head_local).reshape(group_local, per_local)
    carry_init = cut(carry_state, 0, h_off, head_local).reshape(
        group_local, per_local, head_width, state_width
    )
    direct, state_gain, update, span_decay = span_pieces(
        x_conv,
        b_conv,
        c_conv,
        dt_full,
        head_rate,
        seg_blocks,
        starting,
        resumed,
        resume_hit,
        carry_init,
        skip_gain,
    )

    def fold_span(carried, pieces):
        return (
            (pieces[1][..., None, None] * carried[0] + pieces[0], pieces[1] * carried[1]),
            carried,
        )

    empty_state = jnp.zeros((group_local, per_local, head_width, state_width), jnp.float32)
    unit_decay = jnp.ones((group_local, per_local), jnp.float32)
    (local_state, local_decay), (prefix_state, prefix_decay) = lax.scan(
        fold_span, (empty_state, unit_decay), (update, span_decay)
    )
    hop_count = max(1, lax.axis_size("pair") // 4)
    incoming = jnp.zeros_like(local_state)
    reach = jnp.ones_like(local_decay)
    for steps in range(1, hop_count + 1):
        state_back, decay_back = from_behind((local_state, local_decay), "pair", steps)
        incoming = incoming + reach[..., None, None] * state_back
        reach = reach * decay_back
    entering = prefix_decay[..., None, None] * incoming[None] + prefix_state
    from_state = product_of("cghpn,cqgn->cqghp", entering, c_conv)
    ssd_out = (direct + state_gain[..., None] * from_state).reshape(row_count, inner_local)
    gate_act = jax.nn.silu(proj_z.astype(jnp.float32))
    gated = (ssd_out * gate_act).reshape(row_count, group_local, inner_local // group_local)
    squares = jnp.sum(gated * gated, axis=-1, keepdims=True)
    if head_local < per_group:
        squares = lax.psum(squares, "half")
    factor = lax.rsqrt(squares / (per_group * head_width) + EPS)
    normed_y = (
        (gated * factor).reshape(row_count, inner_local) * cut(gated_gain, 0, x_off, inner_local)[None, :]
    ).astype(jnp.bfloat16)
    piece = own_rows // core_count
    by_owner = normed_y.reshape(2, core_count, piece, inner_local)
    chunk_count = 4
    chunk = out_full.shape[1] // chunk_count
    results = []
    for index in range(chunk_count):
        columns = out_full[:, index * chunk : (index + 1) * chunk]
        total = None
        for shift in list(range(1, core_count)) + [0]:
            rows = lax.dynamic_index_in_dim(by_owner, (core + shift) % core_count, 1, keepdims=False)
            part = jnp.einsum("hrc,cd->hrd", rows, columns, preferred_element_type=jnp.float32)
            if shift:
                part = lax.ppermute(
                    part.astype(jnp.bfloat16),
                    "fsdp",
                    [(j, (j + shift) % core_count) for j in range(core_count)],
                ).astype(jnp.float32)
            total = part if total is None else total + part
        mine = lax.dynamic_index_in_dim(total, half, 0, keepdims=False)
        theirs = lax.dynamic_index_in_dim(total, 1 - half, 0, keepdims=False)
        theirs = swap_half(theirs.astype(jnp.bfloat16))
        results.append((mine + theirs.astype(jnp.float32)).astype(jnp.bfloat16))
    return jnp.concatenate(results, axis=1)


def solution(mesh):
    seq_count = mesh.shape["seq"]
    devices = mesh.devices.reshape(seq_count // 2, 2, mesh.shape["fsdp"])
    paired = jax.sharding.Mesh(devices, ("pair", "half", "fsdp"))
    seq = ("pair", "half")
    return jax.shard_map(
        body,
        mesh=paired,
        in_specs=(
            P(seq, None),
            P(),
            P(seq, None, "fsdp"),
            P(seq, None, "fsdp"),
            P(seq, "fsdp"),
            P(None, "fsdp"),
            P(None, None, "fsdp"),
            P("fsdp"),
            P("fsdp"),
            P("fsdp"),
            P("fsdp"),
            P("fsdp", seq),
            P(),
            P(),
            P(),
            P("fsdp", None, None),
            P(None, "fsdp"),
            P(None, None, "fsdp"),
        ),
        out_specs=P(("pair", "half", "fsdp"), None),
        check_vma=False,
    )
```

```python
import jax
import jax.numpy as jnp
from jax import lax
from jax.sharding import PartitionSpec as P

SPAN = 256


EPS = 1e-05


def from_behind(value, axis, steps):
    count = lax.axis_size(axis)
    leading, last = (max(0, -steps), min(count, count - steps))
    return lax.ppermute(value, axis, [(source, source + steps) for source in range(leading, last)])


def ring_order(count):
    return list(range(0, count, 2)) + list(range(count - 1, 0, -2))


def ring_gather(local, axis, order):
    count = len(order)
    forward = [(order[k], order[(k + 1) % count]) for k in range(count)]
    backward = [(order[k], order[(k - 1) % count]) for k in range(count)]
    chunks = [local] + [None] * (count - 1)
    ahead, behind = local, local
    for steps in range(1, count // 2 + 1):
        ahead = lax.ppermute(ahead, axis, forward)
        chunks[steps] = ahead
        if steps < count - steps:
            behind = lax.ppermute(behind, axis, backward)
            chunks[count - steps] = behind
    return chunks


def ring_columns(values, axis, order, width):
    count = len(order)
    table = jnp.asarray(order, jnp.int32)
    places = jnp.asarray([order.index(k) for k in range(count)], jnp.int32)
    place = places[lax.axis_index(axis)]
    blocks = [
        lax.dynamic_slice_in_dim(values, table[(place - offset) % count] * width, width, 1)
        for offset in range(count)
    ]
    return jnp.concatenate(blocks, axis=1)


def product_of(form, left, right):
    if left.dtype == jnp.bfloat16 and right.dtype == jnp.bfloat16:
        return jnp.einsum(form, left, right, preferred_element_type=jnp.float32)
    return jnp.einsum(form, left, right.astype(jnp.float32), precision=lax.Precision.HIGHEST)


def norm_rows(values, row_gain):
    widened = values.astype(jnp.float32)
    factor = lax.rsqrt(jnp.mean(widened * widened, axis=-1, keepdims=True) + EPS)
    return (widened * factor * row_gain[None, :]).astype(jnp.bfloat16)


def layout(prompt_lengths, pack_order, resume_prompt, position):
    prompt_count = pack_order.shape[0]
    slot_ids = jnp.arange(prompt_count, dtype=jnp.int32)
    ordered = jnp.sum(
        jnp.where(pack_order[:, None] == slot_ids[None, :], prompt_lengths[None, :], 0), axis=1
    )
    seg_starts = jnp.cumsum(ordered, dtype=jnp.int32) - ordered
    reached = position[:, None] >= seg_starts[None, :]
    segment = jnp.sum(reached.astype(jnp.int32), axis=1) - 1
    seg_start = jnp.max(jnp.where(reached, seg_starts[None, :], 0), axis=1)
    resume_slot = jnp.sum(jnp.where(pack_order == resume_prompt[0], slot_ids, 0))
    resume_start = jnp.sum(jnp.where(slot_ids == resume_slot, seg_starts, 0))
    return (segment, seg_start, resume_slot, resume_start)


def conv_rows(
    source, prior_rows, weight, carry_rows, segment, seg_start, position, resume_slot, resume_start
):
    row_count = source.shape[0]
    edge_rows = prior_rows.shape[0]
    extended = jnp.concatenate([prior_rows, source], axis=0)
    resumed = (segment == resume_slot)[:, None]
    summed = jnp.zeros(source.shape, jnp.float32)
    for back_by in range(edge_rows + 1):
        shifted = extended[edge_rows - back_by : edge_rows - back_by + row_count].astype(
            jnp.float32
        )
        inside = (position - back_by >= seg_start)[:, None]
        carry_index = position - back_by - resume_start + edge_rows
        from_carry = jnp.zeros(source.shape, jnp.float32)
        for slot_id in range(edge_rows):
            from_carry = from_carry + jnp.where(
                (carry_index == slot_id)[:, None],
                carry_rows[slot_id].astype(jnp.float32)[None, :],
                0.0,
            )
        chosen = jnp.where(inside, shifted, jnp.where(resumed, from_carry, 0.0))
        summed = summed + chosen * weight[edge_rows - back_by].astype(jnp.float32)[None, :]
    return jax.nn.silu(summed).astype(jnp.bfloat16)


def span_pieces(
    x_blocks,
    b_blocks,
    c_blocks,
    dt_blocks,
    head_rate,
    segment,
    starting,
    resumed,
    resume_hit,
    carry_init,
    skip_gain,
):
    block_len = segment.shape[1]
    log_decay = -dt_blocks * head_rate[None, None]
    cumulative = jnp.cumsum(log_decay, axis=1)
    indices = jnp.arange(block_len, dtype=jnp.int32)
    causal = (indices[:, None] >= indices[None, :])[None] & (
        segment[:, :, None] == segment[:, None, :]
    )
    cum_rows = jnp.moveaxis(cumulative, 1, -1)
    log_gap = cum_rows[..., :, None] - cum_rows[..., None, :]
    within = causal[:, None, None]
    decays = jnp.where(within, jnp.exp(jnp.where(within, log_gap, 0.0)), 0.0)
    scores = product_of("cqgn,csgn->cgqs", c_blocks, b_blocks)
    dt_source = jnp.moveaxis(dt_blocks, 1, -1)[..., None, :]
    weights = (scores[:, :, None] * decays * dt_source).astype(jnp.bfloat16)
    direct = product_of("cghqs,csghp->cqghp", weights, x_blocks)
    cum_end = cumulative[:, -1]
    tail_mask = (segment == segment[:, -1:])[:, :, None, None]
    to_end = (
        jnp.where(tail_mask, jnp.exp(jnp.where(tail_mask, cum_end[:, None] - cumulative, 0.0)), 0.0)
        * dt_blocks
    )
    scaled = (x_blocks.astype(jnp.float32) * to_end[..., None]).astype(jnp.bfloat16)
    update = product_of("cqghp,cqgn->cghpn", scaled, b_blocks)
    opened = jnp.any(starting, axis=1)
    span_decay = jnp.where(opened[:, None, None], 0.0, jnp.exp(cum_end))
    hit_mask = resume_hit[:, :, None, None]
    has_hit = jnp.any(resume_hit, axis=1)[:, None, None, None]
    cum_hit = jnp.sum(jnp.where(hit_mask, cumulative - log_decay, 0.0), axis=1, keepdims=True)
    carry_mask = resumed[:, :, None, None] & has_hit
    carry_gain = jnp.where(
        carry_mask, jnp.exp(jnp.where(carry_mask, cumulative - cum_hit, 0.0)), 0.0
    )
    end_gain = carry_gain[:, -1]
    update = update + end_gain[..., None, None] * carry_init[None]
    direct = direct + carry_gain[..., None] * product_of("ghpn,cqgn->cqghp", carry_init, c_blocks)
    direct = direct + skip_gain[None, None, :, :, None] * x_blocks.astype(jnp.float32)
    unopened = jnp.cumsum(starting.astype(jnp.int32), axis=1, dtype=jnp.int32) == 0
    state_gain = jnp.where(unopened[:, :, None, None], jnp.exp(cumulative), 0.0)
    return (direct, state_gain, update, span_decay)


def swap_half(value):
    count = lax.axis_size("half")
    return lax.ppermute(value, "half", [(k, count - 1 - k) for k in range(count)])


def ordered_pair(own, other, half, axis):
    return jnp.where(
        half == 0,
        jnp.concatenate([own, other], axis=axis),
        jnp.concatenate([other, own], axis=axis),
    )


def body(
    tokens,
    norm_gain,
    w_zx,
    w_bc,
    w_dt,
    conv_x,
    conv_bc,
    dt_bias,
    decay_rate,
    d_skip,
    gated_gain,
    w_out,
    prompt_lengths,
    pack_order,
    resume_prompt,
    carry_state,
    carry_conv_x,
    carry_conv_bc,
):
    own_rows = tokens.shape[0]
    row_count = 2 * own_rows
    edge_rows = conv_x.shape[0] - 1
    head_width = carry_state.shape[1]
    state_width = carry_state.shape[2]
    head_fsdp = w_dt.shape[1]
    group_fsdp = w_bc.shape[2] // state_width
    per_group = head_fsdp // group_fsdp
    head_local = head_fsdp // 2
    group_local = max(1, head_local // per_group)
    per_local = min(per_group, head_local)
    inner_local = head_local * head_width
    state_cols = group_local * state_width
    span_count = row_count // SPAN
    half = lax.axis_index("half")
    core = lax.axis_index("fsdp")
    core_count = lax.axis_size("fsdp")
    x_off = half * inner_local
    bc_off = (half * head_local) // per_group * state_width
    h_off = half * head_local

    def cut(value, axis, offset, width):
        return lax.dynamic_slice_in_dim(value, offset, width, axis)

    normed_own = norm_rows(tokens, norm_gain)
    share = own_rows // core_count
    fetched = swap_half(cut(normed_own, 0, core * share, share))
    arrived = [fetched] + [
        lax.ppermute(fetched, "fsdp", [(j, (j + shift) % core_count) for j in range(core_count)])
        for shift in range(1, core_count)
    ]
    arrived = jnp.stack(arrived)
    owners = (core - jnp.arange(core_count, dtype=jnp.int32)) % core_count
    normed_other = jnp.take(arrived, owners, axis=0).reshape(own_rows, tokens.shape[1])
    normed = ordered_pair(normed_own, normed_other, half, 0)

    def first_cols(offset_x, offset_bc, offset_h):
        return jnp.concatenate(
            [
                cut(w_zx[:, 1], 1, offset_x, inner_local),
                cut(w_bc[:, 0], 1, offset_bc, state_cols),
                cut(w_bc[:, 1], 1, offset_bc, state_cols),
                cut(w_dt, 1, offset_h, head_local),
            ],
            axis=1,
        )

    other = 1 - half
    first_mine = first_cols(x_off, bc_off, h_off)
    first_theirs = swap_half(
        first_cols(other * inner_local, (other * head_local) // per_group * state_width, other * head_local)
    )
    first_local = ordered_pair(first_mine, first_theirs, half, 0)
    first_full = lax.all_gather(first_local, "pair", axis=0, tiled=True)
    proj_first = jnp.dot(normed, first_full, preferred_element_type=jnp.float32).astype(
        jnp.bfloat16
    )
    conv_width = inner_local + 2 * state_cols
    conv_in = proj_first[:, :conv_width]
    proj_dt = proj_first[:, conv_width:]
    w_z_all, w_out_all, _ = lax.optimization_barrier((w_zx[:, 0], w_out, proj_first))
    z_local = ordered_pair(
        cut(w_z_all, 1, x_off, inner_local),
        swap_half(cut(w_z_all, 1, other * inner_local, inner_local)),
        half,
        0,
    )
    out_local = ordered_pair(
        cut(w_out_all, 0, x_off, inner_local),
        swap_half(cut(w_out_all, 0, other * inner_local, inner_local)),
        half,
        1,
    )
    out_full = lax.all_gather(out_local, "pair", axis=1, tiled=True)
    z_split = z_local.shape[1] // 2
    z_full = lax.all_gather(z_local[:, :z_split], "pair", axis=0, tiled=True)
    order = ring_order(lax.axis_size("pair"))
    z_chunks = ring_gather(z_local[:, z_split:], "pair", order)
    normed_ring = ring_columns(normed, "pair", order, z_local.shape[0])
    proj_z = jnp.concatenate(
        [
            jnp.dot(normed, z_full, preferred_element_type=jnp.float32),
            jnp.dot(
                normed_ring,
                jnp.concatenate(z_chunks, axis=0),
                preferred_element_type=jnp.float32,
            ),
        ],
        axis=1,
    ).astype(jnp.bfloat16)

    position = lax.axis_index("pair") * row_count + jnp.arange(row_count, dtype=jnp.int32)
    segment, seg_start, resume_slot, resume_start = layout(
        prompt_lengths, pack_order, resume_prompt, position
    )
    prior_rows = from_behind(conv_in[row_count - edge_rows :], "pair", 1)
    weight = jnp.concatenate(
        [
            cut(conv_x, 1, x_off, inner_local),
            cut(conv_bc[:, 0], 1, bc_off, state_cols),
            cut(conv_bc[:, 1], 1, bc_off, state_cols),
        ],
        axis=1,
    )
    carry_rows = jnp.concatenate(
        [
            cut(carry_conv_x, 1, x_off, inner_local),
            cut(carry_conv_bc[:, 0], 1, bc_off, state_cols),
            cut(carry_conv_bc[:, 1], 1, bc_off, state_cols),
        ],
        axis=1,
    )
    conv_out = conv_rows(
        conv_in,
        prior_rows,
        weight,
        carry_rows,
        segment,
        seg_start,
        position,
        resume_slot,
        resume_start,
    )
    x_conv = conv_out[:, :inner_local].reshape(span_count, SPAN, group_local, per_local, head_width)
    b_conv = conv_out[:, inner_local : inner_local + state_cols].reshape(
        span_count, SPAN, group_local, state_width
    )
    c_conv = conv_out[:, inner_local + state_cols :].reshape(
        span_count, SPAN, group_local, state_width
    )
    dt_full = jax.nn.softplus(
        proj_dt.astype(jnp.float32) + cut(dt_bias, 0, h_off, head_local)[None, :]
    ).reshape(span_count, SPAN, group_local, per_local)
    seg_blocks = segment.reshape(span_count, SPAN)
    starting = (position == seg_start).reshape(span_count, SPAN)
    resumed = (segment == resume_slot).reshape(span_count, SPAN)
    resume_hit = (position == resume_start).reshape(span_count, SPAN)
    head_rate = cut(decay_rate, 0, h_off, head_local).reshape(group_local, per_local)
    skip_gain = cut(d_skip, 0, h_off, head_local).reshape(group_local, per_local)
    carry_init = cut(carry_state, 0, h_off, head_local).reshape(
        group_local, per_local, head_width, state_width
    )
    direct, state_gain, update, span_decay = span_pieces(
        x_conv,
        b_conv,
        c_conv,
        dt_full,
        head_rate,
        seg_blocks,
        starting,
        resumed,
        resume_hit,
        carry_init,
        skip_gain,
    )

    def fold_span(carried, pieces):
        return (
            (pieces[1][..., None, None] * carried[0] + pieces[0], pieces[1] * carried[1]),
            carried,
        )

    empty_state = jnp.zeros((group_local, per_local, head_width, state_width), jnp.float32)
    unit_decay = jnp.ones((group_local, per_local), jnp.float32)
    (local_state, local_decay), (prefix_state, prefix_decay) = lax.scan(
        fold_span, (empty_state, unit_decay), (update, span_decay)
    )
    hop_count = max(1, lax.axis_size("pair") // 4)
    incoming = jnp.zeros_like(local_state)
    reach = jnp.ones_like(local_decay)
    for steps in range(1, hop_count + 1):
        state_back, decay_back = from_behind((local_state, local_decay), "pair", steps)
        incoming = incoming + reach[..., None, None] * state_back
        reach = reach * decay_back
    entering = prefix_decay[..., None, None] * incoming[None] + prefix_state
    from_state = product_of("cghpn,cqgn->cqghp", entering, c_conv)
    ssd_out = (direct + state_gain[..., None] * from_state).reshape(row_count, inner_local)
    gate_act = jax.nn.silu(proj_z.astype(jnp.float32))
    gated = (ssd_out * gate_act).reshape(row_count, group_local, inner_local // group_local)
    squares = jnp.sum(gated * gated, axis=-1, keepdims=True)
    if head_local < per_group:
        squares = lax.psum(squares, "half")
    factor = lax.rsqrt(squares / (per_group * head_width) + EPS)
    normed_y = (
        (gated * factor).reshape(row_count, inner_local) * cut(gated_gain, 0, x_off, inner_local)[None, :]
    ).astype(jnp.bfloat16)
    piece = own_rows // core_count
    by_owner = normed_y.reshape(2, core_count, piece, inner_local)
    chunk_count = 4
    chunk = out_full.shape[1] // chunk_count
    results = []
    for index in range(chunk_count):
        columns = out_full[:, index * chunk : (index + 1) * chunk]
        total = None
        for shift in list(range(1, core_count)) + [0]:
            rows = lax.dynamic_index_in_dim(by_owner, (core + shift) % core_count, 1, keepdims=False)
            part = jnp.einsum("hrc,cd->hrd", rows, columns, preferred_element_type=jnp.float32)
            if shift:
                part = lax.ppermute(
                    part.astype(jnp.bfloat16),
                    "fsdp",
                    [(j, (j + shift) % core_count) for j in range(core_count)],
                ).astype(jnp.float32)
            total = part if total is None else total + part
        mine = lax.dynamic_index_in_dim(total, half, 0, keepdims=False)
        theirs = lax.dynamic_index_in_dim(total, 1 - half, 0, keepdims=False)
        theirs = swap_half(theirs.astype(jnp.bfloat16))
        results.append((mine + theirs.astype(jnp.float32)).astype(jnp.bfloat16))
    return jnp.concatenate(results, axis=1)


def solution(mesh):
    seq_count = mesh.shape["seq"]
    devices = mesh.devices.reshape(seq_count // 2, 2, mesh.shape["fsdp"])
    paired = jax.sharding.Mesh(devices, ("pair", "half", "fsdp"))
    seq = ("pair", "half")
    return jax.shard_map(
        body,
        mesh=paired,
        in_specs=(
            P(seq, None),
            P(),
            P(seq, None, "fsdp"),
            P(seq, None, "fsdp"),
            P(seq, "fsdp"),
            P(None, "fsdp"),
            P(None, None, "fsdp"),
            P("fsdp"),
            P("fsdp"),
            P("fsdp"),
            P("fsdp"),
            P("fsdp", seq),
            P(),
            P(),
            P(),
            P("fsdp", None, None),
            P(None, "fsdp"),
            P(None, None, "fsdp"),
        ),
        out_specs=P(("pair", "half", "fsdp"), None),
        check_vma=False,
    )
```

```python
import jax
import jax.numpy as jnp
from jax import lax
from jax.sharding import PartitionSpec as P

SPAN = 256


EPS = 1e-05


def from_behind(value, axis, steps):
    count = lax.axis_size(axis)
    leading, last = (max(0, -steps), min(count, count - steps))
    return lax.ppermute(value, axis, [(source, source + steps) for source in range(leading, last)])


def product_of(form, left, right):
    if left.dtype == jnp.bfloat16 and right.dtype == jnp.bfloat16:
        return jnp.einsum(form, left, right, preferred_element_type=jnp.float32)
    return jnp.einsum(form, left, right.astype(jnp.float32), precision=lax.Precision.HIGHEST)


def norm_rows(values, row_gain):
    widened = values.astype(jnp.float32)
    factor = lax.rsqrt(jnp.mean(widened * widened, axis=-1, keepdims=True) + EPS)
    return (widened * factor * row_gain[None, :]).astype(jnp.bfloat16)


def layout(prompt_lengths, pack_order, resume_prompt, position):
    prompt_count = pack_order.shape[0]
    slot_ids = jnp.arange(prompt_count, dtype=jnp.int32)
    ordered = jnp.sum(
        jnp.where(pack_order[:, None] == slot_ids[None, :], prompt_lengths[None, :], 0), axis=1
    )
    seg_starts = jnp.cumsum(ordered, dtype=jnp.int32) - ordered
    reached = position[:, None] >= seg_starts[None, :]
    segment = jnp.sum(reached.astype(jnp.int32), axis=1) - 1
    seg_start = jnp.max(jnp.where(reached, seg_starts[None, :], 0), axis=1)
    resume_slot = jnp.sum(jnp.where(pack_order == resume_prompt[0], slot_ids, 0))
    resume_start = jnp.sum(jnp.where(slot_ids == resume_slot, seg_starts, 0))
    return (segment, seg_start, resume_slot, resume_start)


def conv_rows(
    source, prior_rows, weight, carry_rows, segment, seg_start, position, resume_slot, resume_start
):
    row_count = source.shape[0]
    edge_rows = prior_rows.shape[0]
    extended = jnp.concatenate([prior_rows, source], axis=0)
    resumed = (segment == resume_slot)[:, None]
    summed = jnp.zeros(source.shape, jnp.float32)
    for back_by in range(edge_rows + 1):
        shifted = extended[edge_rows - back_by : edge_rows - back_by + row_count].astype(
            jnp.float32
        )
        inside = (position - back_by >= seg_start)[:, None]
        carry_index = position - back_by - resume_start + edge_rows
        from_carry = jnp.zeros(source.shape, jnp.float32)
        for slot_id in range(edge_rows):
            from_carry = from_carry + jnp.where(
                (carry_index == slot_id)[:, None],
                carry_rows[slot_id].astype(jnp.float32)[None, :],
                0.0,
            )
        chosen = jnp.where(inside, shifted, jnp.where(resumed, from_carry, 0.0))
        summed = summed + chosen * weight[edge_rows - back_by].astype(jnp.float32)[None, :]
    return jax.nn.silu(summed).astype(jnp.bfloat16)


def span_pieces(
    x_blocks,
    b_blocks,
    c_blocks,
    dt_blocks,
    head_rate,
    segment,
    starting,
    resumed,
    resume_hit,
    carry_init,
    skip_gain,
):
    block_len = segment.shape[1]
    log_decay = -dt_blocks * head_rate[None, None]
    cumulative = jnp.cumsum(log_decay, axis=1)
    indices = jnp.arange(block_len, dtype=jnp.int32)
    causal = (indices[:, None] >= indices[None, :])[None] & (
        segment[:, :, None] == segment[:, None, :]
    )
    cum_rows = jnp.moveaxis(cumulative, 1, -1)
    log_gap = cum_rows[..., :, None] - cum_rows[..., None, :]
    within = causal[:, None, None]
    decays = jnp.where(within, jnp.exp(jnp.where(within, log_gap, 0.0)), 0.0)
    scores = product_of("cqgn,csgn->cgqs", c_blocks, b_blocks)
    dt_source = jnp.moveaxis(dt_blocks, 1, -1)[..., None, :]
    weights = (scores[:, :, None] * decays * dt_source).astype(jnp.bfloat16)
    direct = product_of("cghqs,csghp->cqghp", weights, x_blocks)
    cum_end = cumulative[:, -1]
    tail_mask = (segment == segment[:, -1:])[:, :, None, None]
    to_end = (
        jnp.where(tail_mask, jnp.exp(jnp.where(tail_mask, cum_end[:, None] - cumulative, 0.0)), 0.0)
        * dt_blocks
    )
    scaled = (x_blocks.astype(jnp.float32) * to_end[..., None]).astype(jnp.bfloat16)
    update = product_of("cqghp,cqgn->cghpn", scaled, b_blocks)
    opened = jnp.any(starting, axis=1)
    span_decay = jnp.where(opened[:, None, None], 0.0, jnp.exp(cum_end))
    hit_mask = resume_hit[:, :, None, None]
    has_hit = jnp.any(resume_hit, axis=1)[:, None, None, None]
    cum_hit = jnp.sum(jnp.where(hit_mask, cumulative - log_decay, 0.0), axis=1, keepdims=True)
    carry_mask = resumed[:, :, None, None] & has_hit
    carry_gain = jnp.where(
        carry_mask, jnp.exp(jnp.where(carry_mask, cumulative - cum_hit, 0.0)), 0.0
    )
    end_gain = carry_gain[:, -1]
    update = update + end_gain[..., None, None] * carry_init[None]
    direct = direct + carry_gain[..., None] * product_of("ghpn,cqgn->cqghp", carry_init, c_blocks)
    direct = direct + skip_gain[None, None, :, :, None] * x_blocks.astype(jnp.float32)
    unopened = jnp.cumsum(starting.astype(jnp.int32), axis=1, dtype=jnp.int32) == 0
    state_gain = jnp.where(unopened[:, :, None, None], jnp.exp(cumulative), 0.0)
    return (direct, state_gain, update, span_decay)


def swap_half(value):
    count = lax.axis_size("half")
    return lax.ppermute(value, "half", [(k, count - 1 - k) for k in range(count)])


def ordered_pair(own, other, half, axis):
    return jnp.where(
        half == 0,
        jnp.concatenate([own, other], axis=axis),
        jnp.concatenate([other, own], axis=axis),
    )


def body(
    tokens,
    norm_gain,
    w_zx,
    w_bc,
    w_dt,
    conv_x,
    conv_bc,
    dt_bias,
    decay_rate,
    d_skip,
    gated_gain,
    w_out,
    prompt_lengths,
    pack_order,
    resume_prompt,
    carry_state,
    carry_conv_x,
    carry_conv_bc,
):
    own_rows = tokens.shape[0]
    row_count = 2 * own_rows
    edge_rows = conv_x.shape[0] - 1
    head_width = carry_state.shape[1]
    state_width = carry_state.shape[2]
    head_fsdp = w_dt.shape[1]
    group_fsdp = w_bc.shape[2] // state_width
    per_group = head_fsdp // group_fsdp
    head_local = head_fsdp // 2
    group_local = max(1, head_local // per_group)
    per_local = min(per_group, head_local)
    inner_local = head_local * head_width
    state_cols = group_local * state_width
    span_count = row_count // SPAN
    half = lax.axis_index("half")
    core = lax.axis_index("fsdp")
    core_count = lax.axis_size("fsdp")
    x_off = half * inner_local
    bc_off = (half * head_local) // per_group * state_width
    h_off = half * head_local

    def cut(value, axis, offset, width):
        return lax.dynamic_slice_in_dim(value, offset, width, axis)

    normed_own = norm_rows(tokens, norm_gain)
    share = own_rows // core_count
    fetched = swap_half(cut(normed_own, 0, core * share, share))
    arrived = [fetched] + [
        lax.ppermute(fetched, "fsdp", [(j, (j + shift) % core_count) for j in range(core_count)])
        for shift in range(1, core_count)
    ]
    arrived = jnp.stack(arrived)
    owners = (core - jnp.arange(core_count, dtype=jnp.int32)) % core_count
    normed_other = jnp.take(arrived, owners, axis=0).reshape(own_rows, tokens.shape[1])
    normed = ordered_pair(normed_own, normed_other, half, 0)

    def first_cols(offset_x, offset_bc, offset_h):
        return jnp.concatenate(
            [
                cut(w_zx[:, 1], 1, offset_x, inner_local),
                cut(w_bc[:, 0], 1, offset_bc, state_cols),
                cut(w_bc[:, 1], 1, offset_bc, state_cols),
                cut(w_dt, 1, offset_h, head_local),
            ],
            axis=1,
        )

    other = 1 - half
    first_mine = first_cols(x_off, bc_off, h_off)
    first_theirs = swap_half(
        first_cols(other * inner_local, (other * head_local) // per_group * state_width, other * head_local)
    )
    first_local = ordered_pair(first_mine, first_theirs, half, 0)
    first_full = lax.all_gather(first_local, "pair", axis=0, tiled=True)
    proj_first = jnp.dot(normed, first_full, preferred_element_type=jnp.float32).astype(
        jnp.bfloat16
    )
    conv_width = inner_local + 2 * state_cols
    conv_in = proj_first[:, :conv_width]
    proj_dt = proj_first[:, conv_width:]
    w_z_all, w_out_all, _ = lax.optimization_barrier((w_zx[:, 0], w_out, proj_first))
    z_local = ordered_pair(
        cut(w_z_all, 1, x_off, inner_local),
        swap_half(cut(w_z_all, 1, other * inner_local, inner_local)),
        half,
        0,
    )
    out_local = ordered_pair(
        cut(w_out_all, 0, x_off, inner_local),
        swap_half(cut(w_out_all, 0, other * inner_local, inner_local)),
        half,
        1,
    )
    late_full = lax.all_gather(
        jnp.concatenate([z_local, out_local.T], axis=1), "pair", axis=0, tiled=True
    )
    z_full = late_full[:, :inner_local]
    out_rows = late_full[:, inner_local:]
    proj_z = jnp.dot(normed, z_full, preferred_element_type=jnp.float32).astype(jnp.bfloat16)

    position = lax.axis_index("pair") * row_count + jnp.arange(row_count, dtype=jnp.int32)
    segment, seg_start, resume_slot, resume_start = layout(
        prompt_lengths, pack_order, resume_prompt, position
    )
    prior_rows = from_behind(conv_in[row_count - edge_rows :], "pair", 1)
    weight = jnp.concatenate(
        [
            cut(conv_x, 1, x_off, inner_local),
            cut(conv_bc[:, 0], 1, bc_off, state_cols),
            cut(conv_bc[:, 1], 1, bc_off, state_cols),
        ],
        axis=1,
    )
    carry_rows = jnp.concatenate(
        [
            cut(carry_conv_x, 1, x_off, inner_local),
            cut(carry_conv_bc[:, 0], 1, bc_off, state_cols),
            cut(carry_conv_bc[:, 1], 1, bc_off, state_cols),
        ],
        axis=1,
    )
    conv_out = conv_rows(
        conv_in,
        prior_rows,
        weight,
        carry_rows,
        segment,
        seg_start,
        position,
        resume_slot,
        resume_start,
    )
    x_conv = conv_out[:, :inner_local].reshape(span_count, SPAN, group_local, per_local, head_width)
    b_conv = conv_out[:, inner_local : inner_local + state_cols].reshape(
        span_count, SPAN, group_local, state_width
    )
    c_conv = conv_out[:, inner_local + state_cols :].reshape(
        span_count, SPAN, group_local, state_width
    )
    dt_full = jax.nn.softplus(
        proj_dt.astype(jnp.float32) + cut(dt_bias, 0, h_off, head_local)[None, :]
    ).reshape(span_count, SPAN, group_local, per_local)
    seg_blocks = segment.reshape(span_count, SPAN)
    starting = (position == seg_start).reshape(span_count, SPAN)
    resumed = (segment == resume_slot).reshape(span_count, SPAN)
    resume_hit = (position == resume_start).reshape(span_count, SPAN)
    head_rate = cut(decay_rate, 0, h_off, head_local).reshape(group_local, per_local)
    skip_gain = cut(d_skip, 0, h_off, head_local).reshape(group_local, per_local)
    carry_init = cut(carry_state, 0, h_off, head_local).reshape(
        group_local, per_local, head_width, state_width
    )
    direct, state_gain, update, span_decay = span_pieces(
        x_conv,
        b_conv,
        c_conv,
        dt_full,
        head_rate,
        seg_blocks,
        starting,
        resumed,
        resume_hit,
        carry_init,
        skip_gain,
    )

    def fold_span(carried, pieces):
        return (
            (pieces[1][..., None, None] * carried[0] + pieces[0], pieces[1] * carried[1]),
            carried,
        )

    empty_state = jnp.zeros((group_local, per_local, head_width, state_width), jnp.float32)
    unit_decay = jnp.ones((group_local, per_local), jnp.float32)
    (local_state, local_decay), (prefix_state, prefix_decay) = lax.scan(
        fold_span, (empty_state, unit_decay), (update, span_decay)
    )
    hop_count = max(1, lax.axis_size("pair") // 4)
    incoming = jnp.zeros_like(local_state)
    reach = jnp.ones_like(local_decay)
    for steps in range(1, hop_count + 1):
        state_back, decay_back = from_behind((local_state, local_decay), "pair", steps)
        incoming = incoming + reach[..., None, None] * state_back
        reach = reach * decay_back
    entering = prefix_decay[..., None, None] * incoming[None] + prefix_state
    from_state = product_of("cghpn,cqgn->cqghp", entering, c_conv)
    ssd_out = (direct + state_gain[..., None] * from_state).reshape(row_count, inner_local)
    gate_act = jax.nn.silu(proj_z.astype(jnp.float32))
    gated = (ssd_out * gate_act).reshape(row_count, group_local, inner_local // group_local)
    squares = jnp.sum(gated * gated, axis=-1, keepdims=True)
    if head_local < per_group:
        squares = lax.psum(squares, "half")
    factor = lax.rsqrt(squares / (per_group * head_width) + EPS)
    normed_y = (
        (gated * factor).reshape(row_count, inner_local) * cut(gated_gain, 0, x_off, inner_local)[None, :]
    ).astype(jnp.bfloat16)
    piece = own_rows // core_count
    by_owner = normed_y.reshape(2, core_count, piece, inner_local)
    chunk_count = 4
    chunk = out_rows.shape[0] // chunk_count
    results = []
    for index in range(chunk_count):
        columns = out_rows[index * chunk : (index + 1) * chunk]
        total = None
        for shift in list(range(1, core_count)) + [0]:
            rows = lax.dynamic_index_in_dim(by_owner, (core + shift) % core_count, 1, keepdims=False)
            part = jnp.einsum("hrc,dc->hrd", rows, columns, preferred_element_type=jnp.float32)
            if shift:
                part = lax.ppermute(
                    part.astype(jnp.bfloat16),
                    "fsdp",
                    [(j, (j + shift) % core_count) for j in range(core_count)],
                ).astype(jnp.float32)
            total = part if total is None else total + part
        mine = lax.dynamic_index_in_dim(total, half, 0, keepdims=False)
        theirs = lax.dynamic_index_in_dim(total, 1 - half, 0, keepdims=False)
        theirs = swap_half(theirs.astype(jnp.bfloat16))
        results.append((mine + theirs.astype(jnp.float32)).astype(jnp.bfloat16))
    return jnp.concatenate(results, axis=1)


def solution(mesh):
    seq_count = mesh.shape["seq"]
    devices = mesh.devices.reshape(seq_count // 2, 2, mesh.shape["fsdp"])
    paired = jax.sharding.Mesh(devices, ("pair", "half", "fsdp"))
    seq = ("pair", "half")
    return jax.shard_map(
        body,
        mesh=paired,
        in_specs=(
            P(seq, None),
            P(),
            P(seq, None, "fsdp"),
            P(seq, None, "fsdp"),
            P(seq, "fsdp"),
            P(None, "fsdp"),
            P(None, None, "fsdp"),
            P("fsdp"),
            P("fsdp"),
            P("fsdp"),
            P("fsdp"),
            P("fsdp", seq),
            P(),
            P(),
            P(),
            P("fsdp", None, None),
            P(None, "fsdp"),
            P(None, None, "fsdp"),
        ),
        out_specs=P(("pair", "half", "fsdp"), None),
        check_vma=False,
    )
```

```python
import jax
import jax.numpy as jnp
from jax import lax
from jax.sharding import PartitionSpec as P

SPAN = 256


EPS = 1e-05


def from_behind(value, axis, steps):
    count = lax.axis_size(axis)
    leading, last = (max(0, -steps), min(count, count - steps))
    return lax.ppermute(value, axis, [(source, source + steps) for source in range(leading, last)])


def product_of(form, left, right):
    if left.dtype == jnp.bfloat16 and right.dtype == jnp.bfloat16:
        return jnp.einsum(form, left, right, preferred_element_type=jnp.float32)
    return jnp.einsum(form, left, right.astype(jnp.float32), precision=lax.Precision.HIGHEST)


def norm_rows(values, row_gain):
    widened = values.astype(jnp.float32)
    factor = lax.rsqrt(jnp.mean(widened * widened, axis=-1, keepdims=True) + EPS)
    return (widened * factor * row_gain[None, :]).astype(jnp.bfloat16)


def layout(prompt_lengths, pack_order, resume_prompt, position):
    prompt_count = pack_order.shape[0]
    slot_ids = jnp.arange(prompt_count, dtype=jnp.int32)
    ordered = jnp.sum(
        jnp.where(pack_order[:, None] == slot_ids[None, :], prompt_lengths[None, :], 0), axis=1
    )
    seg_starts = jnp.cumsum(ordered, dtype=jnp.int32) - ordered
    reached = position[:, None] >= seg_starts[None, :]
    segment = jnp.sum(reached.astype(jnp.int32), axis=1) - 1
    seg_start = jnp.max(jnp.where(reached, seg_starts[None, :], 0), axis=1)
    resume_slot = jnp.sum(jnp.where(pack_order == resume_prompt[0], slot_ids, 0))
    resume_start = jnp.sum(jnp.where(slot_ids == resume_slot, seg_starts, 0))
    return (segment, seg_start, resume_slot, resume_start)


def conv_rows(
    source, prior_rows, weight, carry_rows, segment, seg_start, position, resume_slot, resume_start
):
    row_count = source.shape[0]
    edge_rows = prior_rows.shape[0]
    extended = jnp.concatenate([prior_rows, source], axis=0)
    resumed = (segment == resume_slot)[:, None]
    summed = jnp.zeros(source.shape, jnp.float32)
    for back_by in range(edge_rows + 1):
        shifted = extended[edge_rows - back_by : edge_rows - back_by + row_count].astype(
            jnp.float32
        )
        inside = (position - back_by >= seg_start)[:, None]
        carry_index = position - back_by - resume_start + edge_rows
        from_carry = jnp.zeros(source.shape, jnp.float32)
        for slot_id in range(edge_rows):
            from_carry = from_carry + jnp.where(
                (carry_index == slot_id)[:, None],
                carry_rows[slot_id].astype(jnp.float32)[None, :],
                0.0,
            )
        chosen = jnp.where(inside, shifted, jnp.where(resumed, from_carry, 0.0))
        summed = summed + chosen * weight[edge_rows - back_by].astype(jnp.float32)[None, :]
    return jax.nn.silu(summed).astype(jnp.bfloat16)


def span_pieces(
    x_blocks,
    b_blocks,
    c_blocks,
    dt_blocks,
    head_rate,
    segment,
    starting,
    resumed,
    resume_hit,
    carry_init,
    skip_gain,
):
    block_len = segment.shape[1]
    log_decay = -dt_blocks * head_rate[None, None]
    cumulative = jnp.cumsum(log_decay, axis=1)
    indices = jnp.arange(block_len, dtype=jnp.int32)
    causal = (indices[:, None] >= indices[None, :])[None] & (
        segment[:, :, None] == segment[:, None, :]
    )
    cum_rows = jnp.moveaxis(cumulative, 1, -1)
    log_gap = cum_rows[..., :, None] - cum_rows[..., None, :]
    within = causal[:, None, None]
    decays = jnp.where(within, jnp.exp(jnp.where(within, log_gap, 0.0)), 0.0)
    scores = product_of("cqgn,csgn->cgqs", c_blocks, b_blocks)
    dt_source = jnp.moveaxis(dt_blocks, 1, -1)[..., None, :]
    weights = (scores[:, :, None] * decays * dt_source).astype(jnp.bfloat16)
    direct = product_of("cghqs,csghp->cqghp", weights, x_blocks)
    cum_end = cumulative[:, -1]
    tail_mask = (segment == segment[:, -1:])[:, :, None, None]
    to_end = (
        jnp.where(tail_mask, jnp.exp(jnp.where(tail_mask, cum_end[:, None] - cumulative, 0.0)), 0.0)
        * dt_blocks
    )
    scaled = (x_blocks.astype(jnp.float32) * to_end[..., None]).astype(jnp.bfloat16)
    update = product_of("cqghp,cqgn->cghpn", scaled, b_blocks)
    opened = jnp.any(starting, axis=1)
    span_decay = jnp.where(opened[:, None, None], 0.0, jnp.exp(cum_end))
    hit_mask = resume_hit[:, :, None, None]
    has_hit = jnp.any(resume_hit, axis=1)[:, None, None, None]
    cum_hit = jnp.sum(jnp.where(hit_mask, cumulative - log_decay, 0.0), axis=1, keepdims=True)
    carry_mask = resumed[:, :, None, None] & has_hit
    carry_gain = jnp.where(
        carry_mask, jnp.exp(jnp.where(carry_mask, cumulative - cum_hit, 0.0)), 0.0
    )
    end_gain = carry_gain[:, -1]
    update = update + end_gain[..., None, None] * carry_init[None]
    direct = direct + carry_gain[..., None] * product_of("ghpn,cqgn->cqghp", carry_init, c_blocks)
    direct = direct + skip_gain[None, None, :, :, None] * x_blocks.astype(jnp.float32)
    unopened = jnp.cumsum(starting.astype(jnp.int32), axis=1, dtype=jnp.int32) == 0
    state_gain = jnp.where(unopened[:, :, None, None], jnp.exp(cumulative), 0.0)
    return (direct, state_gain, update, span_decay)


def swap_half(value):
    count = lax.axis_size("half")
    return lax.ppermute(value, "half", [(k, count - 1 - k) for k in range(count)])


def ordered_pair(own, other, half, axis):
    return jnp.where(
        half == 0,
        jnp.concatenate([own, other], axis=axis),
        jnp.concatenate([other, own], axis=axis),
    )


def body(
    tokens,
    norm_gain,
    w_zx,
    w_bc,
    w_dt,
    conv_x,
    conv_bc,
    dt_bias,
    decay_rate,
    d_skip,
    gated_gain,
    w_out,
    prompt_lengths,
    pack_order,
    resume_prompt,
    carry_state,
    carry_conv_x,
    carry_conv_bc,
):
    own_rows = tokens.shape[0]
    row_count = 2 * own_rows
    edge_rows = conv_x.shape[0] - 1
    head_width = carry_state.shape[1]
    state_width = carry_state.shape[2]
    head_fsdp = w_dt.shape[1]
    group_fsdp = w_bc.shape[2] // state_width
    per_group = head_fsdp // group_fsdp
    head_local = head_fsdp // 2
    group_local = max(1, head_local // per_group)
    per_local = min(per_group, head_local)
    inner_local = head_local * head_width
    state_cols = group_local * state_width
    span_count = row_count // SPAN
    half = lax.axis_index("half")
    core = lax.axis_index("fsdp")
    core_count = lax.axis_size("fsdp")
    x_off = half * inner_local
    bc_off = (half * head_local) // per_group * state_width
    h_off = half * head_local

    def cut(value, axis, offset, width):
        return lax.dynamic_slice_in_dim(value, offset, width, axis)

    normed_own = norm_rows(tokens, norm_gain)
    share = own_rows // core_count
    fetched = swap_half(cut(normed_own, 0, core * share, share))
    arrived = [fetched] + [
        lax.ppermute(fetched, "fsdp", [(j, (j + shift) % core_count) for j in range(core_count)])
        for shift in range(1, core_count)
    ]
    arrived = jnp.stack(arrived)
    owners = (core - jnp.arange(core_count, dtype=jnp.int32)) % core_count
    normed_other = jnp.take(arrived, owners, axis=0).reshape(own_rows, tokens.shape[1])
    normed = ordered_pair(normed_own, normed_other, half, 0)

    def first_cols(offset_x, offset_bc, offset_h):
        return jnp.concatenate(
            [
                cut(w_zx[:, 1], 1, offset_x, inner_local),
                cut(w_bc[:, 0], 1, offset_bc, state_cols),
                cut(w_bc[:, 1], 1, offset_bc, state_cols),
                cut(w_dt, 1, offset_h, head_local),
            ],
            axis=1,
        )

    other = 1 - half
    first_mine = first_cols(x_off, bc_off, h_off)
    first_theirs = swap_half(
        first_cols(other * inner_local, (other * head_local) // per_group * state_width, other * head_local)
    )
    first_local = ordered_pair(first_mine, first_theirs, half, 0)
    first_full = lax.all_gather(first_local, "pair", axis=0, tiled=True)
    proj_first = jnp.dot(normed, first_full, preferred_element_type=jnp.float32).astype(
        jnp.bfloat16
    )
    conv_width = inner_local + 2 * state_cols
    conv_in = proj_first[:, :conv_width]
    proj_dt = proj_first[:, conv_width:]
    w_z_all, w_out_all, _ = lax.optimization_barrier((w_zx[:, 0], w_out, proj_first))
    z_local = ordered_pair(
        cut(w_z_all, 1, x_off, inner_local),
        swap_half(cut(w_z_all, 1, other * inner_local, inner_local)),
        half,
        0,
    )
    out_local = ordered_pair(
        cut(w_out_all, 0, x_off, inner_local),
        swap_half(cut(w_out_all, 0, other * inner_local, inner_local)),
        half,
        1,
    )
    z_full = lax.all_gather(z_local, "pair", axis=0, tiled=True)
    out_full = lax.all_gather(out_local, "pair", axis=1, tiled=True)
    proj_z = jnp.dot(normed, z_full, preferred_element_type=jnp.float32).astype(jnp.bfloat16)

    position = lax.axis_index("pair") * row_count + jnp.arange(row_count, dtype=jnp.int32)
    segment, seg_start, resume_slot, resume_start = layout(
        prompt_lengths, pack_order, resume_prompt, position
    )
    prior_rows = from_behind(conv_in[row_count - edge_rows :], "pair", 1)
    weight = jnp.concatenate(
        [
            cut(conv_x, 1, x_off, inner_local),
            cut(conv_bc[:, 0], 1, bc_off, state_cols),
            cut(conv_bc[:, 1], 1, bc_off, state_cols),
        ],
        axis=1,
    )
    carry_rows = jnp.concatenate(
        [
            cut(carry_conv_x, 1, x_off, inner_local),
            cut(carry_conv_bc[:, 0], 1, bc_off, state_cols),
            cut(carry_conv_bc[:, 1], 1, bc_off, state_cols),
        ],
        axis=1,
    )
    conv_out = conv_rows(
        conv_in,
        prior_rows,
        weight,
        carry_rows,
        segment,
        seg_start,
        position,
        resume_slot,
        resume_start,
    )
    x_conv = conv_out[:, :inner_local].reshape(span_count, SPAN, group_local, per_local, head_width)
    b_conv = conv_out[:, inner_local : inner_local + state_cols].reshape(
        span_count, SPAN, group_local, state_width
    )
    c_conv = conv_out[:, inner_local + state_cols :].reshape(
        span_count, SPAN, group_local, state_width
    )
    dt_full = jax.nn.softplus(
        proj_dt.astype(jnp.float32) + cut(dt_bias, 0, h_off, head_local)[None, :]
    ).reshape(span_count, SPAN, group_local, per_local)
    seg_blocks = segment.reshape(span_count, SPAN)
    starting = (position == seg_start).reshape(span_count, SPAN)
    resumed = (segment == resume_slot).reshape(span_count, SPAN)
    resume_hit = (position == resume_start).reshape(span_count, SPAN)
    head_rate = cut(decay_rate, 0, h_off, head_local).reshape(group_local, per_local)
    skip_gain = cut(d_skip, 0, h_off, head_local).reshape(group_local, per_local)
    carry_init = cut(carry_state, 0, h_off, head_local).reshape(
        group_local, per_local, head_width, state_width
    )
    direct, state_gain, update, span_decay = span_pieces(
        x_conv,
        b_conv,
        c_conv,
        dt_full,
        head_rate,
        seg_blocks,
        starting,
        resumed,
        resume_hit,
        carry_init,
        skip_gain,
    )

    def fold_span(carried, pieces):
        return (
            (pieces[1][..., None, None] * carried[0] + pieces[0], pieces[1] * carried[1]),
            carried,
        )

    empty_state = jnp.zeros((group_local, per_local, head_width, state_width), jnp.float32)
    unit_decay = jnp.ones((group_local, per_local), jnp.float32)
    (local_state, local_decay), (prefix_state, prefix_decay) = lax.scan(
        fold_span, (empty_state, unit_decay), (update, span_decay)
    )
    hop_count = max(1, lax.axis_size("pair") // 4)
    incoming = jnp.zeros_like(local_state)
    reach = jnp.ones_like(local_decay)
    for steps in range(1, hop_count + 1):
        state_back, decay_back = from_behind((local_state, local_decay), "pair", steps)
        incoming = incoming + reach[..., None, None] * state_back
        reach = reach * decay_back
    entering = prefix_decay[..., None, None] * incoming[None] + prefix_state
    from_state = product_of("cghpn,cqgn->cqghp", entering, c_conv)
    ssd_out = (direct + state_gain[..., None] * from_state).reshape(row_count, inner_local)
    gate_act = jax.nn.silu(proj_z.astype(jnp.float32))
    gated = (ssd_out * gate_act).reshape(row_count, group_local, inner_local // group_local)
    squares = jnp.sum(gated * gated, axis=-1, keepdims=True)
    if head_local < per_group:
        squares = lax.psum(squares, "half")
    factor = lax.rsqrt(squares / (per_group * head_width) + EPS)
    normed_y = (
        (gated * factor).reshape(row_count, inner_local) * cut(gated_gain, 0, x_off, inner_local)[None, :]
    ).astype(jnp.bfloat16)
    piece = own_rows // core_count
    by_owner = normed_y.reshape(2, core_count, piece, inner_local)
    chunk_count = 4
    chunk = out_full.shape[1] // chunk_count
    results = []
    for index in range(chunk_count):
        columns = out_full[:, index * chunk : (index + 1) * chunk]
        total = None
        for shift in list(range(1, core_count)) + [0]:
            rows = lax.dynamic_index_in_dim(by_owner, (core + shift) % core_count, 1, keepdims=False)
            part = jnp.einsum("hrc,cd->hrd", rows, columns, preferred_element_type=jnp.float32)
            if shift:
                part = lax.ppermute(
                    part.astype(jnp.bfloat16),
                    "fsdp",
                    [(j, (j + shift) % core_count) for j in range(core_count)],
                ).astype(jnp.float32)
            total = part if total is None else total + part
        mine = lax.dynamic_index_in_dim(total, half, 0, keepdims=False)
        theirs = lax.dynamic_index_in_dim(total, 1 - half, 0, keepdims=False)
        theirs = theirs.astype(jnp.bfloat16)
        by_owner, theirs = lax.optimization_barrier((by_owner, theirs))
        theirs = swap_half(theirs)
        results.append((mine + theirs.astype(jnp.float32)).astype(jnp.bfloat16))
    return jnp.concatenate(results, axis=1)


def solution(mesh):
    seq_count = mesh.shape["seq"]
    devices = mesh.devices.reshape(seq_count // 2, 2, mesh.shape["fsdp"])
    paired = jax.sharding.Mesh(devices, ("pair", "half", "fsdp"))
    seq = ("pair", "half")
    return jax.shard_map(
        body,
        mesh=paired,
        in_specs=(
            P(seq, None),
            P(),
            P(seq, None, "fsdp"),
            P(seq, None, "fsdp"),
            P(seq, "fsdp"),
            P(None, "fsdp"),
            P(None, None, "fsdp"),
            P("fsdp"),
            P("fsdp"),
            P("fsdp"),
            P("fsdp"),
            P("fsdp", seq),
            P(),
            P(),
            P(),
            P("fsdp", None, None),
            P(None, "fsdp"),
            P(None, None, "fsdp"),
        ),
        out_specs=P(("pair", "half", "fsdp"), None),
        check_vma=False,
    )
```

```python
import jax
import jax.numpy as jnp
from jax import lax
from jax.sharding import PartitionSpec as P

SPAN = 256


EPS = 1e-05


def from_behind(value, axis, steps):
    count = lax.axis_size(axis)
    leading, last = (max(0, -steps), min(count, count - steps))
    return lax.ppermute(value, axis, [(source, source + steps) for source in range(leading, last)])


def product_of(form, left, right):
    if left.dtype == jnp.bfloat16 and right.dtype == jnp.bfloat16:
        return jnp.einsum(form, left, right, preferred_element_type=jnp.float32)
    return jnp.einsum(form, left, right.astype(jnp.float32), precision=lax.Precision.HIGHEST)


def norm_rows(values, row_gain):
    widened = values.astype(jnp.float32)
    factor = lax.rsqrt(jnp.mean(widened * widened, axis=-1, keepdims=True) + EPS)
    return (widened * factor * row_gain[None, :]).astype(jnp.bfloat16)


def layout(prompt_lengths, pack_order, resume_prompt, position):
    prompt_count = pack_order.shape[0]
    slot_ids = jnp.arange(prompt_count, dtype=jnp.int32)
    ordered = jnp.sum(
        jnp.where(pack_order[:, None] == slot_ids[None, :], prompt_lengths[None, :], 0), axis=1
    )
    seg_starts = jnp.cumsum(ordered, dtype=jnp.int32) - ordered
    reached = position[:, None] >= seg_starts[None, :]
    segment = jnp.sum(reached.astype(jnp.int32), axis=1) - 1
    seg_start = jnp.max(jnp.where(reached, seg_starts[None, :], 0), axis=1)
    resume_slot = jnp.sum(jnp.where(pack_order == resume_prompt[0], slot_ids, 0))
    resume_start = jnp.sum(jnp.where(slot_ids == resume_slot, seg_starts, 0))
    return (segment, seg_start, resume_slot, resume_start)


def conv_rows(
    source, prior_rows, weight, carry_rows, segment, seg_start, position, resume_slot, resume_start
):
    row_count = source.shape[0]
    edge_rows = prior_rows.shape[0]
    extended = jnp.concatenate([prior_rows, source], axis=0)
    resumed = (segment == resume_slot)[:, None]
    summed = jnp.zeros(source.shape, jnp.float32)
    for back_by in range(edge_rows + 1):
        shifted = extended[edge_rows - back_by : edge_rows - back_by + row_count].astype(
            jnp.float32
        )
        inside = (position - back_by >= seg_start)[:, None]
        carry_index = position - back_by - resume_start + edge_rows
        from_carry = jnp.zeros(source.shape, jnp.float32)
        for slot_id in range(edge_rows):
            from_carry = from_carry + jnp.where(
                (carry_index == slot_id)[:, None],
                carry_rows[slot_id].astype(jnp.float32)[None, :],
                0.0,
            )
        chosen = jnp.where(inside, shifted, jnp.where(resumed, from_carry, 0.0))
        summed = summed + chosen * weight[edge_rows - back_by].astype(jnp.float32)[None, :]
    return jax.nn.silu(summed).astype(jnp.bfloat16)


def span_pieces(
    x_blocks,
    b_blocks,
    c_blocks,
    dt_blocks,
    head_rate,
    segment,
    starting,
    resumed,
    resume_hit,
    carry_init,
    skip_gain,
):
    block_len = segment.shape[1]
    log_decay = -dt_blocks * head_rate[None, None]
    cumulative = jnp.cumsum(log_decay, axis=1)
    indices = jnp.arange(block_len, dtype=jnp.int32)
    causal = (indices[:, None] >= indices[None, :])[None] & (
        segment[:, :, None] == segment[:, None, :]
    )
    cum_rows = jnp.moveaxis(cumulative, 1, -1)
    log_gap = cum_rows[..., :, None] - cum_rows[..., None, :]
    within = causal[:, None, None]
    decays = jnp.where(within, jnp.exp(jnp.where(within, log_gap, 0.0)), 0.0)
    scores = product_of("cqgn,csgn->cgqs", c_blocks, b_blocks)
    dt_source = jnp.moveaxis(dt_blocks, 1, -1)[..., None, :]
    weights = (scores[:, :, None] * decays * dt_source).astype(jnp.bfloat16)
    direct = product_of("cghqs,csghp->cqghp", weights, x_blocks)
    cum_end = cumulative[:, -1]
    tail_mask = (segment == segment[:, -1:])[:, :, None, None]
    to_end = (
        jnp.where(tail_mask, jnp.exp(jnp.where(tail_mask, cum_end[:, None] - cumulative, 0.0)), 0.0)
        * dt_blocks
    )
    scaled = (x_blocks.astype(jnp.float32) * to_end[..., None]).astype(jnp.bfloat16)
    update = product_of("cqghp,cqgn->cghpn", scaled, b_blocks)
    opened = jnp.any(starting, axis=1)
    span_decay = jnp.where(opened[:, None, None], 0.0, jnp.exp(cum_end))
    hit_mask = resume_hit[:, :, None, None]
    has_hit = jnp.any(resume_hit, axis=1)[:, None, None, None]
    cum_hit = jnp.sum(jnp.where(hit_mask, cumulative - log_decay, 0.0), axis=1, keepdims=True)
    carry_mask = resumed[:, :, None, None] & has_hit
    carry_gain = jnp.where(
        carry_mask, jnp.exp(jnp.where(carry_mask, cumulative - cum_hit, 0.0)), 0.0
    )
    end_gain = carry_gain[:, -1]
    update = update + end_gain[..., None, None] * carry_init[None]
    direct = direct + carry_gain[..., None] * product_of("ghpn,cqgn->cqghp", carry_init, c_blocks)
    direct = direct + skip_gain[None, None, :, :, None] * x_blocks.astype(jnp.float32)
    unopened = jnp.cumsum(starting.astype(jnp.int32), axis=1, dtype=jnp.int32) == 0
    state_gain = jnp.where(unopened[:, :, None, None], jnp.exp(cumulative), 0.0)
    return (direct, state_gain, update, span_decay)


def swap_half(value):
    count = lax.axis_size("half")
    return lax.ppermute(value, "half", [(k, count - 1 - k) for k in range(count)])


def ordered_pair(own, other, half, axis):
    return jnp.where(
        half == 0,
        jnp.concatenate([own, other], axis=axis),
        jnp.concatenate([other, own], axis=axis),
    )


def body(
    tokens,
    norm_gain,
    w_zx,
    w_bc,
    w_dt,
    conv_x,
    conv_bc,
    dt_bias,
    decay_rate,
    d_skip,
    gated_gain,
    w_out,
    prompt_lengths,
    pack_order,
    resume_prompt,
    carry_state,
    carry_conv_x,
    carry_conv_bc,
):
    own_rows = tokens.shape[0]
    row_count = 2 * own_rows
    edge_rows = conv_x.shape[0] - 1
    head_width = carry_state.shape[1]
    state_width = carry_state.shape[2]
    head_fsdp = w_dt.shape[1]
    group_fsdp = w_bc.shape[2] // state_width
    per_group = head_fsdp // group_fsdp
    head_local = head_fsdp // 2
    group_local = max(1, head_local // per_group)
    per_local = min(per_group, head_local)
    inner_local = head_local * head_width
    state_cols = group_local * state_width
    span_count = row_count // SPAN
    half = lax.axis_index("half")
    core = lax.axis_index("fsdp")
    core_count = lax.axis_size("fsdp")
    x_off = half * inner_local
    bc_off = (half * head_local) // per_group * state_width
    h_off = half * head_local

    def cut(value, axis, offset, width):
        return lax.dynamic_slice_in_dim(value, offset, width, axis)

    normed_own = norm_rows(tokens, norm_gain)
    share = own_rows // core_count
    fetched = swap_half(cut(normed_own, 0, core * share, share))
    arrived = [fetched] + [
        lax.ppermute(fetched, "fsdp", [(j, (j + shift) % core_count) for j in range(core_count)])
        for shift in range(1, core_count)
    ]
    arrived = jnp.stack(arrived)
    owners = (core - jnp.arange(core_count, dtype=jnp.int32)) % core_count
    normed_other = jnp.take(arrived, owners, axis=0).reshape(own_rows, tokens.shape[1])
    normed = ordered_pair(normed_own, normed_other, half, 0)

    def first_cols(offset_x, offset_bc, offset_h):
        return jnp.concatenate(
            [
                cut(w_zx[:, 1], 1, offset_x, inner_local),
                cut(w_bc[:, 0], 1, offset_bc, state_cols),
                cut(w_bc[:, 1], 1, offset_bc, state_cols),
                cut(w_dt, 1, offset_h, head_local),
            ],
            axis=1,
        )

    other = 1 - half
    first_mine = first_cols(x_off, bc_off, h_off)
    first_theirs = swap_half(
        first_cols(other * inner_local, (other * head_local) // per_group * state_width, other * head_local)
    )
    mine_full = lax.all_gather(first_mine, "pair", axis=0, tiled=True)
    theirs_full = lax.all_gather(first_theirs, "pair", axis=0, tiled=True)
    block_rows = first_mine.shape[0]
    by_block = normed.reshape(row_count, lax.axis_size("pair"), 2, block_rows)
    normed_mine = lax.dynamic_index_in_dim(by_block, half, 2, keepdims=False)
    normed_theirs = lax.dynamic_index_in_dim(by_block, 1 - half, 2, keepdims=False)
    proj_first = (
        jnp.dot(normed_mine.reshape(row_count, -1), mine_full, preferred_element_type=jnp.float32)
        + jnp.dot(
            normed_theirs.reshape(row_count, -1), theirs_full, preferred_element_type=jnp.float32
        )
    ).astype(jnp.bfloat16)
    conv_width = inner_local + 2 * state_cols
    conv_in = proj_first[:, :conv_width]
    proj_dt = proj_first[:, conv_width:]
    w_z_all, w_out_all, _ = lax.optimization_barrier((w_zx[:, 0], w_out, proj_first))
    z_local = ordered_pair(
        cut(w_z_all, 1, x_off, inner_local),
        swap_half(cut(w_z_all, 1, other * inner_local, inner_local)),
        half,
        0,
    )
    out_local = ordered_pair(
        cut(w_out_all, 0, x_off, inner_local),
        swap_half(cut(w_out_all, 0, other * inner_local, inner_local)),
        half,
        1,
    )
    z_full = lax.all_gather(z_local, "pair", axis=0, tiled=True)
    out_full = lax.all_gather(out_local, "pair", axis=1, tiled=True)
    proj_z = jnp.dot(normed, z_full, preferred_element_type=jnp.float32).astype(jnp.bfloat16)

    position = lax.axis_index("pair") * row_count + jnp.arange(row_count, dtype=jnp.int32)
    segment, seg_start, resume_slot, resume_start = layout(
        prompt_lengths, pack_order, resume_prompt, position
    )
    prior_rows = from_behind(conv_in[row_count - edge_rows :], "pair", 1)
    weight = jnp.concatenate(
        [
            cut(conv_x, 1, x_off, inner_local),
            cut(conv_bc[:, 0], 1, bc_off, state_cols),
            cut(conv_bc[:, 1], 1, bc_off, state_cols),
        ],
        axis=1,
    )
    carry_rows = jnp.concatenate(
        [
            cut(carry_conv_x, 1, x_off, inner_local),
            cut(carry_conv_bc[:, 0], 1, bc_off, state_cols),
            cut(carry_conv_bc[:, 1], 1, bc_off, state_cols),
        ],
        axis=1,
    )
    conv_out = conv_rows(
        conv_in,
        prior_rows,
        weight,
        carry_rows,
        segment,
        seg_start,
        position,
        resume_slot,
        resume_start,
    )
    x_conv = conv_out[:, :inner_local].reshape(span_count, SPAN, group_local, per_local, head_width)
    b_conv = conv_out[:, inner_local : inner_local + state_cols].reshape(
        span_count, SPAN, group_local, state_width
    )
    c_conv = conv_out[:, inner_local + state_cols :].reshape(
        span_count, SPAN, group_local, state_width
    )
    dt_full = jax.nn.softplus(
        proj_dt.astype(jnp.float32) + cut(dt_bias, 0, h_off, head_local)[None, :]
    ).reshape(span_count, SPAN, group_local, per_local)
    seg_blocks = segment.reshape(span_count, SPAN)
    starting = (position == seg_start).reshape(span_count, SPAN)
    resumed = (segment == resume_slot).reshape(span_count, SPAN)
    resume_hit = (position == resume_start).reshape(span_count, SPAN)
    head_rate = cut(decay_rate, 0, h_off, head_local).reshape(group_local, per_local)
    skip_gain = cut(d_skip, 0, h_off, head_local).reshape(group_local, per_local)
    carry_init = cut(carry_state, 0, h_off, head_local).reshape(
        group_local, per_local, head_width, state_width
    )
    direct, state_gain, update, span_decay = span_pieces(
        x_conv,
        b_conv,
        c_conv,
        dt_full,
        head_rate,
        seg_blocks,
        starting,
        resumed,
        resume_hit,
        carry_init,
        skip_gain,
    )

    def fold_span(carried, pieces):
        return (
            (pieces[1][..., None, None] * carried[0] + pieces[0], pieces[1] * carried[1]),
            carried,
        )

    empty_state = jnp.zeros((group_local, per_local, head_width, state_width), jnp.float32)
    unit_decay = jnp.ones((group_local, per_local), jnp.float32)
    (local_state, local_decay), (prefix_state, prefix_decay) = lax.scan(
        fold_span, (empty_state, unit_decay), (update, span_decay)
    )
    hop_count = max(1, lax.axis_size("pair") // 4)
    incoming = jnp.zeros_like(local_state)
    reach = jnp.ones_like(local_decay)
    for steps in range(1, hop_count + 1):
        state_back, decay_back = from_behind((local_state, local_decay), "pair", steps)
        incoming = incoming + reach[..., None, None] * state_back
        reach = reach * decay_back
    entering = prefix_decay[..., None, None] * incoming[None] + prefix_state
    from_state = product_of("cghpn,cqgn->cqghp", entering, c_conv)
    ssd_out = (direct + state_gain[..., None] * from_state).reshape(row_count, inner_local)
    gate_act = jax.nn.silu(proj_z.astype(jnp.float32))
    gated = (ssd_out * gate_act).reshape(row_count, group_local, inner_local // group_local)
    squares = jnp.sum(gated * gated, axis=-1, keepdims=True)
    if head_local < per_group:
        squares = lax.psum(squares, "half")
    factor = lax.rsqrt(squares / (per_group * head_width) + EPS)
    normed_y = (
        (gated * factor).reshape(row_count, inner_local) * cut(gated_gain, 0, x_off, inner_local)[None, :]
    ).astype(jnp.bfloat16)
    piece = own_rows // core_count
    by_owner = normed_y.reshape(2, core_count, piece, inner_local)
    chunk_count = 4
    chunk = out_full.shape[1] // chunk_count
    results = []
    for index in range(chunk_count):
        columns = out_full[:, index * chunk : (index + 1) * chunk]
        total = None
        for shift in list(range(1, core_count)) + [0]:
            rows = lax.dynamic_index_in_dim(by_owner, (core + shift) % core_count, 1, keepdims=False)
            part = jnp.einsum("hrc,cd->hrd", rows, columns, preferred_element_type=jnp.float32)
            if shift:
                part = lax.ppermute(
                    part.astype(jnp.bfloat16),
                    "fsdp",
                    [(j, (j + shift) % core_count) for j in range(core_count)],
                ).astype(jnp.float32)
            total = part if total is None else total + part
        mine = lax.dynamic_index_in_dim(total, half, 0, keepdims=False)
        theirs = lax.dynamic_index_in_dim(total, 1 - half, 0, keepdims=False)
        theirs = swap_half(theirs.astype(jnp.bfloat16))
        results.append((mine + theirs.astype(jnp.float32)).astype(jnp.bfloat16))
    return jnp.concatenate(results, axis=1)


def solution(mesh):
    seq_count = mesh.shape["seq"]
    devices = mesh.devices.reshape(seq_count // 2, 2, mesh.shape["fsdp"])
    paired = jax.sharding.Mesh(devices, ("pair", "half", "fsdp"))
    seq = ("pair", "half")
    return jax.shard_map(
        body,
        mesh=paired,
        in_specs=(
            P(seq, None),
            P(),
            P(seq, None, "fsdp"),
            P(seq, None, "fsdp"),
            P(seq, "fsdp"),
            P(None, "fsdp"),
            P(None, None, "fsdp"),
            P("fsdp"),
            P("fsdp"),
            P("fsdp"),
            P("fsdp"),
            P("fsdp", seq),
            P(),
            P(),
            P(),
            P("fsdp", None, None),
            P(None, "fsdp"),
            P(None, None, "fsdp"),
        ),
        out_specs=P(("pair", "half", "fsdp"), None),
        check_vma=False,
    )
```

```python
import jax
import jax.numpy as jnp
from jax import lax
from jax.sharding import PartitionSpec as P

SPAN = 256


EPS = 1e-05


def from_behind(value, axis, steps):
    count = lax.axis_size(axis)
    leading, last = (max(0, -steps), min(count, count - steps))
    return lax.ppermute(value, axis, [(source, source + steps) for source in range(leading, last)])


def product_of(form, left, right):
    if left.dtype == jnp.bfloat16 and right.dtype == jnp.bfloat16:
        return jnp.einsum(form, left, right, preferred_element_type=jnp.float32)
    return jnp.einsum(form, left, right.astype(jnp.float32), precision=lax.Precision.HIGHEST)


def norm_rows(values, row_gain):
    widened = values.astype(jnp.float32)
    factor = lax.rsqrt(jnp.mean(widened * widened, axis=-1, keepdims=True) + EPS)
    return (widened * factor * row_gain[None, :]).astype(jnp.bfloat16)


def layout(prompt_lengths, pack_order, resume_prompt, position):
    prompt_count = pack_order.shape[0]
    slot_ids = jnp.arange(prompt_count, dtype=jnp.int32)
    ordered = jnp.sum(
        jnp.where(pack_order[:, None] == slot_ids[None, :], prompt_lengths[None, :], 0), axis=1
    )
    seg_starts = jnp.cumsum(ordered, dtype=jnp.int32) - ordered
    reached = position[:, None] >= seg_starts[None, :]
    segment = jnp.sum(reached.astype(jnp.int32), axis=1) - 1
    seg_start = jnp.max(jnp.where(reached, seg_starts[None, :], 0), axis=1)
    resume_slot = jnp.sum(jnp.where(pack_order == resume_prompt[0], slot_ids, 0))
    resume_start = jnp.sum(jnp.where(slot_ids == resume_slot, seg_starts, 0))
    return (segment, seg_start, resume_slot, resume_start)


def conv_rows(
    source, prior_rows, weight, carry_rows, segment, seg_start, position, resume_slot, resume_start
):
    row_count = source.shape[0]
    edge_rows = prior_rows.shape[0]
    extended = jnp.concatenate([prior_rows, source], axis=0)
    resumed = (segment == resume_slot)[:, None]
    summed = jnp.zeros(source.shape, jnp.float32)
    for back_by in range(edge_rows + 1):
        shifted = extended[edge_rows - back_by : edge_rows - back_by + row_count].astype(
            jnp.float32
        )
        inside = (position - back_by >= seg_start)[:, None]
        carry_index = position - back_by - resume_start + edge_rows
        from_carry = jnp.zeros(source.shape, jnp.float32)
        for slot_id in range(edge_rows):
            from_carry = from_carry + jnp.where(
                (carry_index == slot_id)[:, None],
                carry_rows[slot_id].astype(jnp.float32)[None, :],
                0.0,
            )
        chosen = jnp.where(inside, shifted, jnp.where(resumed, from_carry, 0.0))
        summed = summed + chosen * weight[edge_rows - back_by].astype(jnp.float32)[None, :]
    return jax.nn.silu(summed).astype(jnp.bfloat16)


def span_pieces(
    x_blocks,
    b_blocks,
    c_blocks,
    dt_blocks,
    head_rate,
    segment,
    starting,
    resumed,
    resume_hit,
    carry_init,
    skip_gain,
):
    block_len = segment.shape[1]
    log_decay = -dt_blocks * head_rate[None, None]
    cumulative = jnp.cumsum(log_decay, axis=1)
    indices = jnp.arange(block_len, dtype=jnp.int32)
    causal = (indices[:, None] >= indices[None, :])[None] & (
        segment[:, :, None] == segment[:, None, :]
    )
    cum_rows = jnp.moveaxis(cumulative, 1, -1)
    log_gap = cum_rows[..., :, None] - cum_rows[..., None, :]
    within = causal[:, None, None]
    decays = jnp.where(within, jnp.exp(jnp.where(within, log_gap, 0.0)), 0.0)
    scores = product_of("cqgn,csgn->cgqs", c_blocks, b_blocks)
    dt_source = jnp.moveaxis(dt_blocks, 1, -1)[..., None, :]
    weights = (scores[:, :, None] * decays * dt_source).astype(jnp.bfloat16)
    direct = product_of("cghqs,csghp->cqghp", weights, x_blocks)
    cum_end = cumulative[:, -1]
    tail_mask = (segment == segment[:, -1:])[:, :, None, None]
    to_end = (
        jnp.where(tail_mask, jnp.exp(jnp.where(tail_mask, cum_end[:, None] - cumulative, 0.0)), 0.0)
        * dt_blocks
    )
    scaled = (x_blocks.astype(jnp.float32) * to_end[..., None]).astype(jnp.bfloat16)
    update = product_of("cqghp,cqgn->cghpn", scaled, b_blocks)
    opened = jnp.any(starting, axis=1)
    span_decay = jnp.where(opened[:, None, None], 0.0, jnp.exp(cum_end))
    hit_mask = resume_hit[:, :, None, None]
    has_hit = jnp.any(resume_hit, axis=1)[:, None, None, None]
    cum_hit = jnp.sum(jnp.where(hit_mask, cumulative - log_decay, 0.0), axis=1, keepdims=True)
    carry_mask = resumed[:, :, None, None] & has_hit
    carry_gain = jnp.where(
        carry_mask, jnp.exp(jnp.where(carry_mask, cumulative - cum_hit, 0.0)), 0.0
    )
    end_gain = carry_gain[:, -1]
    update = update + end_gain[..., None, None] * carry_init[None]
    direct = direct + carry_gain[..., None] * product_of("ghpn,cqgn->cqghp", carry_init, c_blocks)
    direct = direct + skip_gain[None, None, :, :, None] * x_blocks.astype(jnp.float32)
    unopened = jnp.cumsum(starting.astype(jnp.int32), axis=1, dtype=jnp.int32) == 0
    state_gain = jnp.where(unopened[:, :, None, None], jnp.exp(cumulative), 0.0)
    return (direct, state_gain, update, span_decay)


def swap_half(value):
    count = lax.axis_size("half")
    return lax.ppermute(value, "half", [(k, count - 1 - k) for k in range(count)])


def ordered_pair(own, other, half, axis):
    return jnp.where(
        half == 0,
        jnp.concatenate([own, other], axis=axis),
        jnp.concatenate([other, own], axis=axis),
    )


def body(
    tokens,
    norm_gain,
    w_zx,
    w_bc,
    w_dt,
    conv_x,
    conv_bc,
    dt_bias,
    decay_rate,
    d_skip,
    gated_gain,
    w_out,
    prompt_lengths,
    pack_order,
    resume_prompt,
    carry_state,
    carry_conv_x,
    carry_conv_bc,
):
    own_rows = tokens.shape[0]
    row_count = 2 * own_rows
    edge_rows = conv_x.shape[0] - 1
    head_width = carry_state.shape[1]
    state_width = carry_state.shape[2]
    head_fsdp = w_dt.shape[1]
    group_fsdp = w_bc.shape[2] // state_width
    per_group = head_fsdp // group_fsdp
    head_local = head_fsdp // 2
    group_local = max(1, head_local // per_group)
    per_local = min(per_group, head_local)
    inner_local = head_local * head_width
    state_cols = group_local * state_width
    span_count = row_count // SPAN
    half = lax.axis_index("half")
    core = lax.axis_index("fsdp")
    core_count = lax.axis_size("fsdp")
    x_off = half * inner_local
    bc_off = (half * head_local) // per_group * state_width
    h_off = half * head_local

    def cut(value, axis, offset, width):
        return lax.dynamic_slice_in_dim(value, offset, width, axis)

    normed_own = norm_rows(tokens, norm_gain)
    share = own_rows // core_count
    fetched = swap_half(cut(normed_own, 0, core * share, share))
    arrived = [fetched] + [
        lax.ppermute(fetched, "fsdp", [(j, (j + shift) % core_count) for j in range(core_count)])
        for shift in range(1, core_count)
    ]
    arrived = jnp.stack(arrived)
    owners = (core - jnp.arange(core_count, dtype=jnp.int32)) % core_count
    normed_other = jnp.take(arrived, owners, axis=0).reshape(own_rows, tokens.shape[1])
    normed = ordered_pair(normed_own, normed_other, half, 0)

    def first_cols(offset_x, offset_bc, offset_h):
        return jnp.concatenate(
            [
                cut(w_zx[:, 1], 1, offset_x, inner_local),
                cut(w_bc[:, 0], 1, offset_bc, state_cols),
                cut(w_bc[:, 1], 1, offset_bc, state_cols),
                cut(w_dt, 1, offset_h, head_local),
            ],
            axis=1,
        )

    other = 1 - half
    first_mine = first_cols(x_off, bc_off, h_off)
    first_theirs = swap_half(
        first_cols(other * inner_local, (other * head_local) // per_group * state_width, other * head_local)
    )
    first_local = ordered_pair(first_mine, first_theirs, half, 0)
    first_full = lax.all_gather(first_local, "pair", axis=0, tiled=True)
    proj_first = jnp.dot(normed, first_full, preferred_element_type=jnp.float32).astype(
        jnp.bfloat16
    )
    conv_width = inner_local + 2 * state_cols
    conv_in = proj_first[:, :conv_width]
    proj_dt = proj_first[:, conv_width:]
    w_z_all, w_out_all, _ = lax.optimization_barrier((w_zx[:, 0], w_out, proj_first))
    z_local = ordered_pair(
        cut(w_z_all, 1, x_off, inner_local),
        swap_half(cut(w_z_all, 1, other * inner_local, inner_local)),
        half,
        0,
    )
    out_local = ordered_pair(
        cut(w_out_all, 0, x_off, inner_local),
        swap_half(cut(w_out_all, 0, other * inner_local, inner_local)),
        half,
        1,
    )
    z_full = lax.all_gather(z_local, "pair", axis=0, tiled=True)
    out_full = lax.all_gather(out_local, "pair", axis=1, tiled=True)
    proj_z = jnp.dot(normed, z_full, preferred_element_type=jnp.float32).astype(jnp.bfloat16)

    position = lax.axis_index("pair") * row_count + jnp.arange(row_count, dtype=jnp.int32)
    segment, seg_start, resume_slot, resume_start = layout(
        prompt_lengths, pack_order, resume_prompt, position
    )
    prior_rows = from_behind(conv_in[row_count - edge_rows :], "pair", 1)
    weight = jnp.concatenate(
        [
            cut(conv_x, 1, x_off, inner_local),
            cut(conv_bc[:, 0], 1, bc_off, state_cols),
            cut(conv_bc[:, 1], 1, bc_off, state_cols),
        ],
        axis=1,
    )
    carry_rows = jnp.concatenate(
        [
            cut(carry_conv_x, 1, x_off, inner_local),
            cut(carry_conv_bc[:, 0], 1, bc_off, state_cols),
            cut(carry_conv_bc[:, 1], 1, bc_off, state_cols),
        ],
        axis=1,
    )
    conv_out = conv_rows(
        conv_in,
        prior_rows,
        weight,
        carry_rows,
        segment,
        seg_start,
        position,
        resume_slot,
        resume_start,
    )
    x_conv = conv_out[:, :inner_local].reshape(span_count, SPAN, group_local, per_local, head_width)
    b_conv = conv_out[:, inner_local : inner_local + state_cols].reshape(
        span_count, SPAN, group_local, state_width
    )
    c_conv = conv_out[:, inner_local + state_cols :].reshape(
        span_count, SPAN, group_local, state_width
    )
    dt_full = jax.nn.softplus(
        proj_dt.astype(jnp.float32) + cut(dt_bias, 0, h_off, head_local)[None, :]
    ).reshape(span_count, SPAN, group_local, per_local)
    seg_blocks = segment.reshape(span_count, SPAN)
    starting = (position == seg_start).reshape(span_count, SPAN)
    resumed = (segment == resume_slot).reshape(span_count, SPAN)
    resume_hit = (position == resume_start).reshape(span_count, SPAN)
    head_rate = cut(decay_rate, 0, h_off, head_local).reshape(group_local, per_local)
    skip_gain = cut(d_skip, 0, h_off, head_local).reshape(group_local, per_local)
    carry_init = cut(carry_state, 0, h_off, head_local).reshape(
        group_local, per_local, head_width, state_width
    )
    direct, state_gain, update, span_decay = span_pieces(
        x_conv,
        b_conv,
        c_conv,
        dt_full,
        head_rate,
        seg_blocks,
        starting,
        resumed,
        resume_hit,
        carry_init,
        skip_gain,
    )

    def fold_span(carried, pieces):
        return (
            (pieces[1][..., None, None] * carried[0] + pieces[0], pieces[1] * carried[1]),
            carried,
        )

    empty_state = jnp.zeros((group_local, per_local, head_width, state_width), jnp.float32)
    unit_decay = jnp.ones((group_local, per_local), jnp.float32)
    (local_state, local_decay), (prefix_state, prefix_decay) = lax.scan(
        fold_span, (empty_state, unit_decay), (update, span_decay)
    )
    hop_count = max(1, lax.axis_size("pair") // 4)
    incoming = jnp.zeros_like(local_state)
    reach = jnp.ones_like(local_decay)
    for steps in range(1, hop_count + 1):
        state_back, decay_back = from_behind((local_state, local_decay), "pair", steps)
        incoming = incoming + reach[..., None, None] * state_back
        reach = reach * decay_back
    entering = prefix_decay[..., None, None] * incoming[None] + prefix_state
    from_state = product_of("cghpn,cqgn->cqghp", entering, c_conv)
    ssd_out = (direct + state_gain[..., None] * from_state).reshape(row_count, inner_local)
    gate_act = jax.nn.silu(proj_z.astype(jnp.float32))
    gated = (ssd_out * gate_act).reshape(row_count, group_local, inner_local // group_local)
    squares = jnp.sum(gated * gated, axis=-1, keepdims=True)
    if head_local < per_group:
        squares = lax.psum(squares, "half")
    factor = lax.rsqrt(squares / (per_group * head_width) + EPS)
    normed_y = (
        (gated * factor).reshape(row_count, inner_local) * cut(gated_gain, 0, x_off, inner_local)[None, :]
    ).astype(jnp.bfloat16)
    piece = own_rows // core_count
    by_owner = normed_y.reshape(2, core_count, piece, inner_local)
    chunk_count = 8
    chunk = out_full.shape[1] // chunk_count
    results = []
    for index in range(chunk_count):
        columns = out_full[:, index * chunk : (index + 1) * chunk]
        total = None
        for shift in list(range(1, core_count)) + [0]:
            rows = lax.dynamic_index_in_dim(by_owner, (core + shift) % core_count, 1, keepdims=False)
            part = jnp.einsum("hrc,cd->hrd", rows, columns, preferred_element_type=jnp.float32)
            if shift:
                part = lax.ppermute(
                    part.astype(jnp.bfloat16),
                    "fsdp",
                    [(j, (j + shift) % core_count) for j in range(core_count)],
                ).astype(jnp.float32)
            total = part if total is None else total + part
        mine = lax.dynamic_index_in_dim(total, half, 0, keepdims=False)
        theirs = lax.dynamic_index_in_dim(total, 1 - half, 0, keepdims=False)
        theirs = swap_half(theirs.astype(jnp.bfloat16))
        results.append((mine + theirs.astype(jnp.float32)).astype(jnp.bfloat16))
    return jnp.concatenate(results, axis=1)


def solution(mesh):
    seq_count = mesh.shape["seq"]
    devices = mesh.devices.reshape(seq_count // 2, 2, mesh.shape["fsdp"])
    paired = jax.sharding.Mesh(devices, ("pair", "half", "fsdp"))
    seq = ("pair", "half")
    return jax.shard_map(
        body,
        mesh=paired,
        in_specs=(
            P(seq, None),
            P(),
            P(seq, None, "fsdp"),
            P(seq, None, "fsdp"),
            P(seq, "fsdp"),
            P(None, "fsdp"),
            P(None, None, "fsdp"),
            P("fsdp"),
            P("fsdp"),
            P("fsdp"),
            P("fsdp"),
            P("fsdp", seq),
            P(),
            P(),
            P(),
            P("fsdp", None, None),
            P(None, "fsdp"),
            P(None, None, "fsdp"),
        ),
        out_specs=P(("pair", "half", "fsdp"), None),
        check_vma=False,
    )
```
